32 devices in a mesh: shot: 4 (over x, core), gy: 4 (over z), gx: 2 (over y).
Axes of the slice: x: 2, y: 2, z: 4, core: 2. Of those that a mesh axis runs over, the one named last changes fastest.
Arguments:
- forward_start: float32 [4, 5, 128, 2048], P('shot', None, 'gy', 'gx'), may hold values from -6 to 6
- adjoint_end: float32 [4, 5, 128, 2048], P('shot', None, 'gy', 'gx'), may hold values from -6 to 6
- velocity: float32 [128, 2048], P('gy', 'gx'), may hold values from 1.5 to 3.2
- attenuation: float32 [128, 2048], P('gy', 'gx'), may hold values from 0.05 to 0.5
- wavelet: float32 [4, 3], P('shot'), may hold values from -8 to 8
- source_cell: int32 [4, 1], P('shot'), may hold values from 0 to 262143
- receiver_cells: int32 [4, 8, 128], P('shot', ('gy', 'gx')), may hold values from 0 to 32767
- observed: float32 [4, 3, 8, 128], P('shot', None, ('gy', 'gx')), may hold values from -6 to 6
- aperture: int32 [4, 8], P('shot', ('gy', 'gx')), may hold values 0 or 1
- block_slot: int32 [8, 64], P(('gy', 'gx')), may hold values from 0 to 63, each once within a row
Outputs:
- forward_end: float32 [4, 5, 128, 2048], P('shot', None, 'gy', 'gx')
- adjoint_start: float32 [4, 5, 128, 2048], P('shot', None, 'gy', 'gx')
- model_gradient: float32 [2, 8, 64], P(None, ('gy', 'gx'), 'shot')
The draws below stay inside these ranges and needn't reach their ends.
Inputs may be any that keep to these rules, and one draw needn't show every extreme that they name: `block_slot`: each row is a permutation of the slots. `receiver_cells`: receivers may share a cell.
All inputs are finite; a program needn't handle non-finite values. No bound on the sum of `aperture` on one device may be relied on, other than what follows from the above.
Results may differ from the reference program's by a relative error of at most 0.0003.
Values sent between devices are 32-bit elements; how exact they have to be, the bound alone decides.
No kernel may reach another device: no remote copies, remote signals or barrier semaphores. Data moves between devices by JAX's collectives and lax.ppermute only.
A program may use at most 64 MiB of HBM per device.

```python
import math
import jax
import jax.numpy as jnp
from jax import lax

CY = 32
CX = 32
CZ = 32
REC_TILE = 128
STEPS = 3
BY = 8
BX = 8
BZ = 8
SHOTS = 4
TILES = 8
NY = 128
NX = 64
BLK_DEV = 64
N_GY = 4
N_GX = 2


def with_ends(values, rng, low, high):
    extent = values.shape
    place = [jax.random.randint(jax.random.fold_in(rng, axis), (), 0, extent[axis]) for axis in range(len(extent))]
    values = values.at[tuple(place)].set(low)
    longest = extent.index(max(extent))
    place[longest] = (place[longest] + 1) % extent[longest]
    return values.at[tuple(place)].set(high)


def block_scale(key, extent, pieces, smallest, largest):
    factor_of = 1.0
    for position, parts in pieces:
        heights = jax.random.uniform(jax.random.fold_in(jax.random.fold_in(key, 6), position), (parts,), jnp.float32, smallest / len(pieces), largest / len(pieces))
        factor_of = factor_of * jnp.repeat(jnp.exp(heights), extent[position] // parts).reshape((-1,) + (1,) * (len(extent) - 1 - position))
    return factor_of


def scatter_about(rng, extent, deviation, reach, cuts=(), kind=jnp.bfloat16):
    level = block_scale(rng, extent, cuts, -0.22, 0.18) if cuts else 1.0
    entries = jax.random.normal(rng, extent, jnp.float32) * deviation * level
    return jnp.minimum(jnp.maximum(entries, -reach), reach).astype(kind)


def setup_inputs(seed: int = 0) -> dict:
    seeds = jax.random.split(jax.random.key(seed), 11)
    forward_start = scatter_about(seeds[0], (SHOTS, 5, NY, NX * CZ), 1.0, 6.0, ((0, 4), (2, 4), (3, 2)), jnp.float32)
    adjoint_end = scatter_about(seeds[1], (SHOTS, 5, NY, NX * CZ), 1.0, 6.0, ((0, 4), (2, 4), (3, 2)), jnp.float32)
    velocity = jnp.clip(1.5 + 1.7 * jax.random.uniform(seeds[2], (NY, NX * CZ), jnp.float32) ** block_scale(seeds[2], (NY, NX * CZ), ((0, 4), (1, 2)), -0.2, 0.2), 1.5, 3.2)
    attenuation = jnp.clip(jnp.exp(math.log(0.5) - 2.3025851 * jax.random.uniform(seeds[3], (NY, NX * CZ), jnp.float32) ** block_scale(seeds[3], (NY, NX * CZ), ((0, 4), (1, 2)), -0.2, 0.2)), 0.05, 0.5)
    wavelet = scatter_about(seeds[4], (SHOTS, STEPS), 2.0, 8.0, ((0, 4),), jnp.float32)
    source_cell = with_ends(jax.random.randint(seeds[5], (SHOTS, 1), 0, NY * NX * CZ), jax.random.fold_in(seeds[5], 1), 0, (NY * NX * CZ) - 1).astype(jnp.int32)
    receiver_cells = with_ends(jax.random.randint(seeds[6], (SHOTS, TILES, REC_TILE), 0, CY * CX * CZ), jax.random.fold_in(seeds[6], 1), 0, (CY * CX * CZ) - 1).astype(jnp.int32)
    observed = scatter_about(seeds[7], (SHOTS, STEPS, TILES, REC_TILE), 1.0, 6.0, ((0, 4), (2, 8)), jnp.float32)
    aperture = with_ends((jax.random.randint(seeds[8], (SHOTS, TILES), 0, 4) < 3).astype(jnp.int32), jax.random.fold_in(seeds[8], 1), 0, 1)
    block_slot = jax.vmap(lambda own: jax.random.permutation(own, BLK_DEV))(jax.random.split(seeds[9], TILES)).reshape((TILES, BLK_DEV)).astype(jnp.int32)
    return {"forward_start": forward_start, "adjoint_end": adjoint_end, "velocity": velocity, "attenuation": attenuation, "wavelet": wavelet, "source_cell": source_cell, "receiver_cells": receiver_cells, "observed": observed, "aperture": aperture, "block_slot": block_slot}


coef_near = 9.0 / 8.0
coef_far = -1.0 / 24.0
stiff_scale = 0.02
relax_rate = 0.3


def forward_diff(padded, axis, count):
    def part(s):
        return lax.slice_in_dim(padded, s, s + count, axis=axis)
    return coef_near * (part(3) - part(2)) + coef_far * (part(4) - part(1))


def backward_diff(padded, axis, count):
    def part(s):
        return lax.slice_in_dim(padded, s, s + count, axis=axis)
    return coef_near * (part(2) - part(1)) + coef_far * (part(3) - part(0))


def pad_axis(field, axis):
    widths = [(0, 0), (0, 0), (0, 0)]
    widths[axis] = (2, 2)
    return jnp.pad(field, widths)


def wave_step(state, stiff, attenuation):
    pres, vel_y, vel_x, vel_z, memory = state
    ny, nx, nz = pres.shape
    vel_y = vel_y - forward_diff(pad_axis(pres, 0), 0, ny)
    vel_x = vel_x - forward_diff(pad_axis(pres, 1), 1, nx)
    vel_z = vel_z - forward_diff(pad_axis(pres, 2), 2, nz)
    div = backward_diff(pad_axis(vel_y, 0), 0, ny) + backward_diff(pad_axis(vel_x, 1), 1, nx) + backward_diff(pad_axis(vel_z, 2), 2, nz)
    memory = memory - relax_rate * (memory + stiff * attenuation * div)
    pres = pres - stiff * (1.0 + attenuation) * div - memory
    return [pres, vel_y, vel_x, vel_z, memory], div


def reference(forward_start, adjoint_end, velocity, attenuation, wavelet, source_cell, receiver_cells, observed, aperture, block_slot):
    ny = CY * N_GY
    nx = CX * N_GX
    shots = forward_start.shape[0]
    forward_start = forward_start.reshape(shots, 5, ny, nx, CZ)
    adjoint_end = adjoint_end.reshape(shots, 5, ny, nx, CZ)
    velocity = velocity.reshape(ny, nx, CZ)
    attenuation = attenuation.reshape(ny, nx, CZ)
    stiff = stiff_scale * velocity * velocity
    tile_ids = jnp.arange(N_GY * N_GX, dtype=jnp.int32)
    tile_y = (tile_ids // N_GX)[:, None]
    tile_x = (tile_ids % N_GX)[:, None]
    grad_scale = float(BY * BX * BZ) ** -0.5

    def one_shot(items):
        start, finish, wave, src, recs, obs, ap = items
        loc_y = recs // (CX * CZ)
        loc_x = (recs // CZ) % CX
        loc_z = recs % CZ
        flat = (((tile_y * CY + loc_y) * nx + tile_x * CX + loc_x) * CZ + loc_z).reshape(-1).astype(jnp.int32)
        state = [start[k] for k in range(5)]
        divs = []
        records = []
        for step in range(STEPS):
            state, div = wave_step(state, stiff, attenuation)
            state[0] = state[0].reshape(-1).at[src[0]].add(wave[step]).reshape(ny, nx, CZ)
            divs.append(div)
            records.append(state[0].reshape(-1)[flat])
        adj = [finish[k] for k in range(5)]
        grad_v = jnp.zeros((ny, nx, CZ), jnp.float32)
        grad_a = jnp.zeros((ny, nx, CZ), jnp.float32)
        for step in range(STEPS - 1, -1, -1):
            adj, unused = wave_step(adj, stiff, attenuation)
            resid = records[step] - obs[step].reshape(-1)
            adj[0] = adj[0].reshape(-1).at[flat].add(resid).reshape(ny, nx, CZ)
            div = divs[step]
            deriv_q = (relax_rate * attenuation - (1.0 + attenuation)) * div
            deriv_m = -relax_rate * attenuation * div
            grad_v = grad_v + (adj[0] * deriv_q + adj[4] * deriv_m) * (2.0 * stiff_scale * velocity)
            grad_a = grad_a + (adj[0] * (relax_rate - 1.0) - adj[4] * relax_rate) * stiff * div
        mask = ap.astype(jnp.float32).reshape(N_GY, N_GX)
        mask = jnp.repeat(jnp.repeat(mask, CY, axis=0), CX, axis=1)[:, :, None]
        grads = jnp.stack([grad_v, grad_a]) * mask
        coarse = grads.reshape(2, ny // BY, BY, nx // BX, BX, CZ // BZ, BZ).sum(axis=(2, 4, 6)) * grad_scale
        return jnp.stack(state), jnp.stack(adj), coarse

    forward_end, adjoint_start, coarse = lax.map(one_shot, (forward_start, adjoint_end, wavelet, source_cell, receiver_cells, observed, aperture))
    total = jnp.sum(coarse, axis=0)
    per_tile = total.reshape(2, N_GY, CY // BY, N_GX, CX // BX, CZ // BZ)
    per_tile = per_tile.transpose(0, 1, 3, 2, 4, 5).reshape(2, N_GY * N_GX, -1)
    rows = jnp.broadcast_to(tile_ids[:, None], block_slot.shape)
    model_gradient = jnp.zeros(per_tile.shape, jnp.float32).at[:, rows, block_slot].set(per_tile)
    forward_end = forward_end.reshape(shots, 5, ny, nx * CZ)
    adjoint_start = adjoint_start.reshape(shots, 5, ny, nx * CZ)
    return forward_end, adjoint_start, model_gradient
```

```python
import jax
import jax.numpy as jnp
from jax import lax
from jax.sharding import PartitionSpec as P

CZ = 32
STEPS = 3
BY = 8
BX = 8
BZ = 8
HALO = 3 * STEPS

coef_near = 9.0 / 8.0
coef_far = -1.0 / 24.0
stiff_scale = 0.02
relax_rate = 0.3


def shift(a, d, axis):
    widths = [(0, 0, 0)] * a.ndim
    widths[axis] = (-d, d, 0)
    return lax.pad(a, jnp.zeros((), a.dtype), widths)


def forward_diff(s):
    return coef_near * (s(1) - s(0)) + coef_far * (s(2) - s(-1))


def backward_diff(s):
    return coef_near * (s(0) - s(-1)) + coef_far * (s(1) - s(-2))


def exchange(cells, axis, dim, width):
    count = lax.axis_size(axis)
    ends = count - 1
    head = lax.slice_in_dim(cells, 0, width, axis=dim)
    tail = lax.slice_in_dim(cells, cells.shape[dim] - width, cells.shape[dim], axis=dim)
    below = lax.ppermute(tail, axis, [(i, i + 1) for i in range(ends)])
    above = lax.ppermute(head, axis, [(i + 1, i) for i in range(ends)])
    return below, above


def on_device(
    forward_start,
    adjoint_end,
    velocity,
    attenuation,
    wavelet,
    source_cell,
    receiver_cells,
    observed,
    aperture,
    block_slot,
):
    nz = CZ
    ny = velocity.shape[0]
    lanes = velocity.shape[1]
    nx = lanes // nz
    r = HALO
    ey = ny + 2 * r
    ex = nx + 2 * r
    el = ex * nz
    index_y = lax.axis_index("gy")
    index_x = lax.axis_index("gx")
    total_y = ny * lax.axis_size("gy")
    total_x = nx * lax.axis_size("gx")

    fields = jnp.concatenate(
        [forward_start[0], adjoint_end[0], velocity[None], attenuation[None]], axis=0
    )
    below, above = exchange(fields, "gy", 1, r)
    fields = jnp.concatenate([below, fields, above], axis=1)
    left, right = exchange(fields, "gx", 2, r * nz)
    fields = jnp.concatenate([left, fields, right], axis=2)

    vel = fields[10]
    att = fields[11]
    stiff = stiff_scale * vel * vel

    row = lax.broadcasted_iota(jnp.int32, (ey, el), 0)
    lane = lax.broadcasted_iota(jnp.int32, (ey, el), 1)
    glob_y = index_y * ny - r + row
    glob_x = index_x * nx - r + lane // nz
    inside = (glob_y >= 0) & (glob_y < total_y) & (glob_x >= 0) & (glob_x < total_x)
    depth = lane % nz
    zero = jnp.zeros((ey, el), jnp.float32)

    def zshift(a, d):
        return jnp.where((depth + d >= 0) & (depth + d < nz), shift(a, d, 1), zero)

    def wave_step(state):
        pres, vel_y, vel_x, vel_z, memory = state
        vel_y = jnp.where(inside, vel_y - forward_diff(lambda d: shift(pres, d, 0)), zero)
        vel_x = jnp.where(inside, vel_x - forward_diff(lambda d: shift(pres, d * nz, 1)), zero)
        vel_z = vel_z - forward_diff(lambda d: zshift(pres, d))
        div = (
            backward_diff(lambda d: shift(vel_y, d, 0))
            + backward_diff(lambda d: shift(vel_x, d * nz, 1))
            + backward_diff(lambda d: zshift(vel_z, d))
        )
        memory = memory - relax_rate * (memory + stiff * att * div)
        pres = jnp.where(inside, pres - stiff * (1.0 + att) * div - memory, zero)
        return [pres, vel_y, vel_x, vel_z, memory], div

    def own(a):
        return a[r : r + ny, r * nz : r * nz + lanes]

    cell = source_cell[0, 0]
    src_y = cell // (total_x * nz) - index_y * ny + r
    src_x = cell // nz % total_x - index_x * nx + r
    src_z = cell % nz
    src_here = (row == src_y) & (lane == src_x * nz + src_z)

    recs = receiver_cells[0, 0]
    rec_y = recs // (nx * nz)
    rec_x = recs // nz % nx
    rec_z = recs % nz
    own_flat = (rec_y + r) * el + (rec_x + r) * nz + rec_z

    state = [fields[k] for k in range(5)]
    divs = []
    records = []
    for step in range(STEPS):
        state, div = wave_step(state)
        state[0] = state[0] + jnp.where(src_here, wavelet[0, step], jnp.float32(0.0))
        divs.append(own(div))
        records.append(state[0].reshape(-1)[own_flat])
    forward_end = jnp.stack([own(f) for f in state])[None]

    resid = jnp.stack(records) - observed[0, :, 0]
    message = jnp.concatenate([recs.astype(jnp.float32)[None], resid], axis=0)[None]
    below, above = exchange(message, "gy", 0, 1)
    message = jnp.concatenate([below, message, above], axis=0)
    left, right = exchange(message, "gx", 0, 3)
    message = jnp.concatenate([left, message, right], axis=0)
    off_y = jnp.array([-1, 0, 1] * 3, jnp.int32)[:, None] * ny
    off_x = jnp.repeat(jnp.array([-1, 0, 1], jnp.int32), 3)[:, None] * nx
    cells = message[:, 0].astype(jnp.int32)
    at_y = cells // (nx * nz) + off_y + r
    at_x = cells // nz % nx + off_x + r
    at_z = cells % nz
    fits = (at_y >= 0) & (at_y < ey) & (at_x >= 0) & (at_x < ex)
    flat = jnp.where(fits, at_y * el + at_x * nz + at_z, ey * el).reshape(-1)
    amounts = message[:, 1:].transpose(1, 0, 2).reshape(STEPS, -1)
    inject = jnp.zeros((STEPS, ey * el), jnp.float32).at[:, flat].add(amounts, mode="drop")
    inject = inject.reshape(STEPS, ey, el)

    velocity_own = velocity
    attenuation_own = attenuation
    stiff_own = stiff_scale * velocity_own * velocity_own
    adj = [fields[5 + k] for k in range(5)]
    grad_v = jnp.zeros((ny, lanes), jnp.float32)
    grad_a = jnp.zeros((ny, lanes), jnp.float32)
    for step in range(STEPS - 1, -1, -1):
        adj, unused = wave_step(adj)
        adj[0] = adj[0] + inject[step]
        div = divs[step]
        q = own(adj[0])
        m = own(adj[4])
        deriv_q = (relax_rate * attenuation_own - (1.0 + attenuation_own)) * div
        deriv_m = -relax_rate * attenuation_own * div
        grad_v = grad_v + (q * deriv_q + m * deriv_m) * (2.0 * stiff_scale * velocity_own)
        grad_a = grad_a + (q * (relax_rate - 1.0) - m * relax_rate) * stiff_own * div
    adjoint_start = jnp.stack([own(f) for f in adj])[None]

    grad_scale = float(BY * BX * BZ) ** (-0.5)
    weight = aperture[0, 0].astype(jnp.float32)
    grads = jnp.stack([grad_v, grad_a]) * weight
    blocks = grads.reshape(2, ny // BY, BY, nx // BX, BX, nz // BZ, BZ)
    blocks = blocks.transpose(1, 3, 5, 0, 2, 4, 6).reshape(-1, 2, BY * BX * BZ)
    slots = block_slot[0]
    sums = jnp.sum(blocks, axis=2) * grad_scale
    ordered = jnp.zeros(sums.shape, jnp.float32).at[slots].set(sums)
    coarse = lax.psum_scatter(ordered, "shot", scatter_dimension=0, tiled=True)
    model_gradient = coarse.T[:, None, :]
    return (forward_end, adjoint_start, model_gradient)


def solution(mesh):
    placed = (
        P("shot", None, "gy", "gx"),
        P("shot", None, "gy", "gx"),
        P("gy", "gx"),
        P("gy", "gx"),
        P("shot", None),
        P("shot", None),
        P("shot", ("gy", "gx"), None),
        P("shot", None, ("gy", "gx"), None),
        P("shot", ("gy", "gx")),
        P(("gy", "gx"), None),
    )
    return jax.shard_map(
        on_device,
        mesh=mesh,
        in_specs=placed,
        out_specs=(
            P("shot", None, "gy", "gx"),
            P("shot", None, "gy", "gx"),
            P(None, ("gy", "gx"), "shot"),
        ),
        check_vma=False,
    )
```

```python
import jax
import jax.numpy as jnp
from jax import lax
from jax.sharding import PartitionSpec as P

CZ = 32
STEPS = 3
BY = 8
BX = 8
BZ = 8
HALO = 3 * STEPS

coef_near = 9.0 / 8.0
coef_far = -1.0 / 24.0
stiff_scale = 0.02
relax_rate = 0.3


def shift(a, d, axis):
    widths = [(0, 0, 0)] * a.ndim
    widths[axis] = (-d, d, 0)
    return lax.pad(a, jnp.zeros((), a.dtype), widths)


def forward_diff(s):
    return coef_near * (s(1) - s(0)) + coef_far * (s(2) - s(-1))


def backward_diff(s):
    return coef_near * (s(0) - s(-1)) + coef_far * (s(1) - s(-2))


def exchange(cells, axis, dim, width):
    count = lax.axis_size(axis)
    ends = count - 1
    head = lax.slice_in_dim(cells, 0, width, axis=dim)
    tail = lax.slice_in_dim(cells, cells.shape[dim] - width, cells.shape[dim], axis=dim)
    below = lax.ppermute(tail, axis, [(i, i + 1) for i in range(ends)])
    above = lax.ppermute(head, axis, [(i + 1, i) for i in range(ends)])
    return below, above


def on_device(
    forward_start,
    adjoint_end,
    velocity,
    attenuation,
    wavelet,
    source_cell,
    receiver_cells,
    observed,
    aperture,
    block_slot,
):
    nz = CZ
    ny = velocity.shape[0]
    lanes = velocity.shape[1]
    nx = lanes // nz
    r = HALO
    ey = ny + 2 * r
    ex = nx + 2 * r
    el = ex * nz
    index_y = lax.axis_index("gy")
    index_x = lax.axis_index("gx")
    total_y = ny * lax.axis_size("gy")
    total_x = nx * lax.axis_size("gx")

    fields = jnp.concatenate(
        [forward_start[0], adjoint_end[0], velocity[None], attenuation[None]], axis=0
    )
    below, above = exchange(fields, "gy", 1, r)
    fields = jnp.concatenate([below, fields, above], axis=1)
    left, right = exchange(fields, "gx", 2, r * nz)
    fields = jnp.concatenate([left, fields, right], axis=2)

    vel = fields[10]
    att = fields[11]
    stiff = stiff_scale * vel * vel

    row = lax.broadcasted_iota(jnp.int32, (ey, el), 0)
    lane = lax.broadcasted_iota(jnp.int32, (ey, el), 1)
    glob_y = index_y * ny - r + row
    glob_x = index_x * nx - r + lane // nz
    inside = (glob_y >= 0) & (glob_y < total_y) & (glob_x >= 0) & (glob_x < total_x)
    depth = lane % nz
    zero = jnp.zeros((ey, el), jnp.float32)

    def zshift(a, d):
        return jnp.where((depth + d >= 0) & (depth + d < nz), shift(a, d, 1), zero)

    def wave_step(state):
        pres, vel_y, vel_x, vel_z, memory = state
        vel_y = jnp.where(inside, vel_y - forward_diff(lambda d: shift(pres, d, 0)), zero)
        vel_x = jnp.where(inside, vel_x - forward_diff(lambda d: shift(pres, d * nz, 1)), zero)
        vel_z = vel_z - forward_diff(lambda d: zshift(pres, d))
        div = (
            backward_diff(lambda d: shift(vel_y, d, 0))
            + backward_diff(lambda d: shift(vel_x, d * nz, 1))
            + backward_diff(lambda d: zshift(vel_z, d))
        )
        memory = memory - relax_rate * (memory + stiff * att * div)
        pres = jnp.where(inside, pres - stiff * (1.0 + att) * div - memory, zero)
        return [pres, vel_y, vel_x, vel_z, memory], div

    def own(a):
        return a[r : r + ny, r * nz : r * nz + lanes]

    cell = source_cell[0, 0]
    src_y = cell // (total_x * nz) - index_y * ny + r
    src_x = cell // nz % total_x - index_x * nx + r
    src_z = cell % nz
    src_here = (row == src_y) & (lane == src_x * nz + src_z)

    recs = receiver_cells[0, 0]
    rec_y = recs // (nx * nz)
    rec_x = recs // nz % nx
    rec_z = recs % nz
    own_flat = (rec_y + r) * el + (rec_x + r) * nz + rec_z

    state = [fields[k] for k in range(5)]
    divs = []
    records = []
    for step in range(STEPS):
        state, div = wave_step(state)
        state[0] = state[0] + jnp.where(src_here, wavelet[0, step], jnp.float32(0.0))
        divs.append(own(div))
        records.append(state[0].reshape(-1)[own_flat])
    forward_end = jnp.stack([own(f) for f in state])[None]

    resid = jnp.stack(records) - observed[0, :, 0]
    inject = jnp.stack(
        [jnp.zeros((ny * lanes,), jnp.float32).at[recs].add(resid[n]) for n in range(STEPS)]
    ).reshape(STEPS, ny, lanes)
    below, above = exchange(inject, "gy", 1, r)
    inject = jnp.concatenate([below, inject, above], axis=1)
    left, right = exchange(inject, "gx", 2, r * nz)
    inject = jnp.concatenate([left, inject, right], axis=2)

    velocity_own = velocity
    attenuation_own = attenuation
    stiff_own = stiff_scale * velocity_own * velocity_own
    adj = [fields[5 + k] for k in range(5)]
    grad_v = jnp.zeros((ny, lanes), jnp.float32)
    grad_a = jnp.zeros((ny, lanes), jnp.float32)
    for step in range(STEPS - 1, -1, -1):
        adj, unused = wave_step(adj)
        adj[0] = adj[0] + inject[step]
        div = divs[step]
        q = own(adj[0])
        m = own(adj[4])
        deriv_q = (relax_rate * attenuation_own - (1.0 + attenuation_own)) * div
        deriv_m = -relax_rate * attenuation_own * div
        grad_v = grad_v + (q * deriv_q + m * deriv_m) * (2.0 * stiff_scale * velocity_own)
        grad_a = grad_a + (q * (relax_rate - 1.0) - m * relax_rate) * stiff_own * div
    adjoint_start = jnp.stack([own(f) for f in adj])[None]

    grad_scale = float(BY * BX * BZ) ** (-0.5)
    weight = aperture[0, 0].astype(jnp.float32)
    grads = jnp.stack([grad_v, grad_a]) * weight
    blocks = grads.reshape(2, ny // BY, BY, nx // BX, BX, nz // BZ, BZ)
    blocks = blocks.transpose(1, 3, 5, 0, 2, 4, 6).reshape(-1, 2, BY * BX * BZ)
    slots = block_slot[0]
    sums = jnp.sum(blocks, axis=2) * grad_scale
    ordered = jnp.zeros(sums.shape, jnp.float32).at[slots].set(sums)
    shots = lax.axis_size("shot")
    parts = lax.all_to_all(
        ordered.reshape(shots, -1, 2), "shot", split_axis=0, concat_axis=0, tiled=True
    )
    coarse = jnp.sum(parts, axis=0)
    model_gradient = coarse.T[:, None, :]
    return (forward_end, adjoint_start, model_gradient)


def solution(mesh):
    placed = (
        P("shot", None, "gy", "gx"),
        P("shot", None, "gy", "gx"),
        P("gy", "gx"),
        P("gy", "gx"),
        P("shot", None),
        P("shot", None),
        P("shot", ("gy", "gx"), None),
        P("shot", None, ("gy", "gx"), None),
        P("shot", ("gy", "gx")),
        P(("gy", "gx"), None),
    )
    return jax.shard_map(
        on_device,
        mesh=mesh,
        in_specs=placed,
        out_specs=(
            P("shot", None, "gy", "gx"),
            P("shot", None, "gy", "gx"),
            P(None, ("gy", "gx"), "shot"),
        ),
        check_vma=False,
    )
```

```python
import jax
import jax.numpy as jnp
from jax import lax
from jax.sharding import PartitionSpec as P

CZ = 32
STEPS = 3
BY = 8
BX = 8
BZ = 8
HALO = 3 * STEPS

coef_near = 9.0 / 8.0
coef_far = -1.0 / 24.0
stiff_scale = 0.02
relax_rate = 0.3


def shift(a, d, axis):
    widths = [(0, 0, 0)] * a.ndim
    widths[axis] = (-d, d, 0)
    return lax.pad(a, jnp.zeros((), a.dtype), widths)


def forward_diff(s):
    return coef_near * (s(1) - s(0)) + coef_far * (s(2) - s(-1))


def backward_diff(s):
    return coef_near * (s(0) - s(-1)) + coef_far * (s(1) - s(-2))


def exchange(cells, axis, dim, width):
    count = lax.axis_size(axis)
    ends = count - 1
    head = lax.slice_in_dim(cells, 0, width, axis=dim)
    tail = lax.slice_in_dim(cells, cells.shape[dim] - width, cells.shape[dim], axis=dim)
    below = lax.ppermute(tail, axis, [(i, i + 1) for i in range(ends)])
    above = lax.ppermute(head, axis, [(i + 1, i) for i in range(ends)])
    return below, above


def halo(stack, r, nz):
    k, rows, lanes = stack.shape
    count_y = lax.axis_size("gy")
    count_x = lax.axis_size("gx")
    w = r * nz
    span_y = {-1: (0, r), 0: (0, rows), 1: (rows - r, rows)}
    span_x = {-1: (0, w), 0: (0, lanes), 1: (lanes - w, lanes)}
    got = {}
    for dy in (-1, 0, 1):
        for dx in (-1, 0, 1):
            if dy == 0 and dx == 0:
                continue
            ys = span_y[dy]
            xs = span_x[dx]
            piece = stack[:, ys[0] : ys[1], xs[0] : xs[1]]
            pairs = []
            for y in range(count_y):
                for x in range(count_x):
                    ty, tx = y + dy, x + dx
                    if 0 <= ty < count_y and 0 <= tx < count_x:
                        pairs.append((y * count_x + x, ty * count_x + tx))
            got[(-dy, -dx)] = lax.ppermute(piece, ("gy", "gx"), pairs)
    out = []
    for j in range(k):
        bands = []
        for dy in (-1, 0, 1):
            parts = [stack[j] if (dy, dx) == (0, 0) else got[(dy, dx)][j] for dx in (-1, 0, 1)]
            bands.append(jnp.concatenate(parts, axis=1))
        out.append(jnp.concatenate(bands, axis=0))
    return out


def on_device(
    forward_start,
    adjoint_end,
    velocity,
    attenuation,
    wavelet,
    source_cell,
    receiver_cells,
    observed,
    aperture,
    block_slot,
):
    nz = CZ
    ny = velocity.shape[0]
    lanes = velocity.shape[1]
    nx = lanes // nz
    r = HALO
    ey = ny + 2 * r
    ex = nx + 2 * r
    el = ex * nz
    index_y = lax.axis_index("gy")
    index_x = lax.axis_index("gx")
    total_y = ny * lax.axis_size("gy")
    total_x = nx * lax.axis_size("gx")

    fields = halo(
        jnp.concatenate(
            [forward_start[0], adjoint_end[0], velocity[None], attenuation[None]], axis=0
        ),
        r,
        nz,
    )

    vel = fields[10]
    att = fields[11]
    stiff = stiff_scale * vel * vel

    row = lax.broadcasted_iota(jnp.int32, (ey, el), 0)
    lane = lax.broadcasted_iota(jnp.int32, (ey, el), 1)
    glob_y = index_y * ny - r + row
    glob_x = index_x * nx - r + lane // nz
    inside = (glob_y >= 0) & (glob_y < total_y) & (glob_x >= 0) & (glob_x < total_x)
    depth = lane % nz
    zero = jnp.zeros((ey, el), jnp.float32)

    def zshift(a, d):
        return jnp.where((depth + d >= 0) & (depth + d < nz), shift(a, d, 1), zero)

    def wave_step(state):
        pres, vel_y, vel_x, vel_z, memory = state
        vel_y = jnp.where(inside, vel_y - forward_diff(lambda d: shift(pres, d, 0)), zero)
        vel_x = jnp.where(inside, vel_x - forward_diff(lambda d: shift(pres, d * nz, 1)), zero)
        vel_z = vel_z - forward_diff(lambda d: zshift(pres, d))
        div = (
            backward_diff(lambda d: shift(vel_y, d, 0))
            + backward_diff(lambda d: shift(vel_x, d * nz, 1))
            + backward_diff(lambda d: zshift(vel_z, d))
        )
        memory = memory - relax_rate * (memory + stiff * att * div)
        pres = jnp.where(inside, pres - stiff * (1.0 + att) * div - memory, zero)
        return [pres, vel_y, vel_x, vel_z, memory], div

    def own(a):
        return a[r : r + ny, r * nz : r * nz + lanes]

    cell = source_cell[0, 0]
    src_y = cell // (total_x * nz) - index_y * ny + r
    src_x = cell // nz % total_x - index_x * nx + r
    src_z = cell % nz
    src_here = (row == src_y) & (lane == src_x * nz + src_z)

    recs = receiver_cells[0, 0]
    rec_y = recs // (nx * nz)
    rec_x = recs // nz % nx
    rec_z = recs % nz
    own_flat = (rec_y + r) * el + (rec_x + r) * nz + rec_z

    state = [fields[k] for k in range(5)]
    divs = []
    records = []
    for step in range(STEPS):
        state, div = wave_step(state)
        state[0] = state[0] + jnp.where(src_here, wavelet[0, step], jnp.float32(0.0))
        divs.append(own(div))
        records.append(state[0].reshape(-1)[own_flat])
    forward_end = jnp.stack([own(f) for f in state])[None]

    resid = jnp.stack(records) - observed[0, :, 0]
    inject = jnp.stack(
        [jnp.zeros((ny * lanes,), jnp.float32).at[recs].add(resid[n]) for n in range(STEPS)]
    ).reshape(STEPS, ny, lanes)
    inject = halo(inject, r, nz)

    velocity_own = velocity
    attenuation_own = attenuation
    stiff_own = stiff_scale * velocity_own * velocity_own
    adj = [fields[5 + k] for k in range(5)]
    grad_v = jnp.zeros((ny, lanes), jnp.float32)
    grad_a = jnp.zeros((ny, lanes), jnp.float32)
    for step in range(STEPS - 1, -1, -1):
        adj, unused = wave_step(adj)
        adj[0] = adj[0] + inject[step]
        div = divs[step]
        q = own(adj[0])
        m = own(adj[4])
        deriv_q = (relax_rate * attenuation_own - (1.0 + attenuation_own)) * div
        deriv_m = -relax_rate * attenuation_own * div
        grad_v = grad_v + (q * deriv_q + m * deriv_m) * (2.0 * stiff_scale * velocity_own)
        grad_a = grad_a + (q * (relax_rate - 1.0) - m * relax_rate) * stiff_own * div
    adjoint_start = jnp.stack([own(f) for f in adj])[None]

    grad_scale = float(BY * BX * BZ) ** (-0.5)
    weight = aperture[0, 0].astype(jnp.float32)
    grads = jnp.stack([grad_v, grad_a]) * weight
    blocks = grads.reshape(2, ny // BY, BY, nx // BX, BX, nz // BZ, BZ)
    blocks = blocks.transpose(1, 3, 5, 0, 2, 4, 6).reshape(-1, 2, BY * BX * BZ)
    slots = block_slot[0]
    sums = jnp.sum(blocks, axis=2) * grad_scale
    ordered = jnp.zeros(sums.shape, jnp.float32).at[slots].set(sums)
    shots = lax.axis_size("shot")
    parts = lax.all_to_all(
        ordered.reshape(shots, -1, 2), "shot", split_axis=0, concat_axis=0, tiled=True
    )
    coarse = jnp.sum(parts, axis=0)
    model_gradient = coarse.T[:, None, :]
    return (forward_end, adjoint_start, model_gradient)


def solution(mesh):
    placed = (
        P("shot", None, "gy", "gx"),
        P("shot", None, "gy", "gx"),
        P("gy", "gx"),
        P("gy", "gx"),
        P("shot", None),
        P("shot", None),
        P("shot", ("gy", "gx"), None),
        P("shot", None, ("gy", "gx"), None),
        P("shot", ("gy", "gx")),
        P(("gy", "gx"), None),
    )
    return jax.shard_map(
        on_device,
        mesh=mesh,
        in_specs=placed,
        out_specs=(
            P("shot", None, "gy", "gx"),
            P("shot", None, "gy", "gx"),
            P(None, ("gy", "gx"), "shot"),
        ),
        check_vma=False,
    )
```

```python
import jax
import jax.numpy as jnp
from jax import lax
from jax.experimental import pallas as pl
from jax.experimental.pallas import tpu as pltpu
from jax.sharding import PartitionSpec as P

CZ = 32
STEPS = 3
BY = 8
BX = 8
BZ = 8
HALO = 3 * STEPS

coef_near = 9.0 / 8.0
coef_far = -1.0 / 24.0
stiff_scale = 0.02
relax_rate = 0.3


def round_up(value, unit):
    return (value + unit - 1) // unit * unit


class Frame:
    def __init__(self, ny, lanes):
        self.ny = ny
        self.lanes = lanes
        self.oy = round_up(HALO, 8)
        self.ox = round_up(HALO * CZ, 128)
        self.ey = 2 * self.oy + ny
        self.el = 2 * self.ox + lanes


def send_pieces(stack, frame):
    ny, lanes, ox = frame.ny, frame.lanes, frame.ox
    lo_rows = stack[:, :HALO]
    hi_rows = stack[:, ny - HALO :]
    count_y = lax.axis_size("gy")
    count_x = lax.axis_size("gx")

    def move(piece, dy, dx):
        pairs = []
        for y in range(count_y):
            for x in range(count_x):
                ty, tx = y + dy, x + dx
                if 0 <= ty < count_y and 0 <= tx < count_x:
                    pairs.append((y * count_x + x, ty * count_x + tx))
        return lax.ppermute(piece, ("gy", "gx"), pairs)

    return (
        move(hi_rows, 1, 0),
        move(lo_rows, -1, 0),
        move(stack[:, :, lanes - ox :], 0, 1),
        move(stack[:, :, :ox], 0, -1),
        move(hi_rows[:, :, lanes - ox :], 1, 1),
        move(hi_rows[:, :, :ox], 1, -1),
        move(lo_rows[:, :, lanes - ox :], -1, 1),
        move(lo_rows[:, :, :ox], -1, -1),
    )


def assemble(dst, own, pieces, j, frame):
    ny, lanes, oy, ox, el = frame.ny, frame.lanes, frame.oy, frame.ox, frame.el
    below, above, left, right, b_l, b_r, a_l, a_r = pieces
    lo = slice(oy - HALO, oy)
    mid = slice(oy, oy + ny)
    hi = slice(oy + ny, oy + ny + HALO)
    west = slice(0, ox)
    centre = slice(ox, ox + lanes)
    east = slice(ox + lanes, el)
    dst[...] = jnp.zeros(dst.shape, dst.dtype)
    dst[mid, centre] = own[j]
    dst[lo, centre] = below[j]
    dst[hi, centre] = above[j]
    dst[mid, west] = left[j]
    dst[mid, east] = right[j]
    dst[lo, west] = b_l[j]
    dst[lo, east] = b_r[j]
    dst[hi, west] = a_l[j]
    dst[hi, east] = a_r[j]


def stepper(frame, bounds_ref):
    ey, el = frame.ey, frame.el
    row = lax.broadcasted_iota(jnp.int32, (ey, el), 0)
    lane = lax.broadcasted_iota(jnp.int32, (ey, el), 1)
    inside = (
        (row >= bounds_ref[0])
        & (row < bounds_ref[1])
        & (lane >= bounds_ref[2])
        & (lane < bounds_ref[3])
    )
    depth = lane % CZ
    zero = jnp.zeros((ey, el), jnp.float32)
    z_ok = {d: (depth + d >= 0) & (depth + d < CZ) for d in (-2, -1, 1, 2)}

    def rows(a, d):
        return a if d == 0 else pltpu.roll(a, (-d) % ey, 0)

    def lanes(a, d):
        return a if d == 0 else pltpu.roll(a, (-d) % el, 1)

    def deep(a, d):
        return a if d == 0 else jnp.where(z_ok[d], lanes(a, d), zero)

    def forward_diff(s):
        return coef_near * (s(1) - s(0)) + coef_far * (s(2) - s(-1))

    def backward_diff(s):
        return coef_near * (s(0) - s(-1)) + coef_far * (s(1) - s(-2))

    def wave_step(state, stiff, att):
        pres, vel_y, vel_x, vel_z, memory = state
        vel_y = jnp.where(inside, vel_y - forward_diff(lambda d: rows(pres, d)), zero)
        vel_x = jnp.where(inside, vel_x - forward_diff(lambda d: lanes(pres, d * CZ)), zero)
        vel_z = vel_z - forward_diff(lambda d: deep(pres, d))
        div = (
            backward_diff(lambda d: rows(vel_y, d))
            + backward_diff(lambda d: lanes(vel_x, d * CZ))
            + backward_diff(lambda d: deep(vel_z, d))
        )
        memory = memory - relax_rate * (memory + stiff * att * div)
        pres = jnp.where(inside, pres - stiff * (1.0 + att) * div - memory, zero)
        return [pres, vel_y, vel_x, vel_z, memory], div

    return wave_step, row, lane


def forward_kernel(frame, bounds_ref, source_ref, wave_ref, own_ref, *rest):
    pieces = rest[:8]
    end_ref, div_ref, pres_ref, ext = rest[8:]
    for e, j in enumerate((0, 1, 2, 3, 4, 10, 11)):
        assemble(ext.at[e], own_ref, pieces, j, frame)
    wave_step, row, lane = stepper(frame, bounds_ref)
    source = (row == source_ref[0]) & (lane == source_ref[1])
    vel = ext[5]
    att = ext[6]
    stiff = stiff_scale * vel * vel
    state = [ext[k] for k in range(5)]
    mid = slice(frame.oy, frame.oy + frame.ny)
    centre = slice(frame.ox, frame.ox + frame.lanes)
    for step in range(STEPS):
        state, div = wave_step(state, stiff, att)
        state[0] = state[0] + jnp.where(source, wave_ref[step], jnp.float32(0.0))
        div_ref[step] = div[mid, centre]
        pres_ref[step] = state[0][mid, centre]
    for k in range(5):
        end_ref[0, k] = state[k][mid, centre]


def adjoint_kernel(frame, bounds_ref, own_ref, *rest):
    pieces = rest[:8]
    inject_own = rest[8]
    inject_pieces = rest[9:17]
    div_ref, start_ref, grad_ref, ext = rest[17:]
    for e, j in enumerate((5, 6, 7, 8, 9, 10, 11)):
        assemble(ext.at[e], own_ref, pieces, j, frame)
    for n in range(STEPS):
        assemble(ext.at[7 + n], inject_own, inject_pieces, n, frame)
    wave_step, row, lane = stepper(frame, bounds_ref)
    vel = ext[5]
    att = ext[6]
    stiff = stiff_scale * vel * vel
    mid = slice(frame.oy, frame.oy + frame.ny)
    centre = slice(frame.ox, frame.ox + frame.lanes)
    velocity = vel[mid, centre]
    attenuation = att[mid, centre]
    stiff_own = stiff[mid, centre]
    adj = [ext[k] for k in range(5)]
    grad_v = jnp.zeros((frame.ny, frame.lanes), jnp.float32)
    grad_a = jnp.zeros((frame.ny, frame.lanes), jnp.float32)
    for step in range(STEPS - 1, -1, -1):
        adj, unused = wave_step(adj, stiff, att)
        adj[0] = adj[0] + ext[7 + step]
        div = div_ref[step]
        q = adj[0][mid, centre]
        m = adj[4][mid, centre]
        deriv_q = (relax_rate * attenuation - (1.0 + attenuation)) * div
        deriv_m = -relax_rate * attenuation * div
        grad_v = grad_v + (q * deriv_q + m * deriv_m) * (2.0 * stiff_scale * velocity)
        grad_a = grad_a + (q * (relax_rate - 1.0) - m * relax_rate) * stiff_own * div
    for k in range(5):
        start_ref[0, k] = adj[k][mid, centre]
    for c, g in enumerate((grad_v, grad_a)):
        grad_ref[c] = g.reshape(frame.ny // BY, BY, frame.lanes).sum(axis=1)


def vmem():
    return pl.BlockSpec(memory_space=pltpu.VMEM)


def smem():
    return pl.BlockSpec(memory_space=pltpu.SMEM)


def on_device(
    forward_start,
    adjoint_end,
    velocity,
    attenuation,
    wavelet,
    source_cell,
    receiver_cells,
    observed,
    aperture,
    block_slot,
):
    nz = CZ
    ny = velocity.shape[0]
    lanes = velocity.shape[1]
    nx = lanes // nz
    frame = Frame(ny, lanes)
    index_y = lax.axis_index("gy")
    index_x = lax.axis_index("gx")
    total_y = ny * lax.axis_size("gy")
    total_x = nx * lax.axis_size("gx")

    row_lo = frame.oy - index_y * ny
    lane_lo = frame.ox - index_x * lanes
    bounds = jnp.stack([row_lo, row_lo + total_y, lane_lo, lane_lo + total_x * nz]).astype(jnp.int32)

    cell = source_cell[0, 0]
    src_row = cell // (total_x * nz) + row_lo
    src_lane = cell % (total_x * nz) + lane_lo
    source = jnp.stack([src_row, src_lane]).astype(jnp.int32)

    stack = jnp.concatenate(
        [forward_start[0], adjoint_end[0], velocity[None], attenuation[None]], axis=0
    )
    pieces = send_pieces(stack, frame)

    ext_shape = (frame.ey, frame.el)
    forward_end, divs, pres = pl.pallas_call(
        lambda *refs: forward_kernel(frame, *refs),
        out_shape=(
            jax.ShapeDtypeStruct((1, 5, ny, lanes), jnp.float32),
            jax.ShapeDtypeStruct((STEPS, ny, lanes), jnp.float32),
            jax.ShapeDtypeStruct((STEPS, ny, lanes), jnp.float32),
        ),
        in_specs=[smem(), smem(), smem()] + [vmem()] * 9,
        out_specs=(vmem(), vmem(), vmem()),
        scratch_shapes=[pltpu.VMEM((7,) + ext_shape, jnp.float32)],
        compiler_params=pltpu.CompilerParams(vmem_limit_bytes=48 * 1024 * 1024),
    )(bounds, source, wavelet[0], stack, *pieces)

    recs = receiver_cells[0, 0]
    records = pres.reshape(STEPS, ny * lanes)[:, recs]
    resid = records - observed[0, :, 0]
    inject = jnp.stack(
        [jnp.zeros((ny * lanes,), jnp.float32).at[recs].add(resid[n]) for n in range(STEPS)]
    ).reshape(STEPS, ny, lanes)
    inject_pieces = send_pieces(inject, frame)

    adjoint_start, row_sums = pl.pallas_call(
        lambda *refs: adjoint_kernel(frame, *refs),
        out_shape=(
            jax.ShapeDtypeStruct((1, 5, ny, lanes), jnp.float32),
            jax.ShapeDtypeStruct((2, ny // BY, lanes), jnp.float32),
        ),
        in_specs=[smem()] + [vmem()] * 19,
        out_specs=(vmem(), vmem()),
        scratch_shapes=[pltpu.VMEM((10,) + ext_shape, jnp.float32)],
        compiler_params=pltpu.CompilerParams(vmem_limit_bytes=48 * 1024 * 1024),
    )(bounds, stack, *pieces, inject, *inject_pieces, divs)

    grad_scale = float(BY * BX * BZ) ** (-0.5)
    weight = aperture[0, 0].astype(jnp.float32)
    blocks = row_sums.reshape(2, ny // BY, nx // BX, BX, nz // BZ, BZ).sum(axis=(3, 5))
    sums = blocks.transpose(1, 2, 3, 0).reshape(-1, 2) * (grad_scale * weight)
    slots = block_slot[0]
    ordered = jnp.zeros(sums.shape, jnp.float32).at[slots].set(sums)
    shots = lax.axis_size("shot")
    parts = lax.all_to_all(
        ordered.reshape(shots, -1, 2), "shot", split_axis=0, concat_axis=0, tiled=True
    )
    coarse = jnp.sum(parts, axis=0)
    model_gradient = coarse.T[:, None, :]
    return (forward_end, adjoint_start, model_gradient)


def solution(mesh):
    placed = (
        P("shot", None, "gy", "gx"),
        P("shot", None, "gy", "gx"),
        P("gy", "gx"),
        P("gy", "gx"),
        P("shot", None),
        P("shot", None),
        P("shot", ("gy", "gx"), None),
        P("shot", None, ("gy", "gx"), None),
        P("shot", ("gy", "gx")),
        P(("gy", "gx"), None),
    )
    return jax.shard_map(
        on_device,
        mesh=mesh,
        in_specs=placed,
        out_specs=(
            P("shot", None, "gy", "gx"),
            P("shot", None, "gy", "gx"),
            P(None, ("gy", "gx"), "shot"),
        ),
        check_vma=False,
    )
```

```python
import jax
import jax.numpy as jnp
from jax import lax
from jax.experimental import pallas as pl
from jax.experimental.pallas import tpu as pltpu
from jax.sharding import PartitionSpec as P

CZ = 32
STEPS = 3
BY = 8
BX = 8
BZ = 8
HALO = 3 * STEPS

coef_near = 9.0 / 8.0
coef_far = -1.0 / 24.0
stiff_scale = 0.02
relax_rate = 0.3


def round_up(value, unit):
    return (value + unit - 1) // unit * unit


class Frame:
    def __init__(self, ny, lanes):
        self.ny = ny
        self.lanes = lanes
        self.oy = round_up(HALO, 8)
        self.ox = round_up(HALO * CZ, 128)
        self.ey = 2 * self.oy + ny
        self.el = 2 * self.ox + lanes


def send_pieces(stack, frame):
    ny, lanes, ox = frame.ny, frame.lanes, frame.ox
    lo_rows = stack[:, :HALO]
    hi_rows = stack[:, ny - HALO :]
    count_y = lax.axis_size("gy")
    count_x = lax.axis_size("gx")

    def move(piece, dy, dx):
        pairs = []
        for y in range(count_y):
            for x in range(count_x):
                ty, tx = y + dy, x + dx
                if 0 <= ty < count_y and 0 <= tx < count_x:
                    pairs.append((y * count_x + x, ty * count_x + tx))
        return lax.ppermute(piece, ("gy", "gx"), pairs)

    return (
        move(hi_rows, 1, 0),
        move(lo_rows, -1, 0),
        move(stack[:, :, lanes - ox :], 0, 1),
        move(stack[:, :, :ox], 0, -1),
        move(hi_rows[:, :, lanes - ox :], 1, 1),
        move(hi_rows[:, :, :ox], 1, -1),
        move(lo_rows[:, :, lanes - ox :], -1, 1),
        move(lo_rows[:, :, :ox], -1, -1),
    )


def assemble(dst, own, pieces, j, frame):
    ny, lanes, oy, ox, el = frame.ny, frame.lanes, frame.oy, frame.ox, frame.el
    below, above, left, right, b_l, b_r, a_l, a_r = pieces
    lo = slice(oy - HALO, oy)
    mid = slice(oy, oy + ny)
    hi = slice(oy + ny, oy + ny + HALO)
    west = slice(0, ox)
    centre = slice(ox, ox + lanes)
    east = slice(ox + lanes, el)
    dst[...] = jnp.zeros(dst.shape, dst.dtype)
    dst[mid, centre] = own[j]
    dst[lo, centre] = below[j]
    dst[hi, centre] = above[j]
    dst[mid, west] = left[j]
    dst[mid, east] = right[j]
    dst[lo, west] = b_l[j]
    dst[lo, east] = b_r[j]
    dst[hi, west] = a_l[j]
    dst[hi, east] = a_r[j]


def stepper(frame, bounds_ref):
    ey, el = frame.ey, frame.el
    row = lax.broadcasted_iota(jnp.int32, (ey, el), 0)
    lane = lax.broadcasted_iota(jnp.int32, (ey, el), 1)
    inside = (
        (row >= bounds_ref[0])
        & (row < bounds_ref[1])
        & (lane >= bounds_ref[2])
        & (lane < bounds_ref[3])
    )
    depth = lane % CZ
    zero = jnp.zeros((ey, el), jnp.float32)
    z_ok = {d: (depth + d >= 0) & (depth + d < CZ) for d in (-2, -1, 1, 2)}

    def rows(a, d):
        return a if d == 0 else pltpu.roll(a, (-d) % ey, 0)

    def lanes(a, d):
        return a if d == 0 else pltpu.roll(a, (-d) % el, 1)

    def deep(a, d):
        return a if d == 0 else jnp.where(z_ok[d], lanes(a, d), zero)

    def forward_diff(s):
        return coef_near * (s(1) - s(0)) + coef_far * (s(2) - s(-1))

    def backward_diff(s):
        return coef_near * (s(0) - s(-1)) + coef_far * (s(1) - s(-2))

    def wave_step(state, stiff, att):
        pres, vel_y, vel_x, vel_z, memory = state
        vel_y = jnp.where(inside, vel_y - forward_diff(lambda d: rows(pres, d)), zero)
        vel_x = jnp.where(inside, vel_x - forward_diff(lambda d: lanes(pres, d * CZ)), zero)
        vel_z = vel_z - forward_diff(lambda d: deep(pres, d))
        div = (
            backward_diff(lambda d: rows(vel_y, d))
            + backward_diff(lambda d: lanes(vel_x, d * CZ))
            + backward_diff(lambda d: deep(vel_z, d))
        )
        memory = memory - relax_rate * (memory + stiff * att * div)
        pres = jnp.where(inside, pres - stiff * (1.0 + att) * div - memory, zero)
        return [pres, vel_y, vel_x, vel_z, memory], div

    return wave_step, row, lane


def forward_kernel(frame, bounds_ref, source_ref, wave_ref, own_ref, *rest):
    pieces = rest[:8]
    gauge_ref, end_ref, div_ref, inject_ref, ext = rest[8:]
    for e, j in enumerate((0, 1, 2, 3, 4, 10, 11)):
        assemble(ext.at[e], own_ref, pieces, j, frame)
    wave_step, row, lane = stepper(frame, bounds_ref)
    source = (row == source_ref[0]) & (lane == source_ref[1])
    vel = ext[5]
    att = ext[6]
    stiff = stiff_scale * vel * vel
    state = [ext[k] for k in range(5)]
    mid = slice(frame.oy, frame.oy + frame.ny)
    centre = slice(frame.ox, frame.ox + frame.lanes)
    for step in range(STEPS):
        state, div = wave_step(state, stiff, att)
        state[0] = state[0] + jnp.where(source, wave_ref[step], jnp.float32(0.0))
        div_ref[step] = div[mid, centre]
        inject_ref[step] = gauge_ref[0] * state[0][mid, centre] - gauge_ref[1 + step]
    for k in range(5):
        end_ref[0, k] = state[k][mid, centre]


def adjoint_kernel(frame, bounds_ref, own_ref, *rest):
    pieces = rest[:8]
    inject_own = rest[8]
    inject_pieces = rest[9:17]
    div_ref, start_ref, grad_ref, ext = rest[17:]
    for e, j in enumerate((5, 6, 7, 8, 9, 10, 11)):
        assemble(ext.at[e], own_ref, pieces, j, frame)
    for n in range(STEPS):
        assemble(ext.at[7 + n], inject_own, inject_pieces, n, frame)
    wave_step, row, lane = stepper(frame, bounds_ref)
    vel = ext[5]
    att = ext[6]
    stiff = stiff_scale * vel * vel
    mid = slice(frame.oy, frame.oy + frame.ny)
    centre = slice(frame.ox, frame.ox + frame.lanes)
    velocity = vel[mid, centre]
    attenuation = att[mid, centre]
    stiff_own = stiff[mid, centre]
    adj = [ext[k] for k in range(5)]
    grad_v = jnp.zeros((frame.ny, frame.lanes), jnp.float32)
    grad_a = jnp.zeros((frame.ny, frame.lanes), jnp.float32)
    for step in range(STEPS - 1, -1, -1):
        adj, unused = wave_step(adj, stiff, att)
        adj[0] = adj[0] + ext[7 + step]
        div = div_ref[step]
        q = adj[0][mid, centre]
        m = adj[4][mid, centre]
        deriv_q = (relax_rate * attenuation - (1.0 + attenuation)) * div
        deriv_m = -relax_rate * attenuation * div
        grad_v = grad_v + (q * deriv_q + m * deriv_m) * (2.0 * stiff_scale * velocity)
        grad_a = grad_a + (q * (relax_rate - 1.0) - m * relax_rate) * stiff_own * div
    for k in range(5):
        start_ref[0, k] = adj[k][mid, centre]
    for c, g in enumerate((grad_v, grad_a)):
        grad_ref[c] = g.reshape(frame.ny // BY, BY, frame.lanes).sum(axis=1)


def vmem():
    return pl.BlockSpec(memory_space=pltpu.VMEM)


def smem():
    return pl.BlockSpec(memory_space=pltpu.SMEM)


def on_device(
    forward_start,
    adjoint_end,
    velocity,
    attenuation,
    wavelet,
    source_cell,
    receiver_cells,
    observed,
    aperture,
    block_slot,
):
    nz = CZ
    ny = velocity.shape[0]
    lanes = velocity.shape[1]
    nx = lanes // nz
    frame = Frame(ny, lanes)
    index_y = lax.axis_index("gy")
    index_x = lax.axis_index("gx")
    total_y = ny * lax.axis_size("gy")
    total_x = nx * lax.axis_size("gx")

    row_lo = frame.oy - index_y * ny
    lane_lo = frame.ox - index_x * lanes
    bounds = jnp.stack([row_lo, row_lo + total_y, lane_lo, lane_lo + total_x * nz]).astype(jnp.int32)

    cell = source_cell[0, 0]
    src_row = cell // (total_x * nz) + row_lo
    src_lane = cell % (total_x * nz) + lane_lo
    source = jnp.stack([src_row, src_lane]).astype(jnp.int32)

    stack = jnp.concatenate(
        [forward_start[0], adjoint_end[0], velocity[None], attenuation[None]], axis=0
    )
    pieces = send_pieces(stack, frame)

    ext_shape = (frame.ey, frame.el)
    recs = receiver_cells[0, 0]
    gauge = jnp.stack(
        [jnp.zeros((ny * lanes,), jnp.float32).at[recs].add(1.0)]
        + [jnp.zeros((ny * lanes,), jnp.float32).at[recs].add(observed[0, n, 0]) for n in range(STEPS)]
    ).reshape(1 + STEPS, ny, lanes)

    forward_end, divs, inject = pl.pallas_call(
        lambda *refs: forward_kernel(frame, *refs),
        out_shape=(
            jax.ShapeDtypeStruct((1, 5, ny, lanes), jnp.float32),
            jax.ShapeDtypeStruct((STEPS, ny, lanes), jnp.float32),
            jax.ShapeDtypeStruct((STEPS, ny, lanes), jnp.float32),
        ),
        in_specs=[smem(), smem(), smem()] + [vmem()] * 10,
        out_specs=(vmem(), vmem(), vmem()),
        scratch_shapes=[pltpu.VMEM((7,) + ext_shape, jnp.float32)],
        compiler_params=pltpu.CompilerParams(vmem_limit_bytes=48 * 1024 * 1024),
    )(bounds, source, wavelet[0], stack, *pieces, gauge)
    inject_pieces = send_pieces(inject, frame)

    adjoint_start, row_sums = pl.pallas_call(
        lambda *refs: adjoint_kernel(frame, *refs),
        out_shape=(
            jax.ShapeDtypeStruct((1, 5, ny, lanes), jnp.float32),
            jax.ShapeDtypeStruct((2, ny // BY, lanes), jnp.float32),
        ),
        in_specs=[smem()] + [vmem()] * 19,
        out_specs=(vmem(), vmem()),
        scratch_shapes=[pltpu.VMEM((10,) + ext_shape, jnp.float32)],
        compiler_params=pltpu.CompilerParams(vmem_limit_bytes=48 * 1024 * 1024),
    )(bounds, stack, *pieces, inject, *inject_pieces, divs)

    grad_scale = float(BY * BX * BZ) ** (-0.5)
    weight = aperture[0, 0].astype(jnp.float32)
    blocks = row_sums.reshape(2, ny // BY, nx // BX, BX, nz // BZ, BZ).sum(axis=(3, 5))
    sums = blocks.transpose(1, 2, 3, 0).reshape(-1, 2) * (grad_scale * weight)
    slots = block_slot[0]
    ordered = jnp.zeros(sums.shape, jnp.float32).at[slots].set(sums)
    shots = lax.axis_size("shot")
    parts = lax.all_to_all(
        ordered.reshape(shots, -1, 2), "shot", split_axis=0, concat_axis=0, tiled=True
    )
    coarse = jnp.sum(parts, axis=0)
    model_gradient = coarse.T[:, None, :]
    return (forward_end, adjoint_start, model_gradient)


def solution(mesh):
    placed = (
        P("shot", None, "gy", "gx"),
        P("shot", None, "gy", "gx"),
        P("gy", "gx"),
        P("gy", "gx"),
        P("shot", None),
        P("shot", None),
        P("shot", ("gy", "gx"), None),
        P("shot", None, ("gy", "gx"), None),
        P("shot", ("gy", "gx")),
        P(("gy", "gx"), None),
    )
    return jax.shard_map(
        on_device,
        mesh=mesh,
        in_specs=placed,
        out_specs=(
            P("shot", None, "gy", "gx"),
            P("shot", None, "gy", "gx"),
            P(None, ("gy", "gx"), "shot"),
        ),
        check_vma=False,
    )
```

```python
import jax
import jax.numpy as jnp
from jax import lax
from jax.experimental import pallas as pl
from jax.experimental.pallas import tpu as pltpu
from jax.sharding import PartitionSpec as P

CZ = 32
STEPS = 3
BY = 8
BX = 8
BZ = 8
HALO = 3 * STEPS + 3 * (STEPS - 1)

coef_near = 9.0 / 8.0
coef_far = -1.0 / 24.0
stiff_scale = 0.02
relax_rate = 0.3


def round_up(value, unit):
    return (value + unit - 1) // unit * unit


class Frame:
    def __init__(self, ny, lanes):
        self.ny = ny
        self.lanes = lanes
        self.oy = round_up(HALO, 8)
        self.ox = round_up(HALO * CZ, 128)
        self.ey = 2 * self.oy + ny
        self.el = 2 * self.ox + lanes


def send_pieces(stack, frame):
    ny, lanes, ox = frame.ny, frame.lanes, frame.ox
    lo_rows = stack[:, :HALO]
    hi_rows = stack[:, ny - HALO :]
    count_y = lax.axis_size("gy")
    count_x = lax.axis_size("gx")

    def move(piece, dy, dx):
        pairs = []
        for y in range(count_y):
            for x in range(count_x):
                ty, tx = y + dy, x + dx
                if 0 <= ty < count_y and 0 <= tx < count_x:
                    pairs.append((y * count_x + x, ty * count_x + tx))
        return lax.ppermute(piece, ("gy", "gx"), pairs)

    return (
        move(hi_rows, 1, 0),
        move(lo_rows, -1, 0),
        move(stack[:, :, lanes - ox :], 0, 1),
        move(stack[:, :, :ox], 0, -1),
        move(hi_rows[:, :, lanes - ox :], 1, 1),
        move(hi_rows[:, :, :ox], 1, -1),
        move(lo_rows[:, :, lanes - ox :], -1, 1),
        move(lo_rows[:, :, :ox], -1, -1),
    )


def assemble(dst, own, pieces, j, frame):
    ny, lanes, oy, ox, el = frame.ny, frame.lanes, frame.oy, frame.ox, frame.el
    below, above, left, right, b_l, b_r, a_l, a_r = pieces
    lo = slice(oy - HALO, oy)
    mid = slice(oy, oy + ny)
    hi = slice(oy + ny, oy + ny + HALO)
    west = slice(0, ox)
    centre = slice(ox, ox + lanes)
    east = slice(ox + lanes, el)
    dst[...] = jnp.zeros(dst.shape, dst.dtype)
    dst[mid, centre] = own[j]
    dst[lo, centre] = below[j]
    dst[hi, centre] = above[j]
    dst[mid, west] = left[j]
    dst[mid, east] = right[j]
    dst[lo, west] = b_l[j]
    dst[lo, east] = b_r[j]
    dst[hi, west] = a_l[j]
    dst[hi, east] = a_r[j]


def stepper(frame, bounds_ref):
    ey, el = frame.ey, frame.el
    row = lax.broadcasted_iota(jnp.int32, (ey, el), 0)
    lane = lax.broadcasted_iota(jnp.int32, (ey, el), 1)
    inside = (
        (row >= bounds_ref[0])
        & (row < bounds_ref[1])
        & (lane >= bounds_ref[2])
        & (lane < bounds_ref[3])
    )
    depth = lane % CZ
    zero = jnp.zeros((ey, el), jnp.float32)
    z_ok = {d: (depth + d >= 0) & (depth + d < CZ) for d in (-2, -1, 1, 2)}

    def rows(a, d):
        return a if d == 0 else pltpu.roll(a, (-d) % ey, 0)

    def lanes(a, d):
        return a if d == 0 else pltpu.roll(a, (-d) % el, 1)

    def deep(a, d):
        return a if d == 0 else jnp.where(z_ok[d], lanes(a, d), zero)

    def forward_diff(s):
        return coef_near * (s(1) - s(0)) + coef_far * (s(2) - s(-1))

    def backward_diff(s):
        return coef_near * (s(0) - s(-1)) + coef_far * (s(1) - s(-2))

    def wave_step(state, stiff, att):
        pres, vel_y, vel_x, vel_z, memory = state
        vel_y = jnp.where(inside, vel_y - forward_diff(lambda d: rows(pres, d)), zero)
        vel_x = jnp.where(inside, vel_x - forward_diff(lambda d: lanes(pres, d * CZ)), zero)
        vel_z = vel_z - forward_diff(lambda d: deep(pres, d))
        div = (
            backward_diff(lambda d: rows(vel_y, d))
            + backward_diff(lambda d: lanes(vel_x, d * CZ))
            + backward_diff(lambda d: deep(vel_z, d))
        )
        memory = memory - relax_rate * (memory + stiff * att * div)
        pres = jnp.where(inside, pres - stiff * (1.0 + att) * div - memory, zero)
        return [pres, vel_y, vel_x, vel_z, memory], div

    return wave_step, row, lane


def window_kernel(frame, bounds_ref, source_ref, wave_ref, own_ref, *rest):
    pieces = rest[:8]
    end_ref, start_ref, grad_ref, ext, inject, divs = rest[8:]
    for j in range(16):
        assemble(ext.at[j], own_ref, pieces, j, frame)
    wave_step, row, lane = stepper(frame, bounds_ref)
    source = (row == source_ref[0]) & (lane == source_ref[1])
    vel = ext[10]
    att = ext[11]
    stiff = stiff_scale * vel * vel
    mid = slice(frame.oy, frame.oy + frame.ny)
    centre = slice(frame.ox, frame.ox + frame.lanes)
    state = [ext[k] for k in range(5)]
    for step in range(STEPS):
        state, div = wave_step(state, stiff, att)
        state[0] = state[0] + jnp.where(source, wave_ref[step], jnp.float32(0.0))
        divs[step] = div[mid, centre]
        inject[step] = ext[12] * state[0] - ext[13 + step]
    for k in range(5):
        end_ref[0, k] = state[k][mid, centre]

    velocity = vel[mid, centre]
    attenuation = att[mid, centre]
    stiff_own = stiff[mid, centre]
    adj = [ext[5 + k] for k in range(5)]
    grad_v = jnp.zeros((frame.ny, frame.lanes), jnp.float32)
    grad_a = jnp.zeros((frame.ny, frame.lanes), jnp.float32)
    for step in range(STEPS - 1, -1, -1):
        adj, unused = wave_step(adj, stiff, att)
        adj[0] = adj[0] + inject[step]
        div = divs[step]
        q = adj[0][mid, centre]
        m = adj[4][mid, centre]
        deriv_q = (relax_rate * attenuation - (1.0 + attenuation)) * div
        deriv_m = -relax_rate * attenuation * div
        grad_v = grad_v + (q * deriv_q + m * deriv_m) * (2.0 * stiff_scale * velocity)
        grad_a = grad_a + (q * (relax_rate - 1.0) - m * relax_rate) * stiff_own * div
    for k in range(5):
        start_ref[0, k] = adj[k][mid, centre]
    for c, g in enumerate((grad_v, grad_a)):
        grad_ref[c] = g.reshape(frame.ny // BY, BY, frame.lanes).sum(axis=1)


def vmem():
    return pl.BlockSpec(memory_space=pltpu.VMEM)


def smem():
    return pl.BlockSpec(memory_space=pltpu.SMEM)


def on_device(
    forward_start,
    adjoint_end,
    velocity,
    attenuation,
    wavelet,
    source_cell,
    receiver_cells,
    observed,
    aperture,
    block_slot,
):
    nz = CZ
    ny = velocity.shape[0]
    lanes = velocity.shape[1]
    nx = lanes // nz
    frame = Frame(ny, lanes)
    index_y = lax.axis_index("gy")
    index_x = lax.axis_index("gx")
    total_y = ny * lax.axis_size("gy")
    total_x = nx * lax.axis_size("gx")

    row_lo = frame.oy - index_y * ny
    lane_lo = frame.ox - index_x * lanes
    bounds = jnp.stack([row_lo, row_lo + total_y, lane_lo, lane_lo + total_x * nz]).astype(jnp.int32)

    cell = source_cell[0, 0]
    src_row = cell // (total_x * nz) + row_lo
    src_lane = cell % (total_x * nz) + lane_lo
    source = jnp.stack([src_row, src_lane]).astype(jnp.int32)

    recs = receiver_cells[0, 0]
    at_row = (recs // lanes)[:, None] == lax.broadcasted_iota(jnp.int32, (recs.shape[0], ny), 1)
    at_lane = (recs % lanes)[:, None] == lax.broadcasted_iota(jnp.int32, (recs.shape[0], lanes), 1)
    weights = jnp.concatenate([jnp.ones((1, recs.shape[0]), jnp.float32), observed[0, :, 0]], axis=0)
    gauge = jnp.einsum(
        "nky,kl->nyl",
        weights[:, :, None] * at_row.astype(jnp.float32)[None],
        at_lane.astype(jnp.float32),
        precision=lax.Precision.HIGHEST,
    )

    stack = jnp.concatenate(
        [forward_start[0], adjoint_end[0], velocity[None], attenuation[None], gauge], axis=0
    )
    pieces = send_pieces(stack, frame)

    ext_shape = (frame.ey, frame.el)
    forward_end, adjoint_start, row_sums = pl.pallas_call(
        lambda *refs: window_kernel(frame, *refs),
        out_shape=(
            jax.ShapeDtypeStruct((1, 5, ny, lanes), jnp.float32),
            jax.ShapeDtypeStruct((1, 5, ny, lanes), jnp.float32),
            jax.ShapeDtypeStruct((2, ny // BY, lanes), jnp.float32),
        ),
        in_specs=[smem(), smem(), smem()] + [vmem()] * 9,
        out_specs=(vmem(), vmem(), vmem()),
        scratch_shapes=[
            pltpu.VMEM((16,) + ext_shape, jnp.float32),
            pltpu.VMEM((STEPS,) + ext_shape, jnp.float32),
            pltpu.VMEM((STEPS, ny, lanes), jnp.float32),
        ],
        compiler_params=pltpu.CompilerParams(vmem_limit_bytes=48 * 1024 * 1024),
    )(bounds, source, wavelet[0], stack, *pieces)

    grad_scale = float(BY * BX * BZ) ** (-0.5)
    weight = aperture[0, 0].astype(jnp.float32)
    blocks = row_sums.reshape(2, ny // BY, nx // BX, BX, nz // BZ, BZ).sum(axis=(3, 5))
    sums = blocks.transpose(1, 2, 3, 0).reshape(-1, 2) * (grad_scale * weight)
    slots = block_slot[0]
    ordered = jnp.zeros(sums.shape, jnp.float32).at[slots].set(sums)
    shots = lax.axis_size("shot")
    parts = lax.all_to_all(
        ordered.reshape(shots, -1, 2), "shot", split_axis=0, concat_axis=0, tiled=True
    )
    coarse = jnp.sum(parts, axis=0)
    model_gradient = coarse.T[:, None, :]
    return (forward_end, adjoint_start, model_gradient)


def solution(mesh):
    placed = (
        P("shot", None, "gy", "gx"),
        P("shot", None, "gy", "gx"),
        P("gy", "gx"),
        P("gy", "gx"),
        P("shot", None),
        P("shot", None),
        P("shot", ("gy", "gx"), None),
        P("shot", None, ("gy", "gx"), None),
        P("shot", ("gy", "gx")),
        P(("gy", "gx"), None),
    )
    return jax.shard_map(
        on_device,
        mesh=mesh,
        in_specs=placed,
        out_specs=(
            P("shot", None, "gy", "gx"),
            P("shot", None, "gy", "gx"),
            P(None, ("gy", "gx"), "shot"),
        ),
        check_vma=False,
    )
```

```python
import jax
import jax.numpy as jnp
from jax import lax
from jax.experimental import pallas as pl
from jax.experimental.pallas import tpu as pltpu
from jax.sharding import PartitionSpec as P

CZ = 32
STEPS = 3
BY = 8
BX = 8
BZ = 8
HALO = 3 * STEPS + 3 * (STEPS - 1)

coef_near = 9.0 / 8.0
coef_far = -1.0 / 24.0
stiff_scale = 0.02
relax_rate = 0.3


def round_up(value, unit):
    return (value + unit - 1) // unit * unit


class Frame:
    def __init__(self, ny, lanes):
        self.ny = ny
        self.lanes = lanes
        self.oy = round_up(HALO, 8)
        self.ox = round_up(HALO * CZ, 128)
        self.ey = 2 * self.oy + ny
        self.el = 2 * self.ox + lanes


def lane_halo(halo):
    return round_up(halo * CZ, 128)


def send_pieces(stack, frame, halo):
    ny, lanes, ox = frame.ny, frame.lanes, lane_halo(halo)
    lo_rows = stack[:, :halo]
    hi_rows = stack[:, ny - halo :]
    count_y = lax.axis_size("gy")
    count_x = lax.axis_size("gx")

    def move(piece, dy, dx):
        pairs = []
        for y in range(count_y):
            for x in range(count_x):
                ty, tx = y + dy, x + dx
                if 0 <= ty < count_y and 0 <= tx < count_x:
                    pairs.append((y * count_x + x, ty * count_x + tx))
        return lax.ppermute(piece, ("gy", "gx"), pairs)

    return (
        move(hi_rows, 1, 0),
        move(lo_rows, -1, 0),
        move(stack[:, :, lanes - ox :], 0, 1),
        move(stack[:, :, :ox], 0, -1),
        move(hi_rows[:, :, lanes - ox :], 1, 1),
        move(hi_rows[:, :, :ox], 1, -1),
        move(lo_rows[:, :, lanes - ox :], -1, 1),
        move(lo_rows[:, :, :ox], -1, -1),
    )


def assemble(dst, own, pieces, j, frame, halo):
    ny, lanes, oy, ox = frame.ny, frame.lanes, frame.oy, frame.ox
    w = lane_halo(halo)
    below, above, left, right, b_l, b_r, a_l, a_r = pieces
    lo = slice(oy - halo, oy)
    mid = slice(oy, oy + ny)
    hi = slice(oy + ny, oy + ny + halo)
    west = slice(ox - w, ox)
    centre = slice(ox, ox + lanes)
    east = slice(ox + lanes, ox + lanes + w)
    dst[...] = jnp.zeros(dst.shape, dst.dtype)
    dst[mid, centre] = own[j]
    dst[lo, centre] = below[j]
    dst[hi, centre] = above[j]
    dst[mid, west] = left[j]
    dst[mid, east] = right[j]
    dst[lo, west] = b_l[j]
    dst[lo, east] = b_r[j]
    dst[hi, west] = a_l[j]
    dst[hi, east] = a_r[j]


def stepper(frame, bounds_ref):
    ey, el = frame.ey, frame.el
    row = lax.broadcasted_iota(jnp.int32, (ey, el), 0)
    lane = lax.broadcasted_iota(jnp.int32, (ey, el), 1)
    inside = (
        (row >= bounds_ref[0])
        & (row < bounds_ref[1])
        & (lane >= bounds_ref[2])
        & (lane < bounds_ref[3])
    )
    depth = lane % CZ
    zero = jnp.zeros((ey, el), jnp.float32)
    z_ok = {d: (depth + d >= 0) & (depth + d < CZ) for d in (-2, -1, 1, 2)}

    def rows(a, d):
        return a if d == 0 else pltpu.roll(a, (-d) % ey, 0)

    def lanes(a, d):
        return a if d == 0 else pltpu.roll(a, (-d) % el, 1)

    def deep(a, d):
        return a if d == 0 else jnp.where(z_ok[d], lanes(a, d), zero)

    def forward_diff(s):
        return coef_near * (s(1) - s(0)) + coef_far * (s(2) - s(-1))

    def backward_diff(s):
        return coef_near * (s(0) - s(-1)) + coef_far * (s(1) - s(-2))

    def wave_step(state, stiff, att):
        pres, vel_y, vel_x, vel_z, memory = state
        vel_y = jnp.where(inside, vel_y - forward_diff(lambda d: rows(pres, d)), zero)
        vel_x = jnp.where(inside, vel_x - forward_diff(lambda d: lanes(pres, d * CZ)), zero)
        vel_z = vel_z - forward_diff(lambda d: deep(pres, d))
        div = (
            backward_diff(lambda d: rows(vel_y, d))
            + backward_diff(lambda d: lanes(vel_x, d * CZ))
            + backward_diff(lambda d: deep(vel_z, d))
        )
        memory = memory - relax_rate * (memory + stiff * att * div)
        pres = jnp.where(inside, pres - stiff * (1.0 + att) * div - memory, zero)
        return [pres, vel_y, vel_x, vel_z, memory], div

    return wave_step, row, lane


def forward_kernel(frame, bounds_ref, source_ref, wave_ref, own_ref, *rest):
    pieces = rest[:8]
    end_ref, div_ref, pres_ref, ext = rest[8:]
    for j in range(7):
        assemble(ext.at[j], own_ref, pieces, j, frame, HALO)
    wave_step, row, lane = stepper(frame, bounds_ref)
    source = (row == source_ref[0]) & (lane == source_ref[1])
    vel = ext[5]
    att = ext[6]
    stiff = stiff_scale * vel * vel
    mid = slice(frame.oy, frame.oy + frame.ny)
    centre = slice(frame.ox, frame.ox + frame.lanes)
    state = [ext[k] for k in range(5)]
    for step in range(STEPS):
        state, div = wave_step(state, stiff, att)
        state[0] = state[0] + jnp.where(source, wave_ref[step], jnp.float32(0.0))
        div_ref[step] = div[mid, centre]
        pres_ref[step] = state[0]
    for k in range(5):
        end_ref[0, k] = state[k][mid, centre]


def adjoint_kernel(frame, bounds_ref, model_ref, model_pieces_ref, *rest):
    model_pieces = (model_pieces_ref,) + rest[:7]
    own_ref = rest[7]
    pieces = rest[8:16]
    first_ref, pres_ref, div_ref, start_ref, grad_ref, ext, field = rest[16:]
    for e in range(2):
        assemble(field.at[e], model_ref, model_pieces, 5 + e, frame, HALO)
    for j in range(8):
        assemble(ext.at[j], own_ref, pieces, j, frame, 3 * STEPS)
    wave_step, row, lane = stepper(frame, bounds_ref)
    vel = field[0]
    att = field[1]
    stiff = stiff_scale * vel * vel
    mid = slice(frame.oy, frame.oy + frame.ny)
    centre = slice(frame.ox, frame.ox + frame.lanes)
    velocity = vel[mid, centre]
    attenuation = att[mid, centre]
    stiff_own = stiff[mid, centre]
    adj = [ext[k] for k in range(5)]
    grad_v = jnp.zeros((frame.ny, frame.lanes), jnp.float32)
    grad_a = jnp.zeros((frame.ny, frame.lanes), jnp.float32)
    for step in range(STEPS - 1, -1, -1):
        adj, unused = wave_step(adj, stiff, att)
        if step == 0:
            q = adj[0][mid, centre] + (
                ext[5][mid, centre] * pres_ref[0][mid, centre] - first_ref[...]
            )
        else:
            adj[0] = adj[0] + (ext[5] * pres_ref[step] - ext[5 + step])
            q = adj[0][mid, centre]
        div = div_ref[step]
        m = adj[4][mid, centre]
        deriv_q = (relax_rate * attenuation - (1.0 + attenuation)) * div
        deriv_m = -relax_rate * attenuation * div
        grad_v = grad_v + (q * deriv_q + m * deriv_m) * (2.0 * stiff_scale * velocity)
        grad_a = grad_a + (q * (relax_rate - 1.0) - m * relax_rate) * stiff_own * div
    start_ref[0, 0] = q
    for k in range(1, 5):
        start_ref[0, k] = adj[k][mid, centre]
    for c, g in enumerate((grad_v, grad_a)):
        grad_ref[c] = g.reshape(frame.ny // BY, BY, frame.lanes).sum(axis=1)


def vmem():
    return pl.BlockSpec(memory_space=pltpu.VMEM)


def smem():
    return pl.BlockSpec(memory_space=pltpu.SMEM)


def on_device(
    forward_start,
    adjoint_end,
    velocity,
    attenuation,
    wavelet,
    source_cell,
    receiver_cells,
    observed,
    aperture,
    block_slot,
):
    nz = CZ
    ny = velocity.shape[0]
    lanes = velocity.shape[1]
    nx = lanes // nz
    frame = Frame(ny, lanes)
    index_y = lax.axis_index("gy")
    index_x = lax.axis_index("gx")
    total_y = ny * lax.axis_size("gy")
    total_x = nx * lax.axis_size("gx")

    row_lo = frame.oy - index_y * ny
    lane_lo = frame.ox - index_x * lanes
    bounds = jnp.stack([row_lo, row_lo + total_y, lane_lo, lane_lo + total_x * nz]).astype(jnp.int32)

    cell = source_cell[0, 0]
    src_row = cell // (total_x * nz) + row_lo
    src_lane = cell % (total_x * nz) + lane_lo
    source = jnp.stack([src_row, src_lane]).astype(jnp.int32)

    recs = receiver_cells[0, 0]
    at_row = (recs // lanes)[:, None] == lax.broadcasted_iota(jnp.int32, (recs.shape[0], ny), 1)
    at_lane = (recs % lanes)[:, None] == lax.broadcasted_iota(jnp.int32, (recs.shape[0], lanes), 1)
    weights = jnp.concatenate([jnp.ones((1, recs.shape[0]), jnp.float32), observed[0, :, 0]], axis=0)
    gauge = jnp.einsum(
        "nky,kl->nyl",
        weights[:, :, None] * at_row.astype(jnp.float32)[None],
        at_lane.astype(jnp.float32),
        precision=lax.Precision.HIGHEST,
    )

    model = jnp.concatenate([forward_start[0], velocity[None], attenuation[None]], axis=0)
    model_pieces = send_pieces(model, frame, HALO)
    late = jnp.concatenate([adjoint_end[0], gauge[:1], gauge[2:]], axis=0)
    late_pieces = send_pieces(late, frame, 3 * STEPS)

    ext_shape = (frame.ey, frame.el)
    forward_end, divs, pres = pl.pallas_call(
        lambda *refs: forward_kernel(frame, *refs),
        out_shape=(
            jax.ShapeDtypeStruct((1, 5, ny, lanes), jnp.float32),
            jax.ShapeDtypeStruct((STEPS, ny, lanes), jnp.float32),
            jax.ShapeDtypeStruct((STEPS,) + ext_shape, jnp.float32),
        ),
        in_specs=[smem(), smem(), smem()] + [vmem()] * 9,
        out_specs=(vmem(), vmem(), vmem()),
        scratch_shapes=[pltpu.VMEM((7,) + ext_shape, jnp.float32)],
        compiler_params=pltpu.CompilerParams(vmem_limit_bytes=48 * 1024 * 1024),
    )(bounds, source, wavelet[0], model, *model_pieces)

    adjoint_start, row_sums = pl.pallas_call(
        lambda *refs: adjoint_kernel(frame, *refs),
        out_shape=(
            jax.ShapeDtypeStruct((1, 5, ny, lanes), jnp.float32),
            jax.ShapeDtypeStruct((2, ny // BY, lanes), jnp.float32),
        ),
        in_specs=[smem()] + [vmem()] * 21,
        out_specs=(vmem(), vmem()),
        scratch_shapes=[
            pltpu.VMEM((8,) + ext_shape, jnp.float32),
            pltpu.VMEM((2,) + ext_shape, jnp.float32),
        ],
        compiler_params=pltpu.CompilerParams(vmem_limit_bytes=48 * 1024 * 1024),
    )(bounds, model, *model_pieces, late, *late_pieces, gauge[1], pres, divs)

    grad_scale = float(BY * BX * BZ) ** (-0.5)
    weight = aperture[0, 0].astype(jnp.float32)
    blocks = row_sums.reshape(2, ny // BY, nx // BX, BX, nz // BZ, BZ).sum(axis=(3, 5))
    sums = blocks.transpose(1, 2, 3, 0).reshape(-1, 2) * (grad_scale * weight)
    slots = block_slot[0]
    ordered = jnp.zeros(sums.shape, jnp.float32).at[slots].set(sums)
    shots = lax.axis_size("shot")
    parts = lax.all_to_all(
        ordered.reshape(shots, -1, 2), "shot", split_axis=0, concat_axis=0, tiled=True
    )
    coarse = jnp.sum(parts, axis=0)
    model_gradient = coarse.T[:, None, :]
    return (forward_end, adjoint_start, model_gradient)


def solution(mesh):
    placed = (
        P("shot", None, "gy", "gx"),
        P("shot", None, "gy", "gx"),
        P("gy", "gx"),
        P("gy", "gx"),
        P("shot", None),
        P("shot", None),
        P("shot", ("gy", "gx"), None),
        P("shot", None, ("gy", "gx"), None),
        P("shot", ("gy", "gx")),
        P(("gy", "gx"), None),
    )
    return jax.shard_map(
        on_device,
        mesh=mesh,
        in_specs=placed,
        out_specs=(
            P("shot", None, "gy", "gx"),
            P("shot", None, "gy", "gx"),
            P(None, ("gy", "gx"), "shot"),
        ),
        check_vma=False,
    )
```

```python
import jax
import jax.numpy as jnp
from jax import lax
from jax.experimental import pallas as pl
from jax.experimental.pallas import tpu as pltpu
from jax.sharding import PartitionSpec as P

CZ = 32
STEPS = 3
BY = 8
BX = 8
BZ = 8
HALO = 3 * STEPS + 3 * (STEPS - 1)

coef_near = 9.0 / 8.0
coef_far = -1.0 / 24.0
stiff_scale = 0.02
relax_rate = 0.3


def round_up(value, unit):
    return (value + unit - 1) // unit * unit


class Frame:
    def __init__(self, ny, lanes):
        self.ny = ny
        self.lanes = lanes
        self.oy = round_up(HALO, 8)
        self.ox = round_up(HALO * CZ, 128)
        self.ey = 2 * self.oy + ny
        self.el = 2 * self.ox + lanes


def lane_halo(halo):
    return round_up(halo * CZ, 128)


def send_pieces(stack, frame, halo):
    ny, lanes, ox = frame.ny, frame.lanes, lane_halo(halo)
    lo_rows = stack[:, :halo]
    hi_rows = stack[:, ny - halo :]
    count_y = lax.axis_size("gy")
    count_x = lax.axis_size("gx")

    def move(piece, dy, dx):
        pairs = []
        for y in range(count_y):
            for x in range(count_x):
                ty, tx = y + dy, x + dx
                if 0 <= ty < count_y and 0 <= tx < count_x:
                    pairs.append((y * count_x + x, ty * count_x + tx))
        return lax.ppermute(piece, ("gy", "gx"), pairs)

    return (
        move(hi_rows, 1, 0),
        move(lo_rows, -1, 0),
        move(stack[:, :, lanes - ox :], 0, 1),
        move(stack[:, :, :ox], 0, -1),
        move(hi_rows[:, :, lanes - ox :], 1, 1),
        move(hi_rows[:, :, :ox], 1, -1),
        move(lo_rows[:, :, lanes - ox :], -1, 1),
        move(lo_rows[:, :, :ox], -1, -1),
    )


def assemble(dst, own, pieces, j, frame, halo):
    ny, lanes, oy, ox = frame.ny, frame.lanes, frame.oy, frame.ox
    w = lane_halo(halo)
    below, above, left, right, b_l, b_r, a_l, a_r = pieces
    lo = slice(oy - halo, oy)
    mid = slice(oy, oy + ny)
    hi = slice(oy + ny, oy + ny + halo)
    west = slice(ox - w, ox)
    centre = slice(ox, ox + lanes)
    east = slice(ox + lanes, ox + lanes + w)
    dst[...] = jnp.zeros(dst.shape, dst.dtype)
    dst[mid, centre] = own[j]
    dst[lo, centre] = below[j]
    dst[hi, centre] = above[j]
    dst[mid, west] = left[j]
    dst[mid, east] = right[j]
    dst[lo, west] = b_l[j]
    dst[lo, east] = b_r[j]
    dst[hi, west] = a_l[j]
    dst[hi, east] = a_r[j]


def stepper(frame, bounds_ref):
    ey, el = frame.ey, frame.el
    row = lax.broadcasted_iota(jnp.int32, (ey, el), 0)
    lane = lax.broadcasted_iota(jnp.int32, (ey, el), 1)
    inside = (
        (row >= bounds_ref[0])
        & (row < bounds_ref[1])
        & (lane >= bounds_ref[2])
        & (lane < bounds_ref[3])
    )
    depth = lane % CZ
    zero = jnp.zeros((ey, el), jnp.float32)
    z_ok = {d: (depth + d >= 0) & (depth + d < CZ) for d in (-2, -1, 1, 2)}

    def rows(a, d):
        return a if d == 0 else pltpu.roll(a, (-d) % ey, 0)

    def lanes(a, d):
        return a if d == 0 else pltpu.roll(a, (-d) % el, 1)

    def deep(a, d):
        return a if d == 0 else jnp.where(z_ok[d], lanes(a, d), zero)

    def forward_diff(s):
        return coef_near * (s(1) - s(0)) + coef_far * (s(2) - s(-1))

    def backward_diff(s):
        return coef_near * (s(0) - s(-1)) + coef_far * (s(1) - s(-2))

    def wave_step(state, stiff, att):
        pres, vel_y, vel_x, vel_z, memory = state
        vel_y = jnp.where(inside, vel_y - forward_diff(lambda d: rows(pres, d)), zero)
        vel_x = jnp.where(inside, vel_x - forward_diff(lambda d: lanes(pres, d * CZ)), zero)
        vel_z = vel_z - forward_diff(lambda d: deep(pres, d))
        div = (
            backward_diff(lambda d: rows(vel_y, d))
            + backward_diff(lambda d: lanes(vel_x, d * CZ))
            + backward_diff(lambda d: deep(vel_z, d))
        )
        memory = memory - relax_rate * (memory + stiff * att * div)
        pres = jnp.where(inside, pres - stiff * (1.0 + att) * div - memory, zero)
        return [pres, vel_y, vel_x, vel_z, memory], div

    return wave_step, row, lane


def forward_kernel(frame, bounds_ref, source_ref, wave_ref, own_ref, *rest):
    pieces = rest[:8]
    end_ref, div_ref, pres_ref, ext = rest[8:]
    for j in range(7):
        assemble(ext.at[j], own_ref, pieces, j, frame, HALO)
    wave_step, row, lane = stepper(frame, bounds_ref)
    source = (row == source_ref[0]) & (lane == source_ref[1])
    vel = ext[5]
    att = ext[6]
    stiff = stiff_scale * vel * vel
    mid = slice(frame.oy, frame.oy + frame.ny)
    centre = slice(frame.ox, frame.ox + frame.lanes)
    state = [ext[k] for k in range(5)]
    for step in range(STEPS):
        state, div = wave_step(state, stiff, att)
        state[0] = state[0] + jnp.where(source, wave_ref[step], jnp.float32(0.0))
        div_ref[step] = div[mid, centre]
        pres_ref[step] = state[0]
    for k in range(5):
        end_ref[0, k] = state[k][mid, centre]


def adjoint_kernel(frame, bounds_ref, model_ref, model_pieces_ref, *rest):
    model_pieces = (model_pieces_ref,) + rest[:7]
    own_ref = rest[7]
    pieces = rest[8:16]
    first_ref, pres_ref, div_ref, start_ref, grad_ref, ext, field = rest[16:]
    for e in range(2):
        assemble(field.at[e], model_ref, model_pieces, 5 + e, frame, HALO)
    for j in range(8):
        assemble(ext.at[j], own_ref, pieces, j, frame, 3 * STEPS)
    wave_step, row, lane = stepper(frame, bounds_ref)
    vel = field[0]
    att = field[1]
    stiff = stiff_scale * vel * vel
    mid = slice(frame.oy, frame.oy + frame.ny)
    centre = slice(frame.ox, frame.ox + frame.lanes)
    velocity = vel[mid, centre]
    attenuation = att[mid, centre]
    stiff_own = stiff[mid, centre]
    adj = [ext[k] for k in range(5)]
    grad_v = jnp.zeros((frame.ny, frame.lanes), jnp.float32)
    grad_a = jnp.zeros((frame.ny, frame.lanes), jnp.float32)
    for step in range(STEPS - 1, -1, -1):
        adj, unused = wave_step(adj, stiff, att)
        if step == 0:
            q = adj[0][mid, centre] + (
                ext[5][mid, centre] * pres_ref[0][mid, centre] - first_ref[...]
            )
        else:
            adj[0] = adj[0] + (ext[5] * pres_ref[step] - ext[5 + step])
            q = adj[0][mid, centre]
        div = div_ref[step]
        m = adj[4][mid, centre]
        deriv_q = (relax_rate * attenuation - (1.0 + attenuation)) * div
        deriv_m = -relax_rate * attenuation * div
        grad_v = grad_v + (q * deriv_q + m * deriv_m) * (2.0 * stiff_scale * velocity)
        grad_a = grad_a + (q * (relax_rate - 1.0) - m * relax_rate) * stiff_own * div
    start_ref[0, 0] = q
    for k in range(1, 5):
        start_ref[0, k] = adj[k][mid, centre]
    for c, g in enumerate((grad_v, grad_a)):
        grad_ref[c] = g.reshape(frame.ny // BY, BY, frame.lanes).sum(axis=1)


def vmem():
    return pl.BlockSpec(memory_space=pltpu.VMEM)


def smem():
    return pl.BlockSpec(memory_space=pltpu.SMEM)


def on_device(
    forward_start,
    adjoint_end,
    velocity,
    attenuation,
    wavelet,
    source_cell,
    receiver_cells,
    observed,
    aperture,
    block_slot,
):
    nz = CZ
    ny = velocity.shape[0]
    lanes = velocity.shape[1]
    nx = lanes // nz
    frame = Frame(ny, lanes)
    index_y = lax.axis_index("gy")
    index_x = lax.axis_index("gx")
    total_y = ny * lax.axis_size("gy")
    total_x = nx * lax.axis_size("gx")

    row_lo = frame.oy - index_y * ny
    lane_lo = frame.ox - index_x * lanes
    bounds = jnp.stack([row_lo, row_lo + total_y, lane_lo, lane_lo + total_x * nz]).astype(jnp.int32)

    cell = source_cell[0, 0]
    src_row = cell // (total_x * nz) + row_lo
    src_lane = cell % (total_x * nz) + lane_lo
    source = jnp.stack([src_row, src_lane]).astype(jnp.int32)

    recs = receiver_cells[0, 0]
    at_row = (recs // lanes)[:, None] == lax.broadcasted_iota(jnp.int32, (recs.shape[0], ny), 1)
    at_lane = (recs % lanes)[:, None] == lax.broadcasted_iota(jnp.int32, (recs.shape[0], lanes), 1)
    weights = jnp.concatenate([jnp.ones((1, recs.shape[0]), jnp.float32), observed[0, :, 0]], axis=0)
    gauge = jnp.einsum(
        "nky,kl->nyl",
        weights[:, :, None] * at_row.astype(jnp.float32)[None],
        at_lane.astype(jnp.float32),
        precision=lax.Precision.HIGHEST,
    )

    model = jnp.concatenate([forward_start[0], velocity[None], attenuation[None]], axis=0)
    model_pieces = send_pieces(model, frame, HALO)
    late = jnp.concatenate([adjoint_end[0], gauge[:1], gauge[2:]], axis=0)
    late, model_pieces = lax.optimization_barrier((late, model_pieces))
    late_pieces = send_pieces(late, frame, 3 * STEPS)

    ext_shape = (frame.ey, frame.el)
    forward_end, divs, pres = pl.pallas_call(
        lambda *refs: forward_kernel(frame, *refs),
        out_shape=(
            jax.ShapeDtypeStruct((1, 5, ny, lanes), jnp.float32),
            jax.ShapeDtypeStruct((STEPS, ny, lanes), jnp.float32),
            jax.ShapeDtypeStruct((STEPS,) + ext_shape, jnp.float32),
        ),
        in_specs=[smem(), smem(), smem()] + [vmem()] * 9,
        out_specs=(vmem(), vmem(), vmem()),
        scratch_shapes=[pltpu.VMEM((7,) + ext_shape, jnp.float32)],
        compiler_params=pltpu.CompilerParams(vmem_limit_bytes=48 * 1024 * 1024),
    )(bounds, source, wavelet[0], model, *model_pieces)

    adjoint_start, row_sums = pl.pallas_call(
        lambda *refs: adjoint_kernel(frame, *refs),
        out_shape=(
            jax.ShapeDtypeStruct((1, 5, ny, lanes), jnp.float32),
            jax.ShapeDtypeStruct((2, ny // BY, lanes), jnp.float32),
        ),
        in_specs=[smem()] + [vmem()] * 21,
        out_specs=(vmem(), vmem()),
        scratch_shapes=[
            pltpu.VMEM((8,) + ext_shape, jnp.float32),
            pltpu.VMEM((2,) + ext_shape, jnp.float32),
        ],
        compiler_params=pltpu.CompilerParams(vmem_limit_bytes=48 * 1024 * 1024),
    )(bounds, model, *model_pieces, late, *late_pieces, gauge[1], pres, divs)

    grad_scale = float(BY * BX * BZ) ** (-0.5)
    weight = aperture[0, 0].astype(jnp.float32)
    blocks = row_sums.reshape(2, ny // BY, nx // BX, BX, nz // BZ, BZ).sum(axis=(3, 5))
    sums = blocks.transpose(1, 2, 3, 0).reshape(-1, 2) * (grad_scale * weight)
    slots = block_slot[0]
    ordered = jnp.zeros(sums.shape, jnp.float32).at[slots].set(sums)
    shots = lax.axis_size("shot")
    parts = lax.all_to_all(
        ordered.reshape(shots, -1, 2), "shot", split_axis=0, concat_axis=0, tiled=True
    )
    coarse = jnp.sum(parts, axis=0)
    model_gradient = coarse.T[:, None, :]
    return (forward_end, adjoint_start, model_gradient)


def solution(mesh):
    placed = (
        P("shot", None, "gy", "gx"),
        P("shot", None, "gy", "gx"),
        P("gy", "gx"),
        P("gy", "gx"),
        P("shot", None),
        P("shot", None),
        P("shot", ("gy", "gx"), None),
        P("shot", None, ("gy", "gx"), None),
        P("shot", ("gy", "gx")),
        P(("gy", "gx"), None),
    )
    return jax.shard_map(
        on_device,
        mesh=mesh,
        in_specs=placed,
        out_specs=(
            P("shot", None, "gy", "gx"),
            P("shot", None, "gy", "gx"),
            P(None, ("gy", "gx"), "shot"),
        ),
        check_vma=False,
    )
```

```python
import jax
import jax.numpy as jnp
from jax import lax
from jax.experimental import pallas as pl
from jax.experimental.pallas import tpu as pltpu
from jax.sharding import PartitionSpec as P

CZ = 32
STEPS = 3
BY = 8
BX = 8
BZ = 8
HALO = 3 * STEPS + 3 * (STEPS - 1)

coef_near = 9.0 / 8.0
coef_far = -1.0 / 24.0
stiff_scale = 0.02
relax_rate = 0.3


def round_up(value, unit):
    return (value + unit - 1) // unit * unit


class Frame:
    def __init__(self, ny, lanes):
        self.ny = ny
        self.lanes = lanes
        self.oy = round_up(HALO, 8)
        self.ox = round_up(HALO * CZ, 128)
        self.ey = 2 * self.oy + ny
        self.el = 2 * self.ox + lanes


NEEDS = (
    (15, 15), (14, 12), (12, 14), (12, 12), (12, 12),
    (9, 9), (8, 6), (6, 8), (6, 6), (6, 6),
    (12, 12), (12, 12),
    (6, 6), (0, 0), (3, 3), (6, 6),
)


class Packing:
    def __init__(self, frame):
        self.rows = [h for h, w in NEEDS]
        self.lanes = [round_up(w * CZ, 128) for h, w in NEEDS]
        self.row_at = [sum(self.rows[:j]) for j in range(len(NEEDS))]
        self.lane_at = [sum(self.lanes[:j]) for j in range(len(NEEDS))]
        self.total_rows = sum(self.rows)
        self.total_lanes = sum(self.lanes)
        self.corner = frame.ox


def pack_kernel(frame, packing, fwd_ref, adj_ref, vel_ref, att_ref, gauge_ref, *outs):
    up, down, east, west, up_east, up_west, down_east, down_west = outs
    ny, lanes, cw = frame.ny, frame.lanes, packing.corner

    def field(j):
        if j < 5:
            return fwd_ref.at[0, j]
        if j < 10:
            return adj_ref.at[0, j - 5]
        if j == 10:
            return vel_ref
        if j == 11:
            return att_ref
        return gauge_ref.at[j - 12]

    for j in range(len(NEEDS)):
        h, w = packing.rows[j], packing.lanes[j]
        if h == 0:
            continue
        src = field(j)
        r = slice(packing.row_at[j], packing.row_at[j] + h)
        c = slice(packing.lane_at[j], packing.lane_at[j] + w)
        top = slice(ny - h, ny)
        bottom = slice(0, h)
        up[r, :] = src[top, :]
        down[r, :] = src[bottom, :]
        east[:, c] = src[:, lanes - w : lanes]
        west[:, c] = src[:, 0:w]
        up_east[r, :] = src[top, lanes - cw : lanes]
        up_west[r, :] = src[top, 0:cw]
        down_east[r, :] = src[bottom, lanes - cw : lanes]
        down_west[r, :] = src[bottom, 0:cw]


def send_pieces(packed):
    count_y = lax.axis_size("gy")
    count_x = lax.axis_size("gx")

    def move(piece, dy, dx):
        pairs = []
        for y in range(count_y):
            for x in range(count_x):
                ty, tx = y + dy, x + dx
                if 0 <= ty < count_y and 0 <= tx < count_x:
                    pairs.append((y * count_x + x, ty * count_x + tx))
        return lax.ppermute(piece, ("gy", "gx"), pairs)

    steps = ((1, 0), (-1, 0), (0, 1), (0, -1), (1, 1), (1, -1), (-1, 1), (-1, -1))
    return tuple(move(p, dy, dx) for p, (dy, dx) in zip(packed, steps))


def assemble(dst, own, pieces, j, frame, packing):
    ny, lanes, oy, ox, cw = frame.ny, frame.lanes, frame.oy, frame.ox, packing.corner
    below, above, left, right, b_l, b_r, a_l, a_r = pieces
    h, w = packing.rows[j], packing.lanes[j]
    dst[...] = jnp.zeros(dst.shape, dst.dtype)
    mid = slice(oy, oy + ny)
    centre = slice(ox, ox + lanes)
    dst[mid, centre] = own[...]
    if h == 0:
        return
    r = slice(packing.row_at[j], packing.row_at[j] + h)
    c = slice(packing.lane_at[j], packing.lane_at[j] + w)
    lo = slice(oy - h, oy)
    hi = slice(oy + ny, oy + ny + h)
    west = slice(ox - w, ox)
    east = slice(ox + lanes, ox + lanes + w)
    dst[lo, centre] = below[r, :]
    dst[hi, centre] = above[r, :]
    dst[mid, west] = left[:, c]
    dst[mid, east] = right[:, c]
    dst[lo, west] = b_l[r, cw - w : cw]
    dst[lo, east] = b_r[r, 0:w]
    dst[hi, west] = a_l[r, cw - w : cw]
    dst[hi, east] = a_r[r, 0:w]


def stepper(frame, bounds_ref):
    ey, el = frame.ey, frame.el
    row = lax.broadcasted_iota(jnp.int32, (ey, el), 0)
    lane = lax.broadcasted_iota(jnp.int32, (ey, el), 1)
    inside = (
        (row >= bounds_ref[0])
        & (row < bounds_ref[1])
        & (lane >= bounds_ref[2])
        & (lane < bounds_ref[3])
    )
    depth = lane % CZ
    zero = jnp.zeros((ey, el), jnp.float32)
    z_ok = {d: (depth + d >= 0) & (depth + d < CZ) for d in (-2, -1, 1, 2)}

    def rows(a, d):
        return a if d == 0 else pltpu.roll(a, (-d) % ey, 0)

    def lanes(a, d):
        return a if d == 0 else pltpu.roll(a, (-d) % el, 1)

    def deep(a, d):
        return a if d == 0 else jnp.where(z_ok[d], lanes(a, d), zero)

    def forward_diff(s):
        return coef_near * (s(1) - s(0)) + coef_far * (s(2) - s(-1))

    def backward_diff(s):
        return coef_near * (s(0) - s(-1)) + coef_far * (s(1) - s(-2))

    def wave_step(state, stiff, att):
        pres, vel_y, vel_x, vel_z, memory = state
        vel_y = jnp.where(inside, vel_y - forward_diff(lambda d: rows(pres, d)), zero)
        vel_x = jnp.where(inside, vel_x - forward_diff(lambda d: lanes(pres, d * CZ)), zero)
        vel_z = vel_z - forward_diff(lambda d: deep(pres, d))
        div = (
            backward_diff(lambda d: rows(vel_y, d))
            + backward_diff(lambda d: lanes(vel_x, d * CZ))
            + backward_diff(lambda d: deep(vel_z, d))
        )
        memory = memory - relax_rate * (memory + stiff * att * div)
        pres = jnp.where(inside, pres - stiff * (1.0 + att) * div - memory, zero)
        return [pres, vel_y, vel_x, vel_z, memory], div

    return wave_step, row, lane


def window_kernel(frame, packing, bounds_ref, source_ref, wave_ref, *rest):
    fwd_ref, adj_ref, vel_ref, att_ref, gauge_ref = rest[:5]
    pieces = rest[5:13]
    end_ref, start_ref, grad_ref, ext, inject, divs = rest[13:]
    owns = (
        [fwd_ref.at[0, k] for k in range(5)]
        + [adj_ref.at[0, k] for k in range(5)]
        + [vel_ref, att_ref]
        + [gauge_ref.at[k] for k in range(4)]
    )
    for j in range(16):
        assemble(ext.at[j], owns[j], pieces, j, frame, packing)
    wave_step, row, lane = stepper(frame, bounds_ref)
    source = (row == source_ref[0]) & (lane == source_ref[1])
    vel = ext[10]
    att = ext[11]
    stiff = stiff_scale * vel * vel
    mid = slice(frame.oy, frame.oy + frame.ny)
    centre = slice(frame.ox, frame.ox + frame.lanes)
    state = [ext[k] for k in range(5)]
    for step in range(STEPS):
        state, div = wave_step(state, stiff, att)
        state[0] = state[0] + jnp.where(source, wave_ref[step], jnp.float32(0.0))
        divs[step] = div[mid, centre]
        inject[step] = ext[12] * state[0] - ext[13 + step]
    for k in range(5):
        end_ref[0, k] = state[k][mid, centre]

    velocity = vel[mid, centre]
    attenuation = att[mid, centre]
    stiff_own = stiff[mid, centre]
    adj = [ext[5 + k] for k in range(5)]
    grad_v = jnp.zeros((frame.ny, frame.lanes), jnp.float32)
    grad_a = jnp.zeros((frame.ny, frame.lanes), jnp.float32)
    for step in range(STEPS - 1, -1, -1):
        adj, unused = wave_step(adj, stiff, att)
        adj[0] = adj[0] + inject[step]
        div = divs[step]
        q = adj[0][mid, centre]
        m = adj[4][mid, centre]
        deriv_q = (relax_rate * attenuation - (1.0 + attenuation)) * div
        deriv_m = -relax_rate * attenuation * div
        grad_v = grad_v + (q * deriv_q + m * deriv_m) * (2.0 * stiff_scale * velocity)
        grad_a = grad_a + (q * (relax_rate - 1.0) - m * relax_rate) * stiff_own * div
    for k in range(5):
        start_ref[0, k] = adj[k][mid, centre]
    for c, g in enumerate((grad_v, grad_a)):
        grad_ref[c] = g.reshape(frame.ny // BY, BY, frame.lanes).sum(axis=1)


def vmem():
    return pl.BlockSpec(memory_space=pltpu.VMEM)


def smem():
    return pl.BlockSpec(memory_space=pltpu.SMEM)


def on_device(
    forward_start,
    adjoint_end,
    velocity,
    attenuation,
    wavelet,
    source_cell,
    receiver_cells,
    observed,
    aperture,
    block_slot,
):
    nz = CZ
    ny = velocity.shape[0]
    lanes = velocity.shape[1]
    nx = lanes // nz
    frame = Frame(ny, lanes)
    index_y = lax.axis_index("gy")
    index_x = lax.axis_index("gx")
    total_y = ny * lax.axis_size("gy")
    total_x = nx * lax.axis_size("gx")

    row_lo = frame.oy - index_y * ny
    lane_lo = frame.ox - index_x * lanes
    bounds = jnp.stack([row_lo, row_lo + total_y, lane_lo, lane_lo + total_x * nz]).astype(jnp.int32)

    cell = source_cell[0, 0]
    src_row = cell // (total_x * nz) + row_lo
    src_lane = cell % (total_x * nz) + lane_lo
    source = jnp.stack([src_row, src_lane]).astype(jnp.int32)

    recs = receiver_cells[0, 0]
    at_row = (recs // lanes)[:, None] == lax.broadcasted_iota(jnp.int32, (recs.shape[0], ny), 1)
    at_lane = (recs % lanes)[:, None] == lax.broadcasted_iota(jnp.int32, (recs.shape[0], lanes), 1)
    weights = jnp.concatenate([jnp.ones((1, recs.shape[0]), jnp.float32), observed[0, :, 0]], axis=0)
    gauge = jnp.einsum(
        "nky,kl->nyl",
        weights[:, :, None] * at_row.astype(jnp.float32)[None],
        at_lane.astype(jnp.float32),
        precision=lax.Precision.HIGHEST,
    )

    packing = Packing(frame)
    packed = pl.pallas_call(
        lambda *refs: pack_kernel(frame, packing, *refs),
        out_shape=tuple(
            jax.ShapeDtypeStruct(shape, jnp.float32)
            for shape in (
                [(packing.total_rows, lanes)] * 2
                + [(ny, packing.total_lanes)] * 2
                + [(packing.total_rows, packing.corner)] * 4
            )
        ),
        in_specs=[vmem()] * 5,
        out_specs=tuple([vmem()] * 8),
    )(forward_start, adjoint_end, velocity, attenuation, gauge)
    pieces = send_pieces(packed)

    ext_shape = (frame.ey, frame.el)
    forward_end, adjoint_start, row_sums = pl.pallas_call(
        lambda *refs: window_kernel(frame, packing, *refs),
        out_shape=(
            jax.ShapeDtypeStruct((1, 5, ny, lanes), jnp.float32),
            jax.ShapeDtypeStruct((1, 5, ny, lanes), jnp.float32),
            jax.ShapeDtypeStruct((2, ny // BY, lanes), jnp.float32),
        ),
        in_specs=[smem(), smem(), smem()] + [vmem()] * 13,
        out_specs=(vmem(), vmem(), vmem()),
        scratch_shapes=[
            pltpu.VMEM((16,) + ext_shape, jnp.float32),
            pltpu.VMEM((STEPS,) + ext_shape, jnp.float32),
            pltpu.VMEM((STEPS, ny, lanes), jnp.float32),
        ],
        compiler_params=pltpu.CompilerParams(vmem_limit_bytes=48 * 1024 * 1024),
    )(bounds, source, wavelet[0], forward_start, adjoint_end, velocity, attenuation, gauge, *pieces)

    grad_scale = float(BY * BX * BZ) ** (-0.5)
    weight = aperture[0, 0].astype(jnp.float32)
    blocks = row_sums.reshape(2, ny // BY, nx // BX, BX, nz // BZ, BZ).sum(axis=(3, 5))
    sums = blocks.transpose(1, 2, 3, 0).reshape(-1, 2) * (grad_scale * weight)
    slots = block_slot[0]
    ordered = jnp.zeros(sums.shape, jnp.float32).at[slots].set(sums)
    shots = lax.axis_size("shot")
    parts = lax.all_to_all(
        ordered.reshape(shots, -1, 2), "shot", split_axis=0, concat_axis=0, tiled=True
    )
    coarse = jnp.sum(parts, axis=0)
    model_gradient = coarse.T[:, None, :]
    return (forward_end, adjoint_start, model_gradient)


def solution(mesh):
    placed = (
        P("shot", None, "gy", "gx"),
        P("shot", None, "gy", "gx"),
        P("gy", "gx"),
        P("gy", "gx"),
        P("shot", None),
        P("shot", None),
        P("shot", ("gy", "gx"), None),
        P("shot", None, ("gy", "gx"), None),
        P("shot", ("gy", "gx")),
        P(("gy", "gx"), None),
    )
    return jax.shard_map(
        on_device,
        mesh=mesh,
        in_specs=placed,
        out_specs=(
            P("shot", None, "gy", "gx"),
            P("shot", None, "gy", "gx"),
            P(None, ("gy", "gx"), "shot"),
        ),
        check_vma=False,
    )
```

```python
import jax
import jax.numpy as jnp
from jax import lax
from jax.experimental import pallas as pl
from jax.experimental.pallas import tpu as pltpu
from jax.sharding import PartitionSpec as P

CZ = 32
STEPS = 3
BY = 8
BX = 8
BZ = 8
HALO = 3 * STEPS + 3 * (STEPS - 1)

coef_near = 9.0 / 8.0
coef_far = -1.0 / 24.0
stiff_scale = 0.02
relax_rate = 0.3


def round_up(value, unit):
    return (value + unit - 1) // unit * unit


class Frame:
    def __init__(self, ny, lanes):
        self.ny = ny
        self.lanes = lanes
        self.oy = round_up(HALO, 8)
        self.ox = round_up(HALO * CZ, 128)
        self.ey = 2 * self.oy + ny
        self.el = 2 * self.ox + lanes


NEEDS = (
    (15, 15), (14, 12), (12, 14), (12, 12), (12, 12),
    (9, 9), (8, 6), (6, 8), (6, 6), (6, 6),
    (12, 12), (12, 12),
    (6, 6), (0, 0), (3, 3), (6, 6),
)


class Packing:
    def __init__(self, frame):
        self.rows = [h for h, w in NEEDS]
        self.lanes = [round_up(w * CZ, 128) for h, w in NEEDS]
        self.row_at = [sum(self.rows[:j]) for j in range(len(NEEDS))]
        self.lane_at = [sum(self.lanes[:j]) for j in range(len(NEEDS))]
        self.total_rows = sum(self.rows)
        self.total_lanes = sum(self.lanes)
        self.corner = frame.ox


def pack_kernel(frame, packing, fwd_ref, adj_ref, vel_ref, att_ref, gauge_ref, *outs):
    up, down, east, west, up_east, up_west, down_east, down_west = outs
    ny, lanes, cw = frame.ny, frame.lanes, packing.corner

    def field(j):
        if j < 5:
            return fwd_ref.at[0, j]
        if j < 10:
            return adj_ref.at[0, j - 5]
        if j == 10:
            return vel_ref
        if j == 11:
            return att_ref
        return gauge_ref.at[j - 12]

    for j in range(len(NEEDS)):
        h, w = packing.rows[j], packing.lanes[j]
        if h == 0:
            continue
        src = field(j)
        r = slice(packing.row_at[j], packing.row_at[j] + h)
        c = slice(packing.lane_at[j], packing.lane_at[j] + w)
        top = slice(ny - h, ny)
        bottom = slice(0, h)
        up[r, :] = src[top, :]
        down[r, :] = src[bottom, :]
        east[:, c] = src[:, lanes - w : lanes]
        west[:, c] = src[:, 0:w]
        up_east[r, :] = src[top, lanes - cw : lanes]
        up_west[r, :] = src[top, 0:cw]
        down_east[r, :] = src[bottom, lanes - cw : lanes]
        down_west[r, :] = src[bottom, 0:cw]


def send_pieces(packed):
    count_y = lax.axis_size("gy")
    count_x = lax.axis_size("gx")

    def move(piece, dy, dx):
        pairs = []
        for y in range(count_y):
            for x in range(count_x):
                ty, tx = y + dy, x + dx
                if 0 <= ty < count_y and 0 <= tx < count_x:
                    pairs.append((y * count_x + x, ty * count_x + tx))
        return lax.ppermute(piece, ("gy", "gx"), pairs)

    steps = ((1, 0), (-1, 0), (0, 1), (0, -1), (1, 1), (1, -1), (-1, 1), (-1, -1))
    return tuple(move(p, dy, dx) for p, (dy, dx) in zip(packed, steps))


def assemble(dst, own, pieces, j, frame, packing):
    ny, lanes, oy, ox, cw = frame.ny, frame.lanes, frame.oy, frame.ox, packing.corner
    below, above, left, right, b_l, b_r, a_l, a_r = pieces
    h, w = packing.rows[j], packing.lanes[j]
    mid = slice(oy, oy + ny)
    centre = slice(ox, ox + lanes)
    dst[mid, centre] = own[...]
    if h == 0:
        return
    r = slice(packing.row_at[j], packing.row_at[j] + h)
    c = slice(packing.lane_at[j], packing.lane_at[j] + w)
    lo = slice(oy - h, oy)
    hi = slice(oy + ny, oy + ny + h)
    west = slice(ox - w, ox)
    east = slice(ox + lanes, ox + lanes + w)
    dst[lo, centre] = below[r, :]
    dst[hi, centre] = above[r, :]
    dst[mid, west] = left[:, c]
    dst[mid, east] = right[:, c]
    dst[lo, west] = b_l[r, cw - w : cw]
    dst[lo, east] = b_r[r, 0:w]
    dst[hi, west] = a_l[r, cw - w : cw]
    dst[hi, east] = a_r[r, 0:w]


def stepper(frame, bounds_ref):
    ey, el = frame.ey, frame.el
    row = lax.broadcasted_iota(jnp.int32, (ey, el), 0)
    lane = lax.broadcasted_iota(jnp.int32, (ey, el), 1)
    inside = (
        (row >= bounds_ref[0])
        & (row < bounds_ref[1])
        & (lane >= bounds_ref[2])
        & (lane < bounds_ref[3])
    )
    depth = lane % CZ
    zero = jnp.zeros((ey, el), jnp.float32)
    z_ok = {d: (depth + d >= 0) & (depth + d < CZ) for d in (-2, -1, 1, 2)}

    def rows(a, d):
        return a if d == 0 else pltpu.roll(a, (-d) % ey, 0)

    def lanes(a, d):
        return a if d == 0 else pltpu.roll(a, (-d) % el, 1)

    def deep(a, d):
        return a if d == 0 else jnp.where(z_ok[d], lanes(a, d), zero)

    def forward_diff(s):
        return coef_near * (s(1) - s(0)) + coef_far * (s(2) - s(-1))

    def backward_diff(s):
        return coef_near * (s(0) - s(-1)) + coef_far * (s(1) - s(-2))

    def wave_step(state, stiff, att):
        pres, vel_y, vel_x, vel_z, memory = state
        vel_y = jnp.where(inside, vel_y - forward_diff(lambda d: rows(pres, d)), zero)
        vel_x = jnp.where(inside, vel_x - forward_diff(lambda d: lanes(pres, d * CZ)), zero)
        vel_z = vel_z - forward_diff(lambda d: deep(pres, d))
        div = (
            backward_diff(lambda d: rows(vel_y, d))
            + backward_diff(lambda d: lanes(vel_x, d * CZ))
            + backward_diff(lambda d: deep(vel_z, d))
        )
        memory = memory - relax_rate * (memory + stiff * att * div)
        pres = jnp.where(inside, pres - stiff * (1.0 + att) * div - memory, zero)
        return [pres, vel_y, vel_x, vel_z, memory], div

    return wave_step, row, lane


def window_kernel(frame, packing, bounds_ref, source_ref, wave_ref, *rest):
    fwd_ref, adj_ref, vel_ref, att_ref, gauge_ref = rest[:5]
    pieces = rest[5:13]
    end_ref, start_ref, grad_ref, ext, inject, divs = rest[13:]
    owns = (
        [fwd_ref.at[0, k] for k in range(5)]
        + [adj_ref.at[0, k] for k in range(5)]
        + [vel_ref, att_ref]
        + [gauge_ref.at[k] for k in range(4)]
    )
    for j in range(16):
        assemble(ext.at[j], owns[j], pieces, j, frame, packing)
    wave_step, row, lane = stepper(frame, bounds_ref)
    source = (row == source_ref[0]) & (lane == source_ref[1])
    vel = ext[10]
    att = ext[11]
    stiff = stiff_scale * vel * vel
    mid = slice(frame.oy, frame.oy + frame.ny)
    centre = slice(frame.ox, frame.ox + frame.lanes)
    state = [ext[k] for k in range(5)]
    for step in range(STEPS):
        state, div = wave_step(state, stiff, att)
        state[0] = state[0] + jnp.where(source, wave_ref[step], jnp.float32(0.0))
        divs[step] = div[mid, centre]
        inject[step] = ext[12] * state[0] - ext[13 + step]
    for k in range(5):
        end_ref[0, k] = state[k][mid, centre]

    velocity = vel[mid, centre]
    attenuation = att[mid, centre]
    stiff_own = stiff[mid, centre]
    adj = [ext[5 + k] for k in range(5)]
    grad_v = jnp.zeros((frame.ny, frame.lanes), jnp.float32)
    grad_a = jnp.zeros((frame.ny, frame.lanes), jnp.float32)
    for step in range(STEPS - 1, -1, -1):
        adj, unused = wave_step(adj, stiff, att)
        adj[0] = adj[0] + inject[step]
        div = divs[step]
        q = adj[0][mid, centre]
        m = adj[4][mid, centre]
        deriv_q = (relax_rate * attenuation - (1.0 + attenuation)) * div
        deriv_m = -relax_rate * attenuation * div
        grad_v = grad_v + (q * deriv_q + m * deriv_m) * (2.0 * stiff_scale * velocity)
        grad_a = grad_a + (q * (relax_rate - 1.0) - m * relax_rate) * stiff_own * div
    for k in range(5):
        start_ref[0, k] = adj[k][mid, centre]
    for c, g in enumerate((grad_v, grad_a)):
        grad_ref[c] = g.reshape(frame.ny // BY, BY, frame.lanes).sum(axis=1)


def vmem():
    return pl.BlockSpec(memory_space=pltpu.VMEM)


def smem():
    return pl.BlockSpec(memory_space=pltpu.SMEM)


def on_device(
    forward_start,
    adjoint_end,
    velocity,
    attenuation,
    wavelet,
    source_cell,
    receiver_cells,
    observed,
    aperture,
    block_slot,
):
    nz = CZ
    ny = velocity.shape[0]
    lanes = velocity.shape[1]
    nx = lanes // nz
    frame = Frame(ny, lanes)
    index_y = lax.axis_index("gy")
    index_x = lax.axis_index("gx")
    total_y = ny * lax.axis_size("gy")
    total_x = nx * lax.axis_size("gx")

    row_lo = frame.oy - index_y * ny
    lane_lo = frame.ox - index_x * lanes
    bounds = jnp.stack([row_lo, row_lo + total_y, lane_lo, lane_lo + total_x * nz]).astype(jnp.int32)

    cell = source_cell[0, 0]
    src_row = cell // (total_x * nz) + row_lo
    src_lane = cell % (total_x * nz) + lane_lo
    source = jnp.stack([src_row, src_lane]).astype(jnp.int32)

    recs = receiver_cells[0, 0]
    at_row = (recs // lanes)[:, None] == lax.broadcasted_iota(jnp.int32, (recs.shape[0], ny), 1)
    at_lane = (recs % lanes)[:, None] == lax.broadcasted_iota(jnp.int32, (recs.shape[0], lanes), 1)
    weights = jnp.concatenate([jnp.ones((1, recs.shape[0]), jnp.float32), observed[0, :, 0]], axis=0)
    gauge = jnp.einsum(
        "nky,kl->nyl",
        weights[:, :, None] * at_row.astype(jnp.float32)[None],
        at_lane.astype(jnp.float32),
        precision=lax.Precision.HIGHEST,
    )

    packing = Packing(frame)
    packed = pl.pallas_call(
        lambda *refs: pack_kernel(frame, packing, *refs),
        out_shape=tuple(
            jax.ShapeDtypeStruct(shape, jnp.float32)
            for shape in (
                [(packing.total_rows, lanes)] * 2
                + [(ny, packing.total_lanes)] * 2
                + [(packing.total_rows, packing.corner)] * 4
            )
        ),
        in_specs=[vmem()] * 5,
        out_specs=tuple([vmem()] * 8),
    )(forward_start, adjoint_end, velocity, attenuation, gauge)
    pieces = send_pieces(packed)

    ext_shape = (frame.ey, frame.el)
    forward_end, adjoint_start, row_sums = pl.pallas_call(
        lambda *refs: window_kernel(frame, packing, *refs),
        out_shape=(
            jax.ShapeDtypeStruct((1, 5, ny, lanes), jnp.float32),
            jax.ShapeDtypeStruct((1, 5, ny, lanes), jnp.float32),
            jax.ShapeDtypeStruct((2, ny // BY, lanes), jnp.float32),
        ),
        in_specs=[smem(), smem(), smem()] + [vmem()] * 13,
        out_specs=(vmem(), vmem(), vmem()),
        scratch_shapes=[
            pltpu.VMEM((16,) + ext_shape, jnp.float32),
            pltpu.VMEM((STEPS,) + ext_shape, jnp.float32),
            pltpu.VMEM((STEPS, ny, lanes), jnp.float32),
        ],
        compiler_params=pltpu.CompilerParams(vmem_limit_bytes=48 * 1024 * 1024),
    )(bounds, source, wavelet[0], forward_start, adjoint_end, velocity, attenuation, gauge, *pieces)

    grad_scale = float(BY * BX * BZ) ** (-0.5)
    weight = aperture[0, 0].astype(jnp.float32)
    blocks = row_sums.reshape(2, ny // BY, nx // BX, BX, nz // BZ, BZ).sum(axis=(3, 5))
    sums = blocks.transpose(1, 2, 3, 0).reshape(-1, 2) * (grad_scale * weight)
    slots = block_slot[0]
    ordered = jnp.zeros(sums.shape, jnp.float32).at[slots].set(sums)
    shots = lax.axis_size("shot")
    parts = lax.all_to_all(
        ordered.reshape(shots, -1, 2), "shot", split_axis=0, concat_axis=0, tiled=True
    )
    coarse = jnp.sum(parts, axis=0)
    model_gradient = coarse.T[:, None, :]
    return (forward_end, adjoint_start, model_gradient)


def solution(mesh):
    placed = (
        P("shot", None, "gy", "gx"),
        P("shot", None, "gy", "gx"),
        P("gy", "gx"),
        P("gy", "gx"),
        P("shot", None),
        P("shot", None),
        P("shot", ("gy", "gx"), None),
        P("shot", None, ("gy", "gx"), None),
        P("shot", ("gy", "gx")),
        P(("gy", "gx"), None),
    )
    return jax.shard_map(
        on_device,
        mesh=mesh,
        in_specs=placed,
        out_specs=(
            P("shot", None, "gy", "gx"),
            P("shot", None, "gy", "gx"),
            P(None, ("gy", "gx"), "shot"),
        ),
        check_vma=False,
    )
```

```python
import jax
import jax.numpy as jnp
from jax import lax
from jax.experimental import pallas as pl
from jax.experimental.pallas import tpu as pltpu
from jax.sharding import PartitionSpec as P

CZ = 32
STEPS = 3
BY = 8
BX = 8
BZ = 8
HALO = 3 * STEPS + 3 * (STEPS - 1)

coef_near = 9.0 / 8.0
coef_far = -1.0 / 24.0
stiff_scale = 0.02
relax_rate = 0.3


def round_up(value, unit):
    return (value + unit - 1) // unit * unit


class Frame:
    def __init__(self, ny, lanes):
        self.ny = ny
        self.lanes = lanes
        self.oy = round_up(HALO, 8)
        self.ox = round_up(HALO * CZ, 128)
        self.ey = 2 * self.oy + ny
        self.el = 2 * self.ox + lanes


NEEDS = (
    (15, 15), (14, 12), (12, 14), (12, 12), (12, 12),
    (9, 9), (8, 6), (6, 8), (6, 6), (6, 6),
    (12, 12), (12, 12),
    (6, 6), (0, 0), (3, 3), (6, 6),
)


class Packing:
    def __init__(self, frame):
        self.rows = [h for h, w in NEEDS]
        self.lanes = [round_up(w * CZ, 128) for h, w in NEEDS]
        self.row_at = [sum(self.rows[:j]) for j in range(len(NEEDS))]
        self.lane_at = [sum(self.lanes[:j]) for j in range(len(NEEDS))]
        self.total_rows = sum(self.rows)
        self.total_lanes = sum(self.lanes)
        self.corner = frame.ox


def pack_kernel(frame, packing, fwd_ref, adj_ref, vel_ref, att_ref, gauge_ref, *outs):
    up, down, east, west, up_east, up_west, down_east, down_west = outs
    ny, lanes, cw = frame.ny, frame.lanes, packing.corner

    def field(j):
        if j < 5:
            return fwd_ref.at[0, j]
        if j < 10:
            return adj_ref.at[0, j - 5]
        if j == 10:
            return vel_ref
        if j == 11:
            return att_ref
        return gauge_ref.at[j - 12]

    for j in range(len(NEEDS)):
        h, w = packing.rows[j], packing.lanes[j]
        if h == 0:
            continue
        src = field(j)
        r = slice(packing.row_at[j], packing.row_at[j] + h)
        c = slice(packing.lane_at[j], packing.lane_at[j] + w)
        top = slice(ny - h, ny)
        bottom = slice(0, h)
        up[r, :] = src[top, :]
        down[r, :] = src[bottom, :]
        east[:, c] = src[:, lanes - w : lanes]
        west[:, c] = src[:, 0:w]
        up_east[r, :] = src[top, lanes - cw : lanes]
        up_west[r, :] = src[top, 0:cw]
        down_east[r, :] = src[bottom, lanes - cw : lanes]
        down_west[r, :] = src[bottom, 0:cw]


def send_pieces(packed):
    count_y = lax.axis_size("gy")
    count_x = lax.axis_size("gx")

    def move(piece, dy, dx):
        pairs = []
        for y in range(count_y):
            for x in range(count_x):
                ty, tx = y + dy, x + dx
                if 0 <= ty < count_y and 0 <= tx < count_x:
                    pairs.append((y * count_x + x, ty * count_x + tx))
        return lax.ppermute(piece, ("gy", "gx"), pairs)

    steps = ((1, 0), (-1, 0), (0, 1), (0, -1), (1, 1), (1, -1), (-1, 1), (-1, -1))
    return tuple(move(p, dy, dx) for p, (dy, dx) in zip(packed, steps))


def assemble(dst, own, pieces, j, frame, packing):
    ny, lanes, oy, ox, cw = frame.ny, frame.lanes, frame.oy, frame.ox, packing.corner
    below, above, left, right, b_l, b_r, a_l, a_r = pieces
    h, w = packing.rows[j], packing.lanes[j]
    mid = slice(oy, oy + ny)
    centre = slice(ox, ox + lanes)
    dst[mid, centre] = own[...]
    if h == 0:
        return
    r = slice(packing.row_at[j], packing.row_at[j] + h)
    c = slice(packing.lane_at[j], packing.lane_at[j] + w)
    lo = slice(oy - h, oy)
    hi = slice(oy + ny, oy + ny + h)
    west = slice(ox - w, ox)
    east = slice(ox + lanes, ox + lanes + w)
    dst[lo, centre] = below[r, :]
    dst[hi, centre] = above[r, :]
    dst[mid, west] = left[:, c]
    dst[mid, east] = right[:, c]
    dst[lo, west] = b_l[r, cw - w : cw]
    dst[lo, east] = b_r[r, 0:w]
    dst[hi, west] = a_l[r, cw - w : cw]
    dst[hi, east] = a_r[r, 0:w]


def window(frame, depth):
    r0 = max(0, (frame.oy - depth) // 8 * 8)
    r1 = min(frame.ey, round_up(frame.oy + frame.ny + depth, 8))
    l0 = max(0, (frame.ox - depth * CZ) // 128 * 128)
    l1 = min(frame.el, round_up(frame.ox + frame.lanes + depth * CZ, 128))
    return r0, r1, l0, l1


def stepper(frame, bounds_ref, win):
    r0, r1, l0, l1 = win
    ey, el = r1 - r0, l1 - l0
    row = lax.broadcasted_iota(jnp.int32, (ey, el), 0) + r0
    lane = lax.broadcasted_iota(jnp.int32, (ey, el), 1) + l0
    inside = (
        (row >= bounds_ref[0])
        & (row < bounds_ref[1])
        & (lane >= bounds_ref[2])
        & (lane < bounds_ref[3])
    )
    depth = lane % CZ
    zero = jnp.zeros((ey, el), jnp.float32)
    z_ok = {d: (depth + d >= 0) & (depth + d < CZ) for d in (-2, -1, 1, 2)}

    def rows(a, d):
        return a if d == 0 else pltpu.roll(a, (-d) % ey, 0)

    def lanes(a, d):
        return a if d == 0 else pltpu.roll(a, (-d) % el, 1)

    def deep(a, d):
        return a if d == 0 else jnp.where(z_ok[d], lanes(a, d), zero)

    def forward_diff(s):
        return coef_near * (s(1) - s(0)) + coef_far * (s(2) - s(-1))

    def backward_diff(s):
        return coef_near * (s(0) - s(-1)) + coef_far * (s(1) - s(-2))

    def wave_step(state, stiff, att):
        pres, vel_y, vel_x, vel_z, memory = state
        vel_y = jnp.where(inside, vel_y - forward_diff(lambda d: rows(pres, d)), zero)
        vel_x = jnp.where(inside, vel_x - forward_diff(lambda d: lanes(pres, d * CZ)), zero)
        vel_z = vel_z - forward_diff(lambda d: deep(pres, d))
        div = (
            backward_diff(lambda d: rows(vel_y, d))
            + backward_diff(lambda d: lanes(vel_x, d * CZ))
            + backward_diff(lambda d: deep(vel_z, d))
        )
        memory = memory - relax_rate * (memory + stiff * att * div)
        pres = jnp.where(inside, pres - stiff * (1.0 + att) * div - memory, zero)
        return [pres, vel_y, vel_x, vel_z, memory], div

    return wave_step, row, lane


def window_kernel(frame, packing, bounds_ref, source_ref, wave_ref, *rest):
    fwd_ref, adj_ref, vel_ref, att_ref, gauge_ref = rest[:5]
    pieces = rest[5:13]
    end_ref, start_ref, grad_ref, ext, inject, divs = rest[13:]
    owns = (
        [fwd_ref.at[0, k] for k in range(5)]
        + [adj_ref.at[0, k] for k in range(5)]
        + [vel_ref, att_ref]
        + [gauge_ref.at[k] for k in range(4)]
    )
    for j in range(16):
        assemble(ext.at[j], owns[j], pieces, j, frame, packing)
    vel_all = ext[10]
    att_all = ext[11]
    stiff_all = stiff_scale * vel_all * vel_all

    def cut(a, inner, outer):
        return a[inner[0] - outer[0] : inner[1] - outer[0], inner[2] - outer[2] : inner[3] - outer[2]]

    full = (0, frame.ey, 0, frame.el)
    tile = (frame.oy, frame.oy + frame.ny, frame.ox, frame.ox + frame.lanes)

    state = [ext[k] for k in range(5)]
    where = full
    for step in range(STEPS):
        win = window(frame, 3 * (STEPS - step) + 3 * (STEPS - 1))
        state = [cut(a, win, where) for a in state]
        where = win
        wave_step, row, lane = stepper(frame, bounds_ref, win)
        source = (row == source_ref[0]) & (lane == source_ref[1])
        state, div = wave_step(state, cut(stiff_all, win, full), cut(att_all, win, full))
        state[0] = state[0] + jnp.where(source, wave_ref[step], jnp.float32(0.0))
        divs[step] = cut(div, tile, win)
        inject[step, win[0] : win[1], win[2] : win[3]] = (
            cut(ext[12], win, full) * state[0] - cut(ext[13 + step], win, full)
        )
    for k in range(5):
        end_ref[0, k] = cut(state[k], tile, where)

    velocity = cut(vel_all, tile, full)
    attenuation = cut(att_all, tile, full)
    stiff_own = cut(stiff_all, tile, full)
    adj = [ext[5 + k] for k in range(5)]
    where = full
    grad_v = jnp.zeros((frame.ny, frame.lanes), jnp.float32)
    grad_a = jnp.zeros((frame.ny, frame.lanes), jnp.float32)
    for step in range(STEPS - 1, -1, -1):
        win = window(frame, 3 * (step + 1))
        adj = [cut(a, win, where) for a in adj]
        where = win
        wave_step, row, lane = stepper(frame, bounds_ref, win)
        adj, unused = wave_step(adj, cut(stiff_all, win, full), cut(att_all, win, full))
        adj[0] = adj[0] + inject[step, win[0] : win[1], win[2] : win[3]]
        div = divs[step]
        q = cut(adj[0], tile, win)
        m = cut(adj[4], tile, win)
        deriv_q = (relax_rate * attenuation - (1.0 + attenuation)) * div
        deriv_m = -relax_rate * attenuation * div
        grad_v = grad_v + (q * deriv_q + m * deriv_m) * (2.0 * stiff_scale * velocity)
        grad_a = grad_a + (q * (relax_rate - 1.0) - m * relax_rate) * stiff_own * div
    for k in range(5):
        start_ref[0, k] = cut(adj[k], tile, where)
    for c, g in enumerate((grad_v, grad_a)):
        grad_ref[c] = g.reshape(frame.ny // BY, BY, frame.lanes).sum(axis=1)


def vmem():
    return pl.BlockSpec(memory_space=pltpu.VMEM)


def smem():
    return pl.BlockSpec(memory_space=pltpu.SMEM)


def on_device(
    forward_start,
    adjoint_end,
    velocity,
    attenuation,
    wavelet,
    source_cell,
    receiver_cells,
    observed,
    aperture,
    block_slot,
):
    nz = CZ
    ny = velocity.shape[0]
    lanes = velocity.shape[1]
    nx = lanes // nz
    frame = Frame(ny, lanes)
    index_y = lax.axis_index("gy")
    index_x = lax.axis_index("gx")
    total_y = ny * lax.axis_size("gy")
    total_x = nx * lax.axis_size("gx")

    row_lo = frame.oy - index_y * ny
    lane_lo = frame.ox - index_x * lanes
    bounds = jnp.stack([row_lo, row_lo + total_y, lane_lo, lane_lo + total_x * nz]).astype(jnp.int32)

    cell = source_cell[0, 0]
    src_row = cell // (total_x * nz) + row_lo
    src_lane = cell % (total_x * nz) + lane_lo
    source = jnp.stack([src_row, src_lane]).astype(jnp.int32)

    recs = receiver_cells[0, 0]
    at_row = (recs // lanes)[:, None] == lax.broadcasted_iota(jnp.int32, (recs.shape[0], ny), 1)
    at_lane = (recs % lanes)[:, None] == lax.broadcasted_iota(jnp.int32, (recs.shape[0], lanes), 1)
    weights = jnp.concatenate([jnp.ones((1, recs.shape[0]), jnp.float32), observed[0, :, 0]], axis=0)
    gauge = jnp.einsum(
        "nky,kl->nyl",
        weights[:, :, None] * at_row.astype(jnp.float32)[None],
        at_lane.astype(jnp.float32),
        precision=lax.Precision.HIGHEST,
    )

    packing = Packing(frame)
    packed = pl.pallas_call(
        lambda *refs: pack_kernel(frame, packing, *refs),
        out_shape=tuple(
            jax.ShapeDtypeStruct(shape, jnp.float32)
            for shape in (
                [(packing.total_rows, lanes)] * 2
                + [(ny, packing.total_lanes)] * 2
                + [(packing.total_rows, packing.corner)] * 4
            )
        ),
        in_specs=[vmem()] * 5,
        out_specs=tuple([vmem()] * 8),
    )(forward_start, adjoint_end, velocity, attenuation, gauge)
    pieces = send_pieces(packed)

    ext_shape = (frame.ey, frame.el)
    forward_end, adjoint_start, row_sums = pl.pallas_call(
        lambda *refs: window_kernel(frame, packing, *refs),
        out_shape=(
            jax.ShapeDtypeStruct((1, 5, ny, lanes), jnp.float32),
            jax.ShapeDtypeStruct((1, 5, ny, lanes), jnp.float32),
            jax.ShapeDtypeStruct((2, ny // BY, lanes), jnp.float32),
        ),
        in_specs=[smem(), smem(), smem()] + [vmem()] * 13,
        out_specs=(vmem(), vmem(), vmem()),
        scratch_shapes=[
            pltpu.VMEM((16,) + ext_shape, jnp.float32),
            pltpu.VMEM((STEPS,) + ext_shape, jnp.float32),
            pltpu.VMEM((STEPS, ny, lanes), jnp.float32),
        ],
        compiler_params=pltpu.CompilerParams(vmem_limit_bytes=48 * 1024 * 1024),
    )(bounds, source, wavelet[0], forward_start, adjoint_end, velocity, attenuation, gauge, *pieces)

    grad_scale = float(BY * BX * BZ) ** (-0.5)
    weight = aperture[0, 0].astype(jnp.float32)
    blocks = row_sums.reshape(2, ny // BY, nx // BX, BX, nz // BZ, BZ).sum(axis=(3, 5))
    sums = blocks.transpose(1, 2, 3, 0).reshape(-1, 2) * (grad_scale * weight)
    slots = block_slot[0]
    ordered = jnp.zeros(sums.shape, jnp.float32).at[slots].set(sums)
    shots = lax.axis_size("shot")
    parts = lax.all_to_all(
        ordered.reshape(shots, -1, 2), "shot", split_axis=0, concat_axis=0, tiled=True
    )
    coarse = jnp.sum(parts, axis=0)
    model_gradient = coarse.T[:, None, :]
    return (forward_end, adjoint_start, model_gradient)


def solution(mesh):
    placed = (
        P("shot", None, "gy", "gx"),
        P("shot", None, "gy", "gx"),
        P("gy", "gx"),
        P("gy", "gx"),
        P("shot", None),
        P("shot", None),
        P("shot", ("gy", "gx"), None),
        P("shot", None, ("gy", "gx"), None),
        P("shot", ("gy", "gx")),
        P(("gy", "gx"), None),
    )
    return jax.shard_map(
        on_device,
        mesh=mesh,
        in_specs=placed,
        out_specs=(
            P("shot", None, "gy", "gx"),
            P("shot", None, "gy", "gx"),
            P(None, ("gy", "gx"), "shot"),
        ),
        check_vma=False,
    )
```

```python
import jax
import jax.numpy as jnp
from jax import lax
from jax.experimental import pallas as pl
from jax.experimental.pallas import tpu as pltpu
from jax.sharding import PartitionSpec as P

CZ = 32
STEPS = 3
BY = 8
BX = 8
BZ = 8
HALO = 3 * STEPS + 3 * (STEPS - 1)

coef_near = 9.0 / 8.0
coef_far = -1.0 / 24.0
stiff_scale = 0.02
relax_rate = 0.3


def round_up(value, unit):
    return (value + unit - 1) // unit * unit


class Frame:
    def __init__(self, ny, lanes):
        self.ny = ny
        self.lanes = lanes
        self.oy = round_up(HALO, 8)
        self.ox = round_up(HALO * CZ, 128)
        self.ey = 2 * self.oy + ny
        self.el = 2 * self.ox + lanes


NEEDS = (
    (15, 15), (14, 12), (12, 14), (12, 12), (12, 12),
    (9, 9), (8, 6), (6, 8), (6, 6), (6, 6),
    (12, 12), (12, 12),
    (6, 6), (0, 0), (3, 3), (6, 6),
)


class Packing:
    def __init__(self, frame):
        self.rows = [h for h, w in NEEDS]
        self.lanes = [round_up(w * CZ, 128) for h, w in NEEDS]
        self.row_at = [sum(self.rows[:j]) for j in range(len(NEEDS))]
        self.lane_at = [sum(self.lanes[:j]) for j in range(len(NEEDS))]
        self.total_rows = sum(self.rows)
        self.total_lanes = sum(self.lanes)
        self.corner = frame.ox


def pack_kernel(frame, packing, fwd_ref, adj_ref, vel_ref, att_ref, gauge_ref, *outs):
    up, down, east, west, up_east, up_west, down_east, down_west = outs
    ny, lanes, cw = frame.ny, frame.lanes, packing.corner

    def field(j):
        if j < 5:
            return fwd_ref.at[0, j]
        if j < 10:
            return adj_ref.at[0, j - 5]
        if j == 10:
            return vel_ref
        if j == 11:
            return att_ref
        return gauge_ref.at[j - 12]

    for j in range(len(NEEDS)):
        h, w = packing.rows[j], packing.lanes[j]
        if h == 0:
            continue
        src = field(j)
        r = slice(packing.row_at[j], packing.row_at[j] + h)
        c = slice(packing.lane_at[j], packing.lane_at[j] + w)
        top = slice(ny - h, ny)
        bottom = slice(0, h)
        up[r, :] = src[top, :]
        down[r, :] = src[bottom, :]
        east[:, c] = src[:, lanes - w : lanes]
        west[:, c] = src[:, 0:w]
        up_east[r, :] = src[top, lanes - cw : lanes]
        up_west[r, :] = src[top, 0:cw]
        down_east[r, :] = src[bottom, lanes - cw : lanes]
        down_west[r, :] = src[bottom, 0:cw]


def send_pieces(packed):
    count_y = lax.axis_size("gy")
    count_x = lax.axis_size("gx")

    def move(piece, dy, dx):
        pairs = []
        for y in range(count_y):
            for x in range(count_x):
                ty, tx = y + dy, x + dx
                if 0 <= ty < count_y and 0 <= tx < count_x:
                    pairs.append((y * count_x + x, ty * count_x + tx))
        return lax.ppermute(piece, ("gy", "gx"), pairs)

    steps = ((1, 0), (-1, 0), (0, 1), (0, -1), (1, 1), (1, -1), (-1, 1), (-1, -1))
    return tuple(move(p, dy, dx) for p, (dy, dx) in zip(packed, steps))


def assemble(dst, own, pieces, j, frame, packing):
    ny, lanes, oy, ox, cw = frame.ny, frame.lanes, frame.oy, frame.ox, packing.corner
    below, above, left, right, b_l, b_r, a_l, a_r = pieces
    h, w = packing.rows[j], packing.lanes[j]
    mid = slice(oy, oy + ny)
    centre = slice(ox, ox + lanes)
    dst[mid, centre] = own[...]
    if h == 0:
        return
    r = slice(packing.row_at[j], packing.row_at[j] + h)
    c = slice(packing.lane_at[j], packing.lane_at[j] + w)
    lo = slice(oy - h, oy)
    hi = slice(oy + ny, oy + ny + h)
    west = slice(ox - w, ox)
    east = slice(ox + lanes, ox + lanes + w)
    dst[lo, centre] = below[r, :]
    dst[hi, centre] = above[r, :]
    dst[mid, west] = left[:, c]
    dst[mid, east] = right[:, c]
    dst[lo, west] = b_l[r, cw - w : cw]
    dst[lo, east] = b_r[r, 0:w]
    dst[hi, west] = a_l[r, cw - w : cw]
    dst[hi, east] = a_r[r, 0:w]


def window(frame, depth):
    r0 = max(0, (frame.oy - depth) // 8 * 8)
    r1 = min(frame.ey, round_up(frame.oy + frame.ny + depth, 8))
    l0 = max(0, (frame.ox - depth * CZ) // 128 * 128)
    l1 = min(frame.el, round_up(frame.ox + frame.lanes + depth * CZ, 128))
    return r0, r1, l0, l1


def stepper(frame, bounds_ref, win):
    r0, r1, l0, l1 = win
    ey, el = r1 - r0, l1 - l0
    row = lax.broadcasted_iota(jnp.int32, (ey, el), 0) + r0
    lane = lax.broadcasted_iota(jnp.int32, (ey, el), 1) + l0
    inside = (
        (row >= bounds_ref[0])
        & (row < bounds_ref[1])
        & (lane >= bounds_ref[2])
        & (lane < bounds_ref[3])
    )
    depth = lane % CZ
    zero = jnp.zeros((ey, el), jnp.float32)
    z_ok = {d: (depth + d >= 0) & (depth + d < CZ) for d in (-2, -1, 1, 2)}

    def rows(a, d):
        return a if d == 0 else pltpu.roll(a, (-d) % ey, 0)

    def lanes(a, d):
        return a if d == 0 else pltpu.roll(a, (-d) % el, 1)

    def deep(a, d):
        return a if d == 0 else jnp.where(z_ok[d], lanes(a, d), zero)

    def forward_diff(s):
        return coef_near * (s(1) - s(0)) + coef_far * (s(2) - s(-1))

    def backward_diff(s):
        return coef_near * (s(0) - s(-1)) + coef_far * (s(1) - s(-2))

    def wave_step(state, stiff, att):
        pres, vel_y, vel_x, vel_z, memory = state
        vel_y = jnp.where(inside, vel_y - forward_diff(lambda d: rows(pres, d)), zero)
        vel_x = jnp.where(inside, vel_x - forward_diff(lambda d: lanes(pres, d * CZ)), zero)
        vel_z = vel_z - forward_diff(lambda d: deep(pres, d))
        div = (
            backward_diff(lambda d: rows(vel_y, d))
            + backward_diff(lambda d: lanes(vel_x, d * CZ))
            + backward_diff(lambda d: deep(vel_z, d))
        )
        memory = memory - relax_rate * (memory + stiff * att * div)
        pres = jnp.where(inside, pres - stiff * (1.0 + att) * div - memory, zero)
        return [pres, vel_y, vel_x, vel_z, memory], div

    return wave_step, row, lane


def window_kernel(frame, packing, bounds_ref, source_ref, wave_ref, *rest):
    fwd_ref, adj_ref, vel_ref, att_ref, gauge_ref = rest[:5]
    pieces = rest[5:13]
    end_ref, start_ref, grad_ref, ext, inject, divs = rest[13:]
    owns = (
        [fwd_ref.at[0, k] for k in range(5)]
        + [adj_ref.at[0, k] for k in range(5)]
        + [vel_ref, att_ref]
        + [gauge_ref.at[k] for k in range(4)]
    )
    for j in range(16):
        assemble(ext.at[j], owns[j], pieces, j, frame, packing)
    vel_all = ext[10]
    att_all = ext[11]
    stiff_all = stiff_scale * vel_all * vel_all

    def cut(a, inner, outer):
        return a[inner[0] - outer[0] : inner[1] - outer[0], inner[2] - outer[2] : inner[3] - outer[2]]

    full = (0, frame.ey, 0, frame.el)
    tile = (frame.oy, frame.oy + frame.ny, frame.ox, frame.ox + frame.lanes)

    state = [ext[k] for k in range(5)]
    where = full
    for step in range(STEPS):
        win = window(frame, 3 * (STEPS - step) + 3 * (STEPS - 1))
        state = [cut(a, win, where) for a in state]
        where = win
        wave_step, row, lane = stepper(frame, bounds_ref, win)
        source = (row == source_ref[0]) & (lane == source_ref[1])
        state, div = wave_step(state, cut(stiff_all, win, full), cut(att_all, win, full))
        state[0] = state[0] + jnp.where(source, wave_ref[step], jnp.float32(0.0))
        divs[step] = cut(div, tile, win)
        inject[step, win[0] : win[1], win[2] : win[3]] = (
            cut(ext[12], win, full) * state[0] - cut(ext[13 + step], win, full)
        )
    for k in range(5):
        end_ref[0, k] = cut(state[k], tile, where)

    velocity = cut(vel_all, tile, full)
    attenuation = cut(att_all, tile, full)
    stiff_own = cut(stiff_all, tile, full)
    adj = [ext[5 + k] for k in range(5)]
    where = full
    grad_v = jnp.zeros((frame.ny, frame.lanes), jnp.float32)
    grad_a = jnp.zeros((frame.ny, frame.lanes), jnp.float32)
    for step in range(STEPS - 1, -1, -1):
        win = window(frame, 3 * (step + 1))
        adj = [cut(a, win, where) for a in adj]
        where = win
        wave_step, row, lane = stepper(frame, bounds_ref, win)
        adj, unused = wave_step(adj, cut(stiff_all, win, full), cut(att_all, win, full))
        adj[0] = adj[0] + inject[step, win[0] : win[1], win[2] : win[3]]
        div = divs[step]
        q = cut(adj[0], tile, win)
        m = cut(adj[4], tile, win)
        deriv_q = (relax_rate * attenuation - (1.0 + attenuation)) * div
        deriv_m = -relax_rate * attenuation * div
        grad_v = grad_v + (q * deriv_q + m * deriv_m) * (2.0 * stiff_scale * velocity)
        grad_a = grad_a + (q * (relax_rate - 1.0) - m * relax_rate) * stiff_own * div
    for k in range(5):
        start_ref[0, k] = cut(adj[k], tile, where)
    for c, g in enumerate((grad_v, grad_a)):
        grad_ref[c] = g.reshape(frame.ny // BY, BY, frame.lanes).sum(axis=1)


def vmem():
    return pl.BlockSpec(memory_space=pltpu.VMEM)


def smem():
    return pl.BlockSpec(memory_space=pltpu.SMEM)


def on_device(
    forward_start,
    adjoint_end,
    velocity,
    attenuation,
    wavelet,
    source_cell,
    receiver_cells,
    observed,
    aperture,
    block_slot,
):
    nz = CZ
    ny = velocity.shape[0]
    lanes = velocity.shape[1]
    nx = lanes // nz
    frame = Frame(ny, lanes)
    index_y = lax.axis_index("gy")
    index_x = lax.axis_index("gx")
    total_y = ny * lax.axis_size("gy")
    total_x = nx * lax.axis_size("gx")

    row_lo = frame.oy - index_y * ny
    lane_lo = frame.ox - index_x * lanes
    bounds = jnp.stack([row_lo, row_lo + total_y, lane_lo, lane_lo + total_x * nz]).astype(jnp.int32)

    cell = source_cell[0, 0]
    src_row = cell // (total_x * nz) + row_lo
    src_lane = cell % (total_x * nz) + lane_lo
    source = jnp.stack([src_row, src_lane]).astype(jnp.int32)

    recs = receiver_cells[0, 0]
    at_row = (recs // lanes)[:, None] == lax.broadcasted_iota(jnp.int32, (recs.shape[0], ny), 1)
    at_lane = (recs % lanes)[:, None] == lax.broadcasted_iota(jnp.int32, (recs.shape[0], lanes), 1)
    weights = jnp.concatenate([jnp.ones((1, recs.shape[0]), jnp.float32), observed[0, :, 0]], axis=0)
    gauge = jnp.einsum(
        "nky,kl->nyl",
        weights[:, :, None] * at_row.astype(jnp.float32)[None],
        at_lane.astype(jnp.float32),
        precision=lax.Precision.HIGHEST,
    )

    packing = Packing(frame)
    packed = pl.pallas_call(
        lambda *refs: pack_kernel(frame, packing, *refs),
        out_shape=tuple(
            jax.ShapeDtypeStruct(shape, jnp.float32)
            for shape in (
                [(packing.total_rows, lanes)] * 2
                + [(ny, packing.total_lanes)] * 2
                + [(packing.total_rows, packing.corner)] * 4
            )
        ),
        in_specs=[vmem()] * 5,
        out_specs=tuple([vmem()] * 8),
    )(forward_start, adjoint_end, velocity, attenuation, gauge)
    pieces = send_pieces(packed)

    ext_shape = (frame.ey, frame.el)
    forward_end, adjoint_start, row_sums = pl.pallas_call(
        lambda *refs: window_kernel(frame, packing, *refs),
        out_shape=(
            jax.ShapeDtypeStruct((1, 5, ny, lanes), jnp.float32),
            jax.ShapeDtypeStruct((1, 5, ny, lanes), jnp.float32),
            jax.ShapeDtypeStruct((2, ny // BY, lanes), jnp.float32),
        ),
        in_specs=[smem(), smem(), smem()] + [vmem()] * 13,
        out_specs=(vmem(), vmem(), vmem()),
        scratch_shapes=[
            pltpu.VMEM((16,) + ext_shape, jnp.float32),
            pltpu.VMEM((STEPS,) + ext_shape, jnp.float32),
            pltpu.VMEM((STEPS, ny, lanes), jnp.float32),
        ],
        compiler_params=pltpu.CompilerParams(vmem_limit_bytes=48 * 1024 * 1024),
    )(bounds, source, wavelet[0], forward_start, adjoint_end, velocity, attenuation, gauge, *pieces)

    grad_scale = float(BY * BX * BZ) ** (-0.5)
    weight = aperture[0, 0].astype(jnp.float32)
    blocks = row_sums.reshape(2, ny // BY, nx // BX, BX, nz // BZ, BZ).sum(axis=(3, 5))
    sums = blocks.transpose(1, 2, 3, 0).reshape(-1, 2) * (grad_scale * weight)
    slots = block_slot[0]
    ordered = jnp.zeros(sums.shape, jnp.float32).at[slots].set(sums)
    shots = lax.axis_size("shot")
    me = lax.axis_index("shot")
    held = ordered.reshape(shots, -1, 2)
    span = shots // 2
    while span >= 1:
        halves = held.reshape(2, -1, held.shape[1], 2)
        bit = (me // span) % 2 == 1
        mine = jnp.where(bit, halves[1], halves[0])
        other = jnp.where(bit, halves[0], halves[1])
        held = mine + lax.ppermute(other, "shot", [(i, i ^ span) for i in range(shots)])
        span //= 2
    coarse = held[0]
    model_gradient = coarse.T[:, None, :]
    return (forward_end, adjoint_start, model_gradient)


def solution(mesh):
    placed = (
        P("shot", None, "gy", "gx"),
        P("shot", None, "gy", "gx"),
        P("gy", "gx"),
        P("gy", "gx"),
        P("shot", None),
        P("shot", None),
        P("shot", ("gy", "gx"), None),
        P("shot", None, ("gy", "gx"), None),
        P("shot", ("gy", "gx")),
        P(("gy", "gx"), None),
    )
    return jax.shard_map(
        on_device,
        mesh=mesh,
        in_specs=placed,
        out_specs=(
            P("shot", None, "gy", "gx"),
            P("shot", None, "gy", "gx"),
            P(None, ("gy", "gx"), "shot"),
        ),
        check_vma=False,
    )
```

```python
import jax
import jax.numpy as jnp
from jax import lax
from jax.experimental import pallas as pl
from jax.experimental.pallas import tpu as pltpu
from jax.sharding import PartitionSpec as P

CZ = 32
STEPS = 3
BY = 8
BX = 8
BZ = 8
HALO = 3 * STEPS + 3 * (STEPS - 1)

coef_near = 9.0 / 8.0
coef_far = -1.0 / 24.0
stiff_scale = 0.02
relax_rate = 0.3


def round_up(value, unit):
    return (value + unit - 1) // unit * unit


class Frame:
    def __init__(self, ny, lanes):
        self.ny = ny
        self.lanes = lanes
        self.oy = round_up(HALO, 8)
        self.ox = round_up(HALO * CZ, 128)
        self.ey = 2 * self.oy + ny
        self.el = 2 * self.ox + lanes


NEEDS = (
    (15, 15), (14, 12), (12, 14), (12, 12), (12, 12),
    (9, 9), (8, 6), (6, 8), (6, 6), (6, 6),
    (12, 12), (12, 12),
    (6, 6), (0, 0), (3, 3), (6, 6),
)


class Packing:
    def __init__(self, frame):
        self.rows = [h for h, w in NEEDS]
        self.lanes = [round_up(w * CZ, 128) for h, w in NEEDS]
        self.row_at = [sum(self.rows[:j]) for j in range(len(NEEDS))]
        self.lane_at = [sum(self.lanes[:j]) for j in range(len(NEEDS))]
        self.total_rows = sum(self.rows)
        self.total_lanes = sum(self.lanes)
        self.corner = frame.ox


def pack_kernel(frame, packing, fwd_ref, adj_ref, vel_ref, att_ref, gauge_ref, *outs):
    up, down, east, west, up_east, up_west, down_east, down_west = outs
    ny, lanes, cw = frame.ny, frame.lanes, packing.corner

    def field(j):
        if j < 5:
            return fwd_ref.at[0, j]
        if j < 10:
            return adj_ref.at[0, j - 5]
        if j == 10:
            return vel_ref
        if j == 11:
            return att_ref
        return gauge_ref.at[j - 12]

    for j in range(len(NEEDS)):
        h, w = packing.rows[j], packing.lanes[j]
        if h == 0:
            continue
        src = field(j)
        r = slice(packing.row_at[j], packing.row_at[j] + h)
        c = slice(packing.lane_at[j], packing.lane_at[j] + w)
        top = slice(ny - h, ny)
        bottom = slice(0, h)
        up[r, :] = src[top, :]
        down[r, :] = src[bottom, :]
        east[:, c] = src[:, lanes - w : lanes]
        west[:, c] = src[:, 0:w]
        up_east[r, :] = src[top, lanes - cw : lanes]
        up_west[r, :] = src[top, 0:cw]
        down_east[r, :] = src[bottom, lanes - cw : lanes]
        down_west[r, :] = src[bottom, 0:cw]


def send_pieces(packed):
    count_y = lax.axis_size("gy")
    count_x = lax.axis_size("gx")

    def move(piece, dy, dx):
        pairs = []
        for y in range(count_y):
            for x in range(count_x):
                ty, tx = y + dy, x + dx
                if 0 <= ty < count_y and 0 <= tx < count_x:
                    pairs.append((y * count_x + x, ty * count_x + tx))
        return lax.ppermute(piece, ("gy", "gx"), pairs)

    steps = ((1, 0), (-1, 0), (0, 1), (0, -1), (1, 1), (1, -1), (-1, 1), (-1, -1))
    return tuple(move(p, dy, dx) for p, (dy, dx) in zip(packed, steps))


def assemble(dst, own, pieces, j, frame, packing):
    ny, lanes, oy, ox, cw = frame.ny, frame.lanes, frame.oy, frame.ox, packing.corner
    below, above, left, right, b_l, b_r, a_l, a_r = pieces
    h, w = packing.rows[j], packing.lanes[j]
    mid = slice(oy, oy + ny)
    centre = slice(ox, ox + lanes)
    dst[mid, centre] = own[...]
    if h == 0:
        return
    r = slice(packing.row_at[j], packing.row_at[j] + h)
    c = slice(packing.lane_at[j], packing.lane_at[j] + w)
    lo = slice(oy - h, oy)
    hi = slice(oy + ny, oy + ny + h)
    west = slice(ox - w, ox)
    east = slice(ox + lanes, ox + lanes + w)
    dst[lo, centre] = below[r, :]
    dst[hi, centre] = above[r, :]
    dst[mid, west] = left[:, c]
    dst[mid, east] = right[:, c]
    dst[lo, west] = b_l[r, cw - w : cw]
    dst[lo, east] = b_r[r, 0:w]
    dst[hi, west] = a_l[r, cw - w : cw]
    dst[hi, east] = a_r[r, 0:w]


def window(frame, depth):
    r0 = max(0, (frame.oy - depth) // 8 * 8)
    r1 = min(frame.ey, round_up(frame.oy + frame.ny + depth, 8))
    l0 = max(0, (frame.ox - depth * CZ) // 128 * 128)
    l1 = min(frame.el, round_up(frame.ox + frame.lanes + depth * CZ, 128))
    return r0, r1, l0, l1


def stepper(frame, bounds_ref, win):
    r0, r1, l0, l1 = win
    ey, el = r1 - r0, l1 - l0
    row = lax.broadcasted_iota(jnp.int32, (ey, el), 0) + r0
    lane = lax.broadcasted_iota(jnp.int32, (ey, el), 1) + l0
    inside = (
        (row >= bounds_ref[0])
        & (row < bounds_ref[1])
        & (lane >= bounds_ref[2])
        & (lane < bounds_ref[3])
    )
    depth = lane % CZ
    zero = jnp.zeros((ey, el), jnp.float32)
    z_ok = {d: (depth + d >= 0) & (depth + d < CZ) for d in (-2, -1, 1, 2)}

    def rows(a, d):
        return a if d == 0 else pltpu.roll(a, (-d) % ey, 0)

    def lanes(a, d):
        return a if d == 0 else pltpu.roll(a, (-d) % el, 1)

    def deep(a, d):
        return a if d == 0 else jnp.where(z_ok[d], lanes(a, d), zero)

    def forward_diff(s):
        return coef_near * (s(1) - s(0)) + coef_far * (s(2) - s(-1))

    def backward_diff(s):
        return coef_near * (s(0) - s(-1)) + coef_far * (s(1) - s(-2))

    def wave_step(state, stiff, att):
        pres, vel_y, vel_x, vel_z, memory = state
        vel_y = jnp.where(inside, vel_y - forward_diff(lambda d: rows(pres, d)), zero)
        vel_x = jnp.where(inside, vel_x - forward_diff(lambda d: lanes(pres, d * CZ)), zero)
        vel_z = vel_z - forward_diff(lambda d: deep(pres, d))
        div = (
            backward_diff(lambda d: rows(vel_y, d))
            + backward_diff(lambda d: lanes(vel_x, d * CZ))
            + backward_diff(lambda d: deep(vel_z, d))
        )
        memory = memory - relax_rate * (memory + stiff * att * div)
        pres = jnp.where(inside, pres - stiff * (1.0 + att) * div - memory, zero)
        return [pres, vel_y, vel_x, vel_z, memory], div

    return wave_step, row, lane


def window_kernel(frame, packing, bounds_ref, source_ref, wave_ref, *rest):
    fwd_ref, adj_ref, vel_ref, att_ref, gauge_ref = rest[:5]
    pieces = rest[5:13]
    end_ref, start_ref, grad_ref, ext, inject, divs = rest[13:]
    owns = (
        [fwd_ref.at[0, k] for k in range(5)]
        + [adj_ref.at[0, k] for k in range(5)]
        + [vel_ref, att_ref]
        + [gauge_ref.at[k] for k in range(4)]
    )
    for j in range(16):
        assemble(ext.at[j], owns[j], pieces, j, frame, packing)
    vel_all = ext[10]
    att_all = ext[11]
    stiff_all = stiff_scale * vel_all * vel_all

    def cut(a, inner, outer):
        return a[inner[0] - outer[0] : inner[1] - outer[0], inner[2] - outer[2] : inner[3] - outer[2]]

    full = (0, frame.ey, 0, frame.el)
    tile = (frame.oy, frame.oy + frame.ny, frame.ox, frame.ox + frame.lanes)

    state = [ext[k] for k in range(5)]
    where = full
    for step in range(STEPS):
        win = window(frame, 3 * (STEPS - step) + 3 * (STEPS - 1))
        state = [cut(a, win, where) for a in state]
        where = win
        wave_step, row, lane = stepper(frame, bounds_ref, win)
        source = (row == source_ref[0]) & (lane == source_ref[1])
        state, div = wave_step(state, cut(stiff_all, win, full), cut(att_all, win, full))
        state[0] = state[0] + jnp.where(source, wave_ref[step], jnp.float32(0.0))
        divs[step] = cut(div, tile, win)
        inject[step, win[0] : win[1], win[2] : win[3]] = (
            cut(ext[12], win, full) * state[0] - cut(ext[13 + step], win, full)
        )
    for k in range(5):
        end_ref[0, k] = cut(state[k], tile, where)

    velocity = cut(vel_all, tile, full)
    attenuation = cut(att_all, tile, full)
    stiff_own = cut(stiff_all, tile, full)
    adj = [ext[5 + k] for k in range(5)]
    where = full
    grad_v = jnp.zeros((frame.ny, frame.lanes), jnp.float32)
    grad_a = jnp.zeros((frame.ny, frame.lanes), jnp.float32)
    for step in range(STEPS - 1, -1, -1):
        win = window(frame, 3 * (step + 1))
        adj = [cut(a, win, where) for a in adj]
        where = win
        wave_step, row, lane = stepper(frame, bounds_ref, win)
        adj, unused = wave_step(adj, cut(stiff_all, win, full), cut(att_all, win, full))
        adj[0] = adj[0] + inject[step, win[0] : win[1], win[2] : win[3]]
        div = divs[step]
        q = cut(adj[0], tile, win)
        m = cut(adj[4], tile, win)
        deriv_q = (relax_rate * attenuation - (1.0 + attenuation)) * div
        deriv_m = -relax_rate * attenuation * div
        grad_v = grad_v + (q * deriv_q + m * deriv_m) * (2.0 * stiff_scale * velocity)
        grad_a = grad_a + (q * (relax_rate - 1.0) - m * relax_rate) * stiff_own * div
    for k in range(5):
        start_ref[0, k] = cut(adj[k], tile, where)
    for c, g in enumerate((grad_v, grad_a)):
        grad_ref[c] = g.reshape(frame.ny // BY, BY, frame.lanes).sum(axis=1)


def vmem():
    return pl.BlockSpec(memory_space=pltpu.VMEM)


def smem():
    return pl.BlockSpec(memory_space=pltpu.SMEM)


def on_device(
    forward_start,
    adjoint_end,
    velocity,
    attenuation,
    wavelet,
    source_cell,
    receiver_cells,
    observed,
    aperture,
    block_slot,
):
    nz = CZ
    ny = velocity.shape[0]
    lanes = velocity.shape[1]
    nx = lanes // nz
    frame = Frame(ny, lanes)
    index_y = lax.axis_index("gy")
    index_x = lax.axis_index("gx")
    total_y = ny * lax.axis_size("gy")
    total_x = nx * lax.axis_size("gx")

    row_lo = frame.oy - index_y * ny
    lane_lo = frame.ox - index_x * lanes
    bounds = jnp.stack([row_lo, row_lo + total_y, lane_lo, lane_lo + total_x * nz]).astype(jnp.int32)

    cell = source_cell[0, 0]
    src_row = cell // (total_x * nz) + row_lo
    src_lane = cell % (total_x * nz) + lane_lo
    source = jnp.stack([src_row, src_lane]).astype(jnp.int32)

    recs = receiver_cells[0, 0]
    at_row = lax.div(recs, lanes)[:, None] == lax.broadcasted_iota(jnp.int32, (recs.shape[0], ny), 1)
    at_lane = lax.rem(recs, lanes)[:, None] == lax.broadcasted_iota(jnp.int32, (recs.shape[0], lanes), 1)
    weights = jnp.concatenate([jnp.ones((1, recs.shape[0]), jnp.float32), observed[0, :, 0]], axis=0)
    gauge = jnp.einsum(
        "nky,kl->nyl",
        weights[:, :, None] * at_row.astype(jnp.float32)[None],
        at_lane.astype(jnp.float32),
        precision=lax.Precision.HIGHEST,
    )

    packing = Packing(frame)
    packed = pl.pallas_call(
        lambda *refs: pack_kernel(frame, packing, *refs),
        out_shape=tuple(
            jax.ShapeDtypeStruct(shape, jnp.float32)
            for shape in (
                [(packing.total_rows, lanes)] * 2
                + [(ny, packing.total_lanes)] * 2
                + [(packing.total_rows, packing.corner)] * 4
            )
        ),
        in_specs=[vmem()] * 5,
        out_specs=tuple([vmem()] * 8),
    )(forward_start, adjoint_end, velocity, attenuation, gauge)
    pieces = send_pieces(packed)

    ext_shape = (frame.ey, frame.el)
    forward_end, adjoint_start, row_sums = pl.pallas_call(
        lambda *refs: window_kernel(frame, packing, *refs),
        out_shape=(
            jax.ShapeDtypeStruct((1, 5, ny, lanes), jnp.float32),
            jax.ShapeDtypeStruct((1, 5, ny, lanes), jnp.float32),
            jax.ShapeDtypeStruct((2, ny // BY, lanes), jnp.float32),
        ),
        in_specs=[smem(), smem(), smem()] + [vmem()] * 13,
        out_specs=(vmem(), vmem(), vmem()),
        scratch_shapes=[
            pltpu.VMEM((16,) + ext_shape, jnp.float32),
            pltpu.VMEM((STEPS,) + ext_shape, jnp.float32),
            pltpu.VMEM((STEPS, ny, lanes), jnp.float32),
        ],
        compiler_params=pltpu.CompilerParams(vmem_limit_bytes=48 * 1024 * 1024),
    )(bounds, source, wavelet[0], forward_start, adjoint_end, velocity, attenuation, gauge, *pieces)

    grad_scale = float(BY * BX * BZ) ** (-0.5)
    weight = aperture[0, 0].astype(jnp.float32)
    blocks = row_sums.reshape(2, ny // BY, nx // BX, BX, nz // BZ, BZ).sum(axis=(3, 5))
    sums = blocks.transpose(1, 2, 3, 0).reshape(-1, 2) * (grad_scale * weight)
    slots = block_slot[0]
    ordered = jnp.zeros(sums.shape, jnp.float32).at[slots].set(sums)
    shots = lax.axis_size("shot")
    me = lax.axis_index("shot")
    held = ordered.reshape(shots, -1, 2)
    span = shots // 2
    while span >= 1:
        halves = held.reshape(2, -1, held.shape[1], 2)
        bit = (me // span) % 2 == 1
        mine = jnp.where(bit, halves[1], halves[0])
        other = jnp.where(bit, halves[0], halves[1])
        held = mine + lax.ppermute(other, "shot", [(i, i ^ span) for i in range(shots)])
        span //= 2
    coarse = held[0]
    model_gradient = coarse.T[:, None, :]
    return (forward_end, adjoint_start, model_gradient)


def solution(mesh):
    placed = (
        P("shot", None, "gy", "gx"),
        P("shot", None, "gy", "gx"),
        P("gy", "gx"),
        P("gy", "gx"),
        P("shot", None),
        P("shot", None),
        P("shot", ("gy", "gx"), None),
        P("shot", None, ("gy", "gx"), None),
        P("shot", ("gy", "gx")),
        P(("gy", "gx"), None),
    )
    return jax.shard_map(
        on_device,
        mesh=mesh,
        in_specs=placed,
        out_specs=(
            P("shot", None, "gy", "gx"),
            P("shot", None, "gy", "gx"),
            P(None, ("gy", "gx"), "shot"),
        ),
        check_vma=False,
    )
```

```python
import jax
import jax.numpy as jnp
from jax import lax
from jax.experimental import pallas as pl
from jax.experimental.pallas import tpu as pltpu
from jax.sharding import PartitionSpec as P

CZ = 32
STEPS = 3
BY = 8
BX = 8
BZ = 8
HALO = 3 * STEPS + 3 * (STEPS - 1)

coef_near = 9.0 / 8.0
coef_far = -1.0 / 24.0
stiff_scale = 0.02
relax_rate = 0.3


def round_up(value, unit):
    return (value + unit - 1) // unit * unit


class Frame:
    def __init__(self, ny, lanes):
        self.ny = ny
        self.lanes = lanes
        self.oy = round_up(HALO, 8)
        self.ox = round_up(HALO * CZ, 128)
        self.ey = 2 * self.oy + ny
        self.el = 2 * self.ox + lanes


NEEDS = (
    (15, 15), (14, 12), (12, 14), (12, 12), (12, 12),
    (9, 9), (8, 6), (6, 8), (6, 6), (6, 6),
    (12, 12), (12, 12),
    (6, 6), (0, 0), (3, 3), (6, 6),
)


class Packing:
    def __init__(self, frame):
        self.rows = [h for h, w in NEEDS]
        self.lanes = [round_up(w * CZ, 128) for h, w in NEEDS]
        self.row_at = [sum(self.rows[:j]) for j in range(len(NEEDS))]
        self.lane_at = [sum(self.lanes[:j]) for j in range(len(NEEDS))]
        self.total_rows = sum(self.rows)
        self.total_lanes = sum(self.lanes)
        self.corner = frame.ox


def pack_kernel(frame, packing, fwd_ref, adj_ref, vel_ref, att_ref, rec_row_ref, rec_col_ref, weight_ref, *outs):
    up, down, east, west, up_east, up_west, down_east, down_west, gauge_ref = outs
    ny, lanes, cw = frame.ny, frame.lanes, packing.corner
    count = rec_row_ref.shape[1]
    at_row = lax.broadcasted_iota(jnp.int32, (ny, count), 0) == lax.div(rec_row_ref[...], lanes)
    at_lane = (
        lax.rem(rec_col_ref[...], lanes) == lax.broadcasted_iota(jnp.int32, (count, lanes), 1)
    ).astype(jnp.float32)
    for n in range(1 + STEPS):
        gauge_ref[n] = jnp.dot(
            jnp.where(at_row, weight_ref[n : n + 1, :], 0.0),
            at_lane,
            precision=lax.Precision.HIGHEST,
            preferred_element_type=jnp.float32,
        )

    def field(j):
        if j < 5:
            return fwd_ref.at[0, j]
        if j < 10:
            return adj_ref.at[0, j - 5]
        if j == 10:
            return vel_ref
        if j == 11:
            return att_ref
        return gauge_ref.at[j - 12]

    for j in range(len(NEEDS)):
        h, w = packing.rows[j], packing.lanes[j]
        if h == 0:
            continue
        src = field(j)
        r = slice(packing.row_at[j], packing.row_at[j] + h)
        c = slice(packing.lane_at[j], packing.lane_at[j] + w)
        top = slice(ny - h, ny)
        bottom = slice(0, h)
        up[r, :] = src[top, :]
        down[r, :] = src[bottom, :]
        east[:, c] = src[:, lanes - w : lanes]
        west[:, c] = src[:, 0:w]
        up_east[r, :] = src[top, lanes - cw : lanes]
        up_west[r, :] = src[top, 0:cw]
        down_east[r, :] = src[bottom, lanes - cw : lanes]
        down_west[r, :] = src[bottom, 0:cw]


def send_pieces(packed):
    count_y = lax.axis_size("gy")
    count_x = lax.axis_size("gx")

    def move(piece, dy, dx):
        pairs = []
        for y in range(count_y):
            for x in range(count_x):
                ty, tx = y + dy, x + dx
                if 0 <= ty < count_y and 0 <= tx < count_x:
                    pairs.append((y * count_x + x, ty * count_x + tx))
        return lax.ppermute(piece, ("gy", "gx"), pairs)

    steps = ((1, 0), (-1, 0), (0, 1), (0, -1), (1, 1), (1, -1), (-1, 1), (-1, -1))
    return tuple(move(p, dy, dx) for p, (dy, dx) in zip(packed, steps))


def assemble(dst, own, pieces, j, frame, packing):
    ny, lanes, oy, ox, cw = frame.ny, frame.lanes, frame.oy, frame.ox, packing.corner
    below, above, left, right, b_l, b_r, a_l, a_r = pieces
    h, w = packing.rows[j], packing.lanes[j]
    mid = slice(oy, oy + ny)
    centre = slice(ox, ox + lanes)
    dst[mid, centre] = own[...]
    if h == 0:
        return
    r = slice(packing.row_at[j], packing.row_at[j] + h)
    c = slice(packing.lane_at[j], packing.lane_at[j] + w)
    lo = slice(oy - h, oy)
    hi = slice(oy + ny, oy + ny + h)
    west = slice(ox - w, ox)
    east = slice(ox + lanes, ox + lanes + w)
    dst[lo, centre] = below[r, :]
    dst[hi, centre] = above[r, :]
    dst[mid, west] = left[:, c]
    dst[mid, east] = right[:, c]
    dst[lo, west] = b_l[r, cw - w : cw]
    dst[lo, east] = b_r[r, 0:w]
    dst[hi, west] = a_l[r, cw - w : cw]
    dst[hi, east] = a_r[r, 0:w]


def window(frame, depth):
    r0 = max(0, (frame.oy - depth) // 8 * 8)
    r1 = min(frame.ey, round_up(frame.oy + frame.ny + depth, 8))
    l0 = max(0, (frame.ox - depth * CZ) // 128 * 128)
    l1 = min(frame.el, round_up(frame.ox + frame.lanes + depth * CZ, 128))
    return r0, r1, l0, l1


def stepper(frame, bounds_ref, win):
    r0, r1, l0, l1 = win
    ey, el = r1 - r0, l1 - l0
    row = lax.broadcasted_iota(jnp.int32, (ey, el), 0) + r0
    lane = lax.broadcasted_iota(jnp.int32, (ey, el), 1) + l0
    inside = (
        (row >= bounds_ref[0])
        & (row < bounds_ref[1])
        & (lane >= bounds_ref[2])
        & (lane < bounds_ref[3])
    )
    depth = lane % CZ
    zero = jnp.zeros((ey, el), jnp.float32)
    z_ok = {d: (depth + d >= 0) & (depth + d < CZ) for d in (-2, -1, 1, 2)}

    def rows(a, d):
        return a if d == 0 else pltpu.roll(a, (-d) % ey, 0)

    def lanes(a, d):
        return a if d == 0 else pltpu.roll(a, (-d) % el, 1)

    def deep(a, d):
        return a if d == 0 else jnp.where(z_ok[d], lanes(a, d), zero)

    def forward_diff(s):
        return coef_near * (s(1) - s(0)) + coef_far * (s(2) - s(-1))

    def backward_diff(s):
        return coef_near * (s(0) - s(-1)) + coef_far * (s(1) - s(-2))

    def wave_step(state, stiff, att):
        pres, vel_y, vel_x, vel_z, memory = state
        vel_y = jnp.where(inside, vel_y - forward_diff(lambda d: rows(pres, d)), zero)
        vel_x = jnp.where(inside, vel_x - forward_diff(lambda d: lanes(pres, d * CZ)), zero)
        vel_z = vel_z - forward_diff(lambda d: deep(pres, d))
        div = (
            backward_diff(lambda d: rows(vel_y, d))
            + backward_diff(lambda d: lanes(vel_x, d * CZ))
            + backward_diff(lambda d: deep(vel_z, d))
        )
        memory = memory - relax_rate * (memory + stiff * att * div)
        pres = jnp.where(inside, pres - stiff * (1.0 + att) * div - memory, zero)
        return [pres, vel_y, vel_x, vel_z, memory], div

    return wave_step, row, lane


def window_kernel(frame, packing, bounds_ref, source_ref, wave_ref, *rest):
    fwd_ref, adj_ref, vel_ref, att_ref, gauge_ref = rest[:5]
    pieces = rest[5:13]
    end_ref, start_ref, grad_ref, ext, inject, divs = rest[13:]
    owns = (
        [fwd_ref.at[0, k] for k in range(5)]
        + [adj_ref.at[0, k] for k in range(5)]
        + [vel_ref, att_ref]
        + [gauge_ref.at[k] for k in range(4)]
    )
    for j in range(16):
        assemble(ext.at[j], owns[j], pieces, j, frame, packing)
    vel_all = ext[10]
    att_all = ext[11]
    stiff_all = stiff_scale * vel_all * vel_all

    def cut(a, inner, outer):
        return a[inner[0] - outer[0] : inner[1] - outer[0], inner[2] - outer[2] : inner[3] - outer[2]]

    full = (0, frame.ey, 0, frame.el)
    tile = (frame.oy, frame.oy + frame.ny, frame.ox, frame.ox + frame.lanes)

    state = [ext[k] for k in range(5)]
    where = full
    for step in range(STEPS):
        win = window(frame, 3 * (STEPS - step) + 3 * (STEPS - 1))
        state = [cut(a, win, where) for a in state]
        where = win
        wave_step, row, lane = stepper(frame, bounds_ref, win)
        source = (row == source_ref[0]) & (lane == source_ref[1])
        state, div = wave_step(state, cut(stiff_all, win, full), cut(att_all, win, full))
        state[0] = state[0] + jnp.where(source, wave_ref[step], jnp.float32(0.0))
        divs[step] = cut(div, tile, win)
        inject[step, win[0] : win[1], win[2] : win[3]] = (
            cut(ext[12], win, full) * state[0] - cut(ext[13 + step], win, full)
        )
    for k in range(5):
        end_ref[0, k] = cut(state[k], tile, where)

    velocity = cut(vel_all, tile, full)
    attenuation = cut(att_all, tile, full)
    stiff_own = cut(stiff_all, tile, full)
    adj = [ext[5 + k] for k in range(5)]
    where = full
    grad_v = jnp.zeros((frame.ny, frame.lanes), jnp.float32)
    grad_a = jnp.zeros((frame.ny, frame.lanes), jnp.float32)
    for step in range(STEPS - 1, -1, -1):
        win = window(frame, 3 * (step + 1))
        adj = [cut(a, win, where) for a in adj]
        where = win
        wave_step, row, lane = stepper(frame, bounds_ref, win)
        adj, unused = wave_step(adj, cut(stiff_all, win, full), cut(att_all, win, full))
        adj[0] = adj[0] + inject[step, win[0] : win[1], win[2] : win[3]]
        div = divs[step]
        q = cut(adj[0], tile, win)
        m = cut(adj[4], tile, win)
        deriv_q = (relax_rate * attenuation - (1.0 + attenuation)) * div
        deriv_m = -relax_rate * attenuation * div
        grad_v = grad_v + (q * deriv_q + m * deriv_m) * (2.0 * stiff_scale * velocity)
        grad_a = grad_a + (q * (relax_rate - 1.0) - m * relax_rate) * stiff_own * div
    for k in range(5):
        start_ref[0, k] = cut(adj[k], tile, where)
    for c, g in enumerate((grad_v, grad_a)):
        grad_ref[c] = g.reshape(frame.ny // BY, BY, frame.lanes).sum(axis=1)


def vmem():
    return pl.BlockSpec(memory_space=pltpu.VMEM)


def smem():
    return pl.BlockSpec(memory_space=pltpu.SMEM)


def on_device(
    forward_start,
    adjoint_end,
    velocity,
    attenuation,
    wavelet,
    source_cell,
    receiver_cells,
    observed,
    aperture,
    block_slot,
):
    nz = CZ
    ny = velocity.shape[0]
    lanes = velocity.shape[1]
    nx = lanes // nz
    frame = Frame(ny, lanes)
    index_y = lax.axis_index("gy")
    index_x = lax.axis_index("gx")
    total_y = ny * lax.axis_size("gy")
    total_x = nx * lax.axis_size("gx")

    row_lo = frame.oy - index_y * ny
    lane_lo = frame.ox - index_x * lanes
    bounds = jnp.stack([row_lo, row_lo + total_y, lane_lo, lane_lo + total_x * nz]).astype(jnp.int32)

    cell = source_cell[0, 0]
    src_row = cell // (total_x * nz) + row_lo
    src_lane = cell % (total_x * nz) + lane_lo
    source = jnp.stack([src_row, src_lane]).astype(jnp.int32)

    recs = receiver_cells[0, 0]
    weights = jnp.concatenate([jnp.ones((1, recs.shape[0]), jnp.float32), observed[0, :, 0]], axis=0)

    packing = Packing(frame)
    packed = pl.pallas_call(
        lambda *refs: pack_kernel(frame, packing, *refs),
        out_shape=tuple(
            jax.ShapeDtypeStruct(shape, jnp.float32)
            for shape in (
                [(packing.total_rows, lanes)] * 2
                + [(ny, packing.total_lanes)] * 2
                + [(packing.total_rows, packing.corner)] * 4
                + [(1 + STEPS, ny, lanes)]
            )
        ),
        in_specs=[vmem()] * 7,
        out_specs=tuple([vmem()] * 9),
    )(forward_start, adjoint_end, velocity, attenuation, recs[None], recs[:, None], weights)
    gauge = packed[8]
    pieces = send_pieces(packed[:8])

    ext_shape = (frame.ey, frame.el)
    forward_end, adjoint_start, row_sums = pl.pallas_call(
        lambda *refs: window_kernel(frame, packing, *refs),
        out_shape=(
            jax.ShapeDtypeStruct((1, 5, ny, lanes), jnp.float32),
            jax.ShapeDtypeStruct((1, 5, ny, lanes), jnp.float32),
            jax.ShapeDtypeStruct((2, ny // BY, lanes), jnp.float32),
        ),
        in_specs=[smem(), smem(), smem()] + [vmem()] * 13,
        out_specs=(vmem(), vmem(), vmem()),
        scratch_shapes=[
            pltpu.VMEM((16,) + ext_shape, jnp.float32),
            pltpu.VMEM((STEPS,) + ext_shape, jnp.float32),
            pltpu.VMEM((STEPS, ny, lanes), jnp.float32),
        ],
        compiler_params=pltpu.CompilerParams(vmem_limit_bytes=48 * 1024 * 1024),
    )(bounds, source, wavelet[0], forward_start, adjoint_end, velocity, attenuation, gauge, *pieces)

    grad_scale = float(BY * BX * BZ) ** (-0.5)
    weight = aperture[0, 0].astype(jnp.float32)
    blocks = row_sums.reshape(2, ny // BY, nx // BX, BX, nz // BZ, BZ).sum(axis=(3, 5))
    sums = blocks.transpose(1, 2, 3, 0).reshape(-1, 2) * (grad_scale * weight)
    slots = block_slot[0]
    ordered = jnp.zeros(sums.shape, jnp.float32).at[slots].set(sums)
    shots = lax.axis_size("shot")
    me = lax.axis_index("shot")
    held = ordered.reshape(shots, -1, 2)
    span = shots // 2
    while span >= 1:
        halves = held.reshape(2, -1, held.shape[1], 2)
        bit = (me // span) % 2 == 1
        mine = jnp.where(bit, halves[1], halves[0])
        other = jnp.where(bit, halves[0], halves[1])
        held = mine + lax.ppermute(other, "shot", [(i, i ^ span) for i in range(shots)])
        span //= 2
    coarse = held[0]
    model_gradient = coarse.T[:, None, :]
    return (forward_end, adjoint_start, model_gradient)


def solution(mesh):
    placed = (
        P("shot", None, "gy", "gx"),
        P("shot", None, "gy", "gx"),
        P("gy", "gx"),
        P("gy", "gx"),
        P("shot", None),
        P("shot", None),
        P("shot", ("gy", "gx"), None),
        P("shot", None, ("gy", "gx"), None),
        P("shot", ("gy", "gx")),
        P(("gy", "gx"), None),
    )
    return jax.shard_map(
        on_device,
        mesh=mesh,
        in_specs=placed,
        out_specs=(
            P("shot", None, "gy", "gx"),
            P("shot", None, "gy", "gx"),
            P(None, ("gy", "gx"), "shot"),
        ),
        check_vma=False,
    )
```

```python
import jax
import jax.numpy as jnp
from jax import lax
from jax.experimental import pallas as pl
from jax.experimental.pallas import tpu as pltpu
from jax.sharding import PartitionSpec as P

CZ = 32
STEPS = 3
BY = 8
BX = 8
BZ = 8
HALO = 3 * STEPS + 3 * (STEPS - 1)

coef_near = 9.0 / 8.0
coef_far = -1.0 / 24.0
stiff_scale = 0.02
relax_rate = 0.3


def round_up(value, unit):
    return (value + unit - 1) // unit * unit


class Frame:
    def __init__(self, ny, lanes):
        self.ny = ny
        self.lanes = lanes
        self.oy = round_up(HALO, 8)
        self.ox = round_up(HALO * CZ, 128)
        self.ey = 2 * self.oy + ny
        self.el = 2 * self.ox + lanes


NEEDS = (
    (15, 15), (14, 12), (12, 14), (12, 12), (12, 12),
    (9, 9), (8, 6), (6, 8), (6, 6), (6, 6),
    (12, 12), (12, 12),
    (6, 6), (0, 0), (3, 3), (6, 6),
)


class Packing:
    def __init__(self, frame):
        self.rows = [h for h, w in NEEDS]
        self.lanes = [round_up(w * CZ, 128) for h, w in NEEDS]
        self.row_at = [sum(self.rows[:j]) for j in range(len(NEEDS))]
        self.lane_at = [sum(self.lanes[:j]) for j in range(len(NEEDS))]
        self.total_rows = sum(self.rows)
        self.total_lanes = sum(self.lanes)
        self.corner = frame.ox
        shelves = []
        self.corner_at = [(0, 0)] * len(NEEDS)
        order = sorted(range(len(NEEDS)), key=lambda j: (-self.lanes[j], -self.rows[j]))
        for j in order:
            h, w = self.rows[j], self.lanes[j]
            if h == 0:
                continue
            for shelf in shelves:
                if shelf[2] + w <= self.corner and shelf[1] >= h:
                    self.corner_at[j] = (shelf[0], shelf[2])
                    shelf[2] += w
                    break
            else:
                top = sum(shelf[1] for shelf in shelves)
                shelves.append([top, h, w])
                self.corner_at[j] = (top, 0)
        self.corner_rows = sum(shelf[1] for shelf in shelves)


def pack_kernel(frame, packing, fwd_ref, adj_ref, vel_ref, att_ref, gauge_ref, *outs):
    up, down, east, west, up_east, up_west, down_east, down_west = outs
    ny, lanes, cw = frame.ny, frame.lanes, packing.corner

    def field(j):
        if j < 5:
            return fwd_ref.at[0, j]
        if j < 10:
            return adj_ref.at[0, j - 5]
        if j == 10:
            return vel_ref
        if j == 11:
            return att_ref
        return gauge_ref.at[j - 12]

    for j in range(len(NEEDS)):
        h, w = packing.rows[j], packing.lanes[j]
        if h == 0:
            continue
        src = field(j)
        r = slice(packing.row_at[j], packing.row_at[j] + h)
        c = slice(packing.lane_at[j], packing.lane_at[j] + w)
        top = slice(ny - h, ny)
        bottom = slice(0, h)
        up[r, :] = src[top, :]
        down[r, :] = src[bottom, :]
        east[:, c] = src[:, lanes - w : lanes]
        west[:, c] = src[:, 0:w]
        cr, cl = packing.corner_at[j]
        cr = slice(cr, cr + h)
        cl = slice(cl, cl + w)
        up_east[cr, cl] = src[top, lanes - w : lanes]
        up_west[cr, cl] = src[top, 0:w]
        down_east[cr, cl] = src[bottom, lanes - w : lanes]
        down_west[cr, cl] = src[bottom, 0:w]


def send_pieces(packed):
    count_y = lax.axis_size("gy")
    count_x = lax.axis_size("gx")

    def move(piece, dy, dx):
        pairs = []
        for y in range(count_y):
            for x in range(count_x):
                ty, tx = y + dy, x + dx
                if 0 <= ty < count_y and 0 <= tx < count_x:
                    pairs.append((y * count_x + x, ty * count_x + tx))
        return lax.ppermute(piece, ("gy", "gx"), pairs)

    steps = ((1, 0), (-1, 0), (0, 1), (0, -1), (1, 1), (1, -1), (-1, 1), (-1, -1))
    return tuple(move(p, dy, dx) for p, (dy, dx) in zip(packed, steps))


def assemble(dst, own, pieces, j, frame, packing):
    ny, lanes, oy, ox, cw = frame.ny, frame.lanes, frame.oy, frame.ox, packing.corner
    below, above, left, right, b_l, b_r, a_l, a_r = pieces
    h, w = packing.rows[j], packing.lanes[j]
    mid = slice(oy, oy + ny)
    centre = slice(ox, ox + lanes)
    dst[mid, centre] = own[...]
    if h == 0:
        return
    r = slice(packing.row_at[j], packing.row_at[j] + h)
    c = slice(packing.lane_at[j], packing.lane_at[j] + w)
    lo = slice(oy - h, oy)
    hi = slice(oy + ny, oy + ny + h)
    west = slice(ox - w, ox)
    east = slice(ox + lanes, ox + lanes + w)
    dst[lo, centre] = below[r, :]
    dst[hi, centre] = above[r, :]
    dst[mid, west] = left[:, c]
    dst[mid, east] = right[:, c]
    cr, cl = packing.corner_at[j]
    cr = slice(cr, cr + h)
    cl = slice(cl, cl + w)
    dst[lo, west] = b_l[cr, cl]
    dst[lo, east] = b_r[cr, cl]
    dst[hi, west] = a_l[cr, cl]
    dst[hi, east] = a_r[cr, cl]


def window(frame, depth):
    r0 = max(0, (frame.oy - depth) // 8 * 8)
    r1 = min(frame.ey, round_up(frame.oy + frame.ny + depth, 8))
    l0 = max(0, (frame.ox - depth * CZ) // 128 * 128)
    l1 = min(frame.el, round_up(frame.ox + frame.lanes + depth * CZ, 128))
    return r0, r1, l0, l1


def stepper(frame, bounds_ref, win):
    r0, r1, l0, l1 = win
    ey, el = r1 - r0, l1 - l0
    row = lax.broadcasted_iota(jnp.int32, (ey, el), 0) + r0
    lane = lax.broadcasted_iota(jnp.int32, (ey, el), 1) + l0
    inside = (
        (row >= bounds_ref[0])
        & (row < bounds_ref[1])
        & (lane >= bounds_ref[2])
        & (lane < bounds_ref[3])
    )
    depth = lane % CZ
    zero = jnp.zeros((ey, el), jnp.float32)
    z_ok = {d: (depth + d >= 0) & (depth + d < CZ) for d in (-2, -1, 1, 2)}

    def rows(a, d):
        return a if d == 0 else pltpu.roll(a, (-d) % ey, 0)

    def lanes(a, d):
        return a if d == 0 else pltpu.roll(a, (-d) % el, 1)

    def deep(a, d):
        return a if d == 0 else jnp.where(z_ok[d], lanes(a, d), zero)

    def forward_diff(s):
        return coef_near * (s(1) - s(0)) + coef_far * (s(2) - s(-1))

    def backward_diff(s):
        return coef_near * (s(0) - s(-1)) + coef_far * (s(1) - s(-2))

    def wave_step(state, stiff, att):
        pres, vel_y, vel_x, vel_z, memory = state
        vel_y = jnp.where(inside, vel_y - forward_diff(lambda d: rows(pres, d)), zero)
        vel_x = jnp.where(inside, vel_x - forward_diff(lambda d: lanes(pres, d * CZ)), zero)
        vel_z = vel_z - forward_diff(lambda d: deep(pres, d))
        div = (
            backward_diff(lambda d: rows(vel_y, d))
            + backward_diff(lambda d: lanes(vel_x, d * CZ))
            + backward_diff(lambda d: deep(vel_z, d))
        )
        memory = memory - relax_rate * (memory + stiff * att * div)
        pres = jnp.where(inside, pres - stiff * (1.0 + att) * div - memory, zero)
        return [pres, vel_y, vel_x, vel_z, memory], div

    return wave_step, row, lane


def window_kernel(frame, packing, bounds_ref, source_ref, wave_ref, *rest):
    fwd_ref, adj_ref, vel_ref, att_ref, gauge_ref = rest[:5]
    pieces = rest[5:13]
    end_ref, start_ref, grad_ref, ext, inject, divs = rest[13:]
    owns = (
        [fwd_ref.at[0, k] for k in range(5)]
        + [adj_ref.at[0, k] for k in range(5)]
        + [vel_ref, att_ref]
        + [gauge_ref.at[k] for k in range(4)]
    )
    for j in range(16):
        assemble(ext.at[j], owns[j], pieces, j, frame, packing)
    vel_all = ext[10]
    att_all = ext[11]
    stiff_all = stiff_scale * vel_all * vel_all

    def cut(a, inner, outer):
        return a[inner[0] - outer[0] : inner[1] - outer[0], inner[2] - outer[2] : inner[3] - outer[2]]

    full = (0, frame.ey, 0, frame.el)
    tile = (frame.oy, frame.oy + frame.ny, frame.ox, frame.ox + frame.lanes)

    state = [ext[k] for k in range(5)]
    where = full
    for step in range(STEPS):
        win = window(frame, 3 * (STEPS - step) + 3 * (STEPS - 1))
        state = [cut(a, win, where) for a in state]
        where = win
        wave_step, row, lane = stepper(frame, bounds_ref, win)
        source = (row == source_ref[0]) & (lane == source_ref[1])
        state, div = wave_step(state, cut(stiff_all, win, full), cut(att_all, win, full))
        state[0] = state[0] + jnp.where(source, wave_ref[step], jnp.float32(0.0))
        divs[step] = cut(div, tile, win)
        inject[step, win[0] : win[1], win[2] : win[3]] = (
            cut(ext[12], win, full) * state[0] - cut(ext[13 + step], win, full)
        )
    for k in range(5):
        end_ref[0, k] = cut(state[k], tile, where)

    velocity = cut(vel_all, tile, full)
    attenuation = cut(att_all, tile, full)
    stiff_own = cut(stiff_all, tile, full)
    adj = [ext[5 + k] for k in range(5)]
    where = full
    grad_v = jnp.zeros((frame.ny, frame.lanes), jnp.float32)
    grad_a = jnp.zeros((frame.ny, frame.lanes), jnp.float32)
    for step in range(STEPS - 1, -1, -1):
        win = window(frame, 3 * (step + 1))
        adj = [cut(a, win, where) for a in adj]
        where = win
        wave_step, row, lane = stepper(frame, bounds_ref, win)
        adj, unused = wave_step(adj, cut(stiff_all, win, full), cut(att_all, win, full))
        adj[0] = adj[0] + inject[step, win[0] : win[1], win[2] : win[3]]
        div = divs[step]
        q = cut(adj[0], tile, win)
        m = cut(adj[4], tile, win)
        deriv_q = (relax_rate * attenuation - (1.0 + attenuation)) * div
        deriv_m = -relax_rate * attenuation * div
        grad_v = grad_v + (q * deriv_q + m * deriv_m) * (2.0 * stiff_scale * velocity)
        grad_a = grad_a + (q * (relax_rate - 1.0) - m * relax_rate) * stiff_own * div
    for k in range(5):
        start_ref[0, k] = cut(adj[k], tile, where)
    for c, g in enumerate((grad_v, grad_a)):
        grad_ref[c] = g.reshape(frame.ny // BY, BY, frame.lanes).sum(axis=1)


def vmem():
    return pl.BlockSpec(memory_space=pltpu.VMEM)


def smem():
    return pl.BlockSpec(memory_space=pltpu.SMEM)


def on_device(
    forward_start,
    adjoint_end,
    velocity,
    attenuation,
    wavelet,
    source_cell,
    receiver_cells,
    observed,
    aperture,
    block_slot,
):
    nz = CZ
    ny = velocity.shape[0]
    lanes = velocity.shape[1]
    nx = lanes // nz
    frame = Frame(ny, lanes)
    index_y = lax.axis_index("gy")
    index_x = lax.axis_index("gx")
    total_y = ny * lax.axis_size("gy")
    total_x = nx * lax.axis_size("gx")

    row_lo = frame.oy - index_y * ny
    lane_lo = frame.ox - index_x * lanes
    bounds = jnp.stack([row_lo, row_lo + total_y, lane_lo, lane_lo + total_x * nz]).astype(jnp.int32)

    cell = source_cell[0, 0]
    src_row = cell // (total_x * nz) + row_lo
    src_lane = cell % (total_x * nz) + lane_lo
    source = jnp.stack([src_row, src_lane]).astype(jnp.int32)

    recs = receiver_cells[0, 0]
    at_row = (recs // lanes)[:, None] == lax.broadcasted_iota(jnp.int32, (recs.shape[0], ny), 1)
    at_lane = (recs % lanes)[:, None] == lax.broadcasted_iota(jnp.int32, (recs.shape[0], lanes), 1)
    weights = jnp.concatenate([jnp.ones((1, recs.shape[0]), jnp.float32), observed[0, :, 0]], axis=0)
    gauge = jnp.einsum(
        "nky,kl->nyl",
        weights[:, :, None] * at_row.astype(jnp.float32)[None],
        at_lane.astype(jnp.float32),
        precision=lax.Precision.HIGHEST,
    )

    packing = Packing(frame)
    packed = pl.pallas_call(
        lambda *refs: pack_kernel(frame, packing, *refs),
        out_shape=tuple(
            jax.ShapeDtypeStruct(shape, jnp.float32)
            for shape in (
                [(packing.total_rows, lanes)] * 2
                + [(ny, packing.total_lanes)] * 2
                + [(packing.corner_rows, packing.corner)] * 4
            )
        ),
        in_specs=[vmem()] * 5,
        out_specs=tuple([vmem()] * 8),
    )(forward_start, adjoint_end, velocity, attenuation, gauge)
    pieces = send_pieces(packed)

    ext_shape = (frame.ey, frame.el)
    forward_end, adjoint_start, row_sums = pl.pallas_call(
        lambda *refs: window_kernel(frame, packing, *refs),
        out_shape=(
            jax.ShapeDtypeStruct((1, 5, ny, lanes), jnp.float32),
            jax.ShapeDtypeStruct((1, 5, ny, lanes), jnp.float32),
            jax.ShapeDtypeStruct((2, ny // BY, lanes), jnp.float32),
        ),
        in_specs=[smem(), smem(), smem()] + [vmem()] * 13,
        out_specs=(vmem(), vmem(), vmem()),
        scratch_shapes=[
            pltpu.VMEM((16,) + ext_shape, jnp.float32),
            pltpu.VMEM((STEPS,) + ext_shape, jnp.float32),
            pltpu.VMEM((STEPS, ny, lanes), jnp.float32),
        ],
        compiler_params=pltpu.CompilerParams(vmem_limit_bytes=48 * 1024 * 1024),
    )(bounds, source, wavelet[0], forward_start, adjoint_end, velocity, attenuation, gauge, *pieces)

    grad_scale = float(BY * BX * BZ) ** (-0.5)
    weight = aperture[0, 0].astype(jnp.float32)
    blocks = row_sums.reshape(2, ny // BY, nx // BX, BX, nz // BZ, BZ).sum(axis=(3, 5))
    sums = blocks.transpose(1, 2, 3, 0).reshape(-1, 2) * (grad_scale * weight)
    slots = block_slot[0]
    ordered = jnp.zeros(sums.shape, jnp.float32).at[slots].set(sums)
    shots = lax.axis_size("shot")
    me = lax.axis_index("shot")
    held = ordered.reshape(shots, -1, 2)
    span = shots // 2
    while span >= 1:
        halves = held.reshape(2, -1, held.shape[1], 2)
        bit = (me // span) % 2 == 1
        mine = jnp.where(bit, halves[1], halves[0])
        other = jnp.where(bit, halves[0], halves[1])
        held = mine + lax.ppermute(other, "shot", [(i, i ^ span) for i in range(shots)])
        span //= 2
    coarse = held[0]
    model_gradient = coarse.T[:, None, :]
    return (forward_end, adjoint_start, model_gradient)


def solution(mesh):
    placed = (
        P("shot", None, "gy", "gx"),
        P("shot", None, "gy", "gx"),
        P("gy", "gx"),
        P("gy", "gx"),
        P("shot", None),
        P("shot", None),
        P("shot", ("gy", "gx"), None),
        P("shot", None, ("gy", "gx"), None),
        P("shot", ("gy", "gx")),
        P(("gy", "gx"), None),
    )
    return jax.shard_map(
        on_device,
        mesh=mesh,
        in_specs=placed,
        out_specs=(
            P("shot", None, "gy", "gx"),
            P("shot", None, "gy", "gx"),
            P(None, ("gy", "gx"), "shot"),
        ),
        check_vma=False,
    )
```

```python
import jax
import jax.numpy as jnp
from jax import lax
from jax.experimental import pallas as pl
from jax.experimental.pallas import tpu as pltpu
from jax.sharding import PartitionSpec as P

CZ = 32
STEPS = 3
BY = 8
BX = 8
BZ = 8
HALO = 3 * STEPS + 3 * (STEPS - 1)

coef_near = 9.0 / 8.0
coef_far = -1.0 / 24.0
stiff_scale = 0.02
relax_rate = 0.3


def round_up(value, unit):
    return (value + unit - 1) // unit * unit


class Frame:
    def __init__(self, ny, lanes):
        self.ny = ny
        self.lanes = lanes
        self.oy = round_up(HALO, 8)
        self.ox = round_up(HALO * CZ, 128)
        self.ey = 2 * self.oy + ny
        self.el = 2 * self.ox + lanes


NEEDS = (
    (15, 15), (14, 12), (12, 14), (12, 12), (12, 12),
    (9, 9), (8, 6), (6, 8), (6, 6), (6, 6),
    (12, 12), (12, 12),
    (6, 6), (0, 0), (3, 3), (6, 6),
)


class Packing:
    def __init__(self, frame):
        self.rows = [h for h, w in NEEDS]
        self.lanes = [round_up(w * CZ, 128) for h, w in NEEDS]
        self.row_at = [sum(self.rows[:j]) for j in range(len(NEEDS))]
        self.side = [w * CZ for h, w in NEEDS]
        self.lane_at = [sum(self.side[:j]) for j in range(len(NEEDS))]
        self.total_rows = sum(self.rows)
        self.total_lanes = sum(self.side)
        self.corner = frame.ox
        shelves = []
        self.corner_at = [(0, 0)] * len(NEEDS)
        order = sorted(range(len(NEEDS)), key=lambda j: (-self.lanes[j], -self.rows[j]))
        for j in order:
            h, w = self.rows[j], self.lanes[j]
            if h == 0:
                continue
            for shelf in shelves:
                if shelf[2] + w <= self.corner and shelf[1] >= h:
                    self.corner_at[j] = (shelf[0], shelf[2])
                    shelf[2] += w
                    break
            else:
                top = sum(shelf[1] for shelf in shelves)
                shelves.append([top, h, w])
                self.corner_at[j] = (top, 0)
        self.corner_rows = sum(shelf[1] for shelf in shelves)


def pack_kernel(frame, packing, fwd_ref, adj_ref, vel_ref, att_ref, gauge_ref, *outs):
    up, down, east, west, up_east, up_west, down_east, down_west = outs
    ny, lanes, cw = frame.ny, frame.lanes, packing.corner

    def field(j):
        if j < 5:
            return fwd_ref.at[0, j]
        if j < 10:
            return adj_ref.at[0, j - 5]
        if j == 10:
            return vel_ref
        if j == 11:
            return att_ref
        return gauge_ref.at[j - 12]

    for j in range(len(NEEDS)):
        h, w = packing.rows[j], packing.lanes[j]
        if h == 0:
            continue
        src = field(j)
        r = slice(packing.row_at[j], packing.row_at[j] + h)
        ws = packing.side[j]
        c = slice(packing.lane_at[j], packing.lane_at[j] + ws)
        top = slice(ny - h, ny)
        bottom = slice(0, h)
        up[r, :] = src[top, :]
        down[r, :] = src[bottom, :]
        east[:, c] = src[:, lanes - ws : lanes]
        west[:, c] = src[:, 0:ws]
        cr, cl = packing.corner_at[j]
        cr = slice(cr, cr + h)
        cl = slice(cl, cl + w)
        up_east[cr, cl] = src[top, lanes - w : lanes]
        up_west[cr, cl] = src[top, 0:w]
        down_east[cr, cl] = src[bottom, lanes - w : lanes]
        down_west[cr, cl] = src[bottom, 0:w]


def send_pieces(packed):
    count_y = lax.axis_size("gy")
    count_x = lax.axis_size("gx")

    def move(piece, dy, dx):
        pairs = []
        for y in range(count_y):
            for x in range(count_x):
                ty, tx = y + dy, x + dx
                if 0 <= ty < count_y and 0 <= tx < count_x:
                    pairs.append((y * count_x + x, ty * count_x + tx))
        return lax.ppermute(piece, ("gy", "gx"), pairs)

    steps = ((1, 0), (-1, 0), (0, 1), (0, -1), (1, 1), (1, -1), (-1, 1), (-1, -1))
    return tuple(move(p, dy, dx) for p, (dy, dx) in zip(packed, steps))


def assemble(dst, own, pieces, j, frame, packing):
    ny, lanes, oy, ox, cw = frame.ny, frame.lanes, frame.oy, frame.ox, packing.corner
    below, above, left, right, b_l, b_r, a_l, a_r = pieces
    h, w = packing.rows[j], packing.lanes[j]
    mid = slice(oy, oy + ny)
    centre = slice(ox, ox + lanes)
    dst[mid, centre] = own[...]
    if h == 0:
        return
    r = slice(packing.row_at[j], packing.row_at[j] + h)
    ws = packing.side[j]
    c = slice(packing.lane_at[j], packing.lane_at[j] + ws)
    lo = slice(oy - h, oy)
    hi = slice(oy + ny, oy + ny + h)
    west = slice(ox - w, ox)
    east = slice(ox + lanes, ox + lanes + w)
    dst[lo, centre] = below[r, :]
    dst[hi, centre] = above[r, :]
    dst[mid, ox - ws : ox] = left[:, c]
    dst[mid, ox + lanes : ox + lanes + ws] = right[:, c]
    cr, cl = packing.corner_at[j]
    cr = slice(cr, cr + h)
    cl = slice(cl, cl + w)
    dst[lo, west] = b_l[cr, cl]
    dst[lo, east] = b_r[cr, cl]
    dst[hi, west] = a_l[cr, cl]
    dst[hi, east] = a_r[cr, cl]


def window(frame, depth):
    r0 = max(0, (frame.oy - depth) // 8 * 8)
    r1 = min(frame.ey, round_up(frame.oy + frame.ny + depth, 8))
    l0 = max(0, (frame.ox - depth * CZ) // 128 * 128)
    l1 = min(frame.el, round_up(frame.ox + frame.lanes + depth * CZ, 128))
    return r0, r1, l0, l1


def stepper(frame, bounds_ref, win):
    r0, r1, l0, l1 = win
    ey, el = r1 - r0, l1 - l0
    row = lax.broadcasted_iota(jnp.int32, (ey, el), 0) + r0
    lane = lax.broadcasted_iota(jnp.int32, (ey, el), 1) + l0
    inside = (
        (row >= bounds_ref[0])
        & (row < bounds_ref[1])
        & (lane >= bounds_ref[2])
        & (lane < bounds_ref[3])
    )
    depth = lane % CZ
    zero = jnp.zeros((ey, el), jnp.float32)
    z_ok = {d: (depth + d >= 0) & (depth + d < CZ) for d in (-2, -1, 1, 2)}

    def rows(a, d):
        return a if d == 0 else pltpu.roll(a, (-d) % ey, 0)

    def lanes(a, d):
        return a if d == 0 else pltpu.roll(a, (-d) % el, 1)

    def deep(a, d):
        return a if d == 0 else jnp.where(z_ok[d], lanes(a, d), zero)

    def forward_diff(s):
        return coef_near * (s(1) - s(0)) + coef_far * (s(2) - s(-1))

    def backward_diff(s):
        return coef_near * (s(0) - s(-1)) + coef_far * (s(1) - s(-2))

    def wave_step(state, stiff, att):
        pres, vel_y, vel_x, vel_z, memory = state
        vel_y = jnp.where(inside, vel_y - forward_diff(lambda d: rows(pres, d)), zero)
        vel_x = jnp.where(inside, vel_x - forward_diff(lambda d: lanes(pres, d * CZ)), zero)
        vel_z = vel_z - forward_diff(lambda d: deep(pres, d))
        div = (
            backward_diff(lambda d: rows(vel_y, d))
            + backward_diff(lambda d: lanes(vel_x, d * CZ))
            + backward_diff(lambda d: deep(vel_z, d))
        )
        memory = memory - relax_rate * (memory + stiff * att * div)
        pres = jnp.where(inside, pres - stiff * (1.0 + att) * div - memory, zero)
        return [pres, vel_y, vel_x, vel_z, memory], div

    return wave_step, row, lane


def window_kernel(frame, packing, bounds_ref, source_ref, wave_ref, *rest):
    fwd_ref, adj_ref, vel_ref, att_ref, gauge_ref = rest[:5]
    pieces = rest[5:13]
    end_ref, start_ref, grad_ref, ext, inject, divs = rest[13:]
    owns = (
        [fwd_ref.at[0, k] for k in range(5)]
        + [adj_ref.at[0, k] for k in range(5)]
        + [vel_ref, att_ref]
        + [gauge_ref.at[k] for k in range(4)]
    )
    for j in range(16):
        assemble(ext.at[j], owns[j], pieces, j, frame, packing)
    vel_all = ext[10]
    att_all = ext[11]
    stiff_all = stiff_scale * vel_all * vel_all

    def cut(a, inner, outer):
        return a[inner[0] - outer[0] : inner[1] - outer[0], inner[2] - outer[2] : inner[3] - outer[2]]

    full = (0, frame.ey, 0, frame.el)
    tile = (frame.oy, frame.oy + frame.ny, frame.ox, frame.ox + frame.lanes)

    state = [ext[k] for k in range(5)]
    where = full
    for step in range(STEPS):
        win = window(frame, 3 * (STEPS - step) + 3 * (STEPS - 1))
        state = [cut(a, win, where) for a in state]
        where = win
        wave_step, row, lane = stepper(frame, bounds_ref, win)
        source = (row == source_ref[0]) & (lane == source_ref[1])
        state, div = wave_step(state, cut(stiff_all, win, full), cut(att_all, win, full))
        state[0] = state[0] + jnp.where(source, wave_ref[step], jnp.float32(0.0))
        divs[step] = cut(div, tile, win)
        inject[step, win[0] : win[1], win[2] : win[3]] = (
            cut(ext[12], win, full) * state[0] - cut(ext[13 + step], win, full)
        )
    for k in range(5):
        end_ref[0, k] = cut(state[k], tile, where)

    velocity = cut(vel_all, tile, full)
    attenuation = cut(att_all, tile, full)
    stiff_own = cut(stiff_all, tile, full)
    adj = [ext[5 + k] for k in range(5)]
    where = full
    grad_v = jnp.zeros((frame.ny, frame.lanes), jnp.float32)
    grad_a = jnp.zeros((frame.ny, frame.lanes), jnp.float32)
    for step in range(STEPS - 1, -1, -1):
        win = window(frame, 3 * (step + 1))
        adj = [cut(a, win, where) for a in adj]
        where = win
        wave_step, row, lane = stepper(frame, bounds_ref, win)
        adj, unused = wave_step(adj, cut(stiff_all, win, full), cut(att_all, win, full))
        adj[0] = adj[0] + inject[step, win[0] : win[1], win[2] : win[3]]
        div = divs[step]
        q = cut(adj[0], tile, win)
        m = cut(adj[4], tile, win)
        deriv_q = (relax_rate * attenuation - (1.0 + attenuation)) * div
        deriv_m = -relax_rate * attenuation * div
        grad_v = grad_v + (q * deriv_q + m * deriv_m) * (2.0 * stiff_scale * velocity)
        grad_a = grad_a + (q * (relax_rate - 1.0) - m * relax_rate) * stiff_own * div
    for k in range(5):
        start_ref[0, k] = cut(adj[k], tile, where)
    for c, g in enumerate((grad_v, grad_a)):
        grad_ref[c] = g.reshape(frame.ny // BY, BY, frame.lanes).sum(axis=1)


def vmem():
    return pl.BlockSpec(memory_space=pltpu.VMEM)


def smem():
    return pl.BlockSpec(memory_space=pltpu.SMEM)


def on_device(
    forward_start,
    adjoint_end,
    velocity,
    attenuation,
    wavelet,
    source_cell,
    receiver_cells,
    observed,
    aperture,
    block_slot,
):
    nz = CZ
    ny = velocity.shape[0]
    lanes = velocity.shape[1]
    nx = lanes // nz
    frame = Frame(ny, lanes)
    index_y = lax.axis_index("gy")
    index_x = lax.axis_index("gx")
    total_y = ny * lax.axis_size("gy")
    total_x = nx * lax.axis_size("gx")

    row_lo = frame.oy - index_y * ny
    lane_lo = frame.ox - index_x * lanes
    bounds = jnp.stack([row_lo, row_lo + total_y, lane_lo, lane_lo + total_x * nz]).astype(jnp.int32)

    cell = source_cell[0, 0]
    src_row = cell // (total_x * nz) + row_lo
    src_lane = cell % (total_x * nz) + lane_lo
    source = jnp.stack([src_row, src_lane]).astype(jnp.int32)

    recs = receiver_cells[0, 0]
    at_row = (recs // lanes)[:, None] == lax.broadcasted_iota(jnp.int32, (recs.shape[0], ny), 1)
    at_lane = (recs % lanes)[:, None] == lax.broadcasted_iota(jnp.int32, (recs.shape[0], lanes), 1)
    weights = jnp.concatenate([jnp.ones((1, recs.shape[0]), jnp.float32), observed[0, :, 0]], axis=0)
    gauge = jnp.einsum(
        "nky,kl->nyl",
        weights[:, :, None] * at_row.astype(jnp.float32)[None],
        at_lane.astype(jnp.float32),
        precision=lax.Precision.HIGHEST,
    )

    packing = Packing(frame)
    packed = pl.pallas_call(
        lambda *refs: pack_kernel(frame, packing, *refs),
        out_shape=tuple(
            jax.ShapeDtypeStruct(shape, jnp.float32)
            for shape in (
                [(packing.total_rows, lanes)] * 2
                + [(ny, packing.total_lanes)] * 2
                + [(packing.corner_rows, packing.corner)] * 4
            )
        ),
        in_specs=[vmem()] * 5,
        out_specs=tuple([vmem()] * 8),
    )(forward_start, adjoint_end, velocity, attenuation, gauge)
    pieces = send_pieces(packed)

    ext_shape = (frame.ey, frame.el)
    forward_end, adjoint_start, row_sums = pl.pallas_call(
        lambda *refs: window_kernel(frame, packing, *refs),
        out_shape=(
            jax.ShapeDtypeStruct((1, 5, ny, lanes), jnp.float32),
            jax.ShapeDtypeStruct((1, 5, ny, lanes), jnp.float32),
            jax.ShapeDtypeStruct((2, ny // BY, lanes), jnp.float32),
        ),
        in_specs=[smem(), smem(), smem()] + [vmem()] * 13,
        out_specs=(vmem(), vmem(), vmem()),
        scratch_shapes=[
            pltpu.VMEM((16,) + ext_shape, jnp.float32),
            pltpu.VMEM((STEPS,) + ext_shape, jnp.float32),
            pltpu.VMEM((STEPS, ny, lanes), jnp.float32),
        ],
        compiler_params=pltpu.CompilerParams(vmem_limit_bytes=48 * 1024 * 1024),
    )(bounds, source, wavelet[0], forward_start, adjoint_end, velocity, attenuation, gauge, *pieces)

    grad_scale = float(BY * BX * BZ) ** (-0.5)
    weight = aperture[0, 0].astype(jnp.float32)
    blocks = row_sums.reshape(2, ny // BY, nx // BX, BX, nz // BZ, BZ).sum(axis=(3, 5))
    sums = blocks.transpose(1, 2, 3, 0).reshape(-1, 2) * (grad_scale * weight)
    slots = block_slot[0]
    ordered = jnp.zeros(sums.shape, jnp.float32).at[slots].set(sums)
    shots = lax.axis_size("shot")
    me = lax.axis_index("shot")
    held = ordered.reshape(shots, -1, 2)
    span = shots // 2
    while span >= 1:
        halves = held.reshape(2, -1, held.shape[1], 2)
        bit = (me // span) % 2 == 1
        mine = jnp.where(bit, halves[1], halves[0])
        other = jnp.where(bit, halves[0], halves[1])
        held = mine + lax.ppermute(other, "shot", [(i, i ^ span) for i in range(shots)])
        span //= 2
    coarse = held[0]
    model_gradient = coarse.T[:, None, :]
    return (forward_end, adjoint_start, model_gradient)


def solution(mesh):
    placed = (
        P("shot", None, "gy", "gx"),
        P("shot", None, "gy", "gx"),
        P("gy", "gx"),
        P("gy", "gx"),
        P("shot", None),
        P("shot", None),
        P("shot", ("gy", "gx"), None),
        P("shot", None, ("gy", "gx"), None),
        P("shot", ("gy", "gx")),
        P(("gy", "gx"), None),
    )
    return jax.shard_map(
        on_device,
        mesh=mesh,
        in_specs=placed,
        out_specs=(
            P("shot", None, "gy", "gx"),
            P("shot", None, "gy", "gx"),
            P(None, ("gy", "gx"), "shot"),
        ),
        check_vma=False,
    )
```
